32 devices in a mesh: dp: 8 (over y, x, core), tensor: 4 (over z).
Axes of the slice: x: 2, y: 2, z: 4, core: 2. Of those that a mesh axis runs over, the one named last changes fastest.
Arguments:
- inputs: bfloat16 [16384, 768], P(('dp', 'tensor')), may hold values from -6 to 6
- prefix: int32 [16], P('dp'), may hold values from 102 to 512, as said below
- cotangent: bfloat16 [16384, 768], P(('dp', 'tensor')), may hold values from -6 to 6
- w_query: bfloat16 [768, 768], P('dp', 'tensor'), may hold values from -0.3125 to 0.3125
- w_key: bfloat16 [768, 768], P('dp', 'tensor'), may hold values from -0.3125 to 0.3125
- w_value: bfloat16 [768, 768], P('dp', 'tensor'), may hold values from -0.21875 to 0.21875
- w_out: bfloat16 [768, 768], P('tensor', 'dp'), may hold values from -0.875 to 0.875
- w_up: bfloat16 [768, 3072], P('dp', 'tensor'), may hold values from -0.21875 to 0.21875
- w_down: bfloat16 [3072, 768], P('tensor', 'dp'), may hold values from -0.109375 to 0.109375
- b_query: bfloat16 [768], replicated, may hold values from -3 to 3
- b_value: bfloat16 [768], replicated, may hold values from -3 to 3
- b_out: bfloat16 [768], replicated, may hold values from -2 to 2
- b_up: bfloat16 [3072], replicated, may hold values from -3 to 3
- b_down: bfloat16 [768], replicated, may hold values from -2 to 2
- gain_one: bfloat16 [768], replicated, may hold values from 0.25 to 1.75
- shift_one: bfloat16 [768], replicated, may hold values from -2 to 2
- gain_two: bfloat16 [768], replicated, may hold values from 0.25 to 1.75
- shift_two: bfloat16 [768], replicated, may hold values from -2 to 2
Outputs:
- output: bfloat16 [16384, 768], P(('dp', 'tensor'))
- grad_input: float32 [16384, 768], P(('dp', 'tensor'))
- grad_w_query: float32 [768, 768], P('dp', 'tensor')
- grad_w_key: float32 [768, 768], P('dp', 'tensor')
- grad_w_value: float32 [768, 768], P('dp', 'tensor')
- grad_w_out: float32 [768, 768], P('tensor', 'dp')
- grad_w_up: float32 [768, 3072], P('dp', 'tensor')
- grad_w_down: float32 [3072, 768], P('tensor', 'dp')
- grad_b_query: float32 [768], replicated
- grad_b_value: float32 [768], replicated
- grad_b_out: float32 [768], replicated
- grad_b_up: float32 [3072], replicated
- grad_b_down: float32 [768], replicated
- grad_gain_one: float32 [768], replicated
- grad_shift_one: float32 [768], replicated
- grad_gain_two: float32 [768], replicated
- grad_shift_two: float32 [768], replicated
The draws below stay inside these ranges and needn't reach their ends.
Inputs may be any that keep to these rules, and one draw needn't show every extreme that they name: Every draw has a sequence whose prefix is exactly 512.
All inputs are finite; a program needn't handle non-finite values.
Results may differ from the reference program's by a relative error of at most 0.015.
Values may be sent and summed in bfloat16 or wider, within the bound.
No kernel may reach another device: no remote copies, remote signals or barrier semaphores. Data moves between devices by JAX's collectives and lax.ppermute only.
A program may use at most 192 MiB of HBM per device.

```python
import math
import jax
import jax.numpy as jnp
from jax import lax

D = 768
HEADS = 12
HEAD = 64
FF = 3072
SEQ_LEN = 1024
SEQS = 16
TOKENS = 16384


def draw_prefix(key, part):
    length_key, spot_key = jax.random.split(jax.random.fold_in(key, 17))
    shortest = SEQ_LEN // 10
    longest = SEQ_LEN // 2
    drawn = jax.random.randint(length_key, (SEQS,), shortest, longest + 1)
    chosen = jax.random.randint(spot_key, (), 0, SEQS)
    marked = jnp.arange(SEQS, dtype=jnp.int32) == chosen
    return jnp.where(marked, longest, drawn).astype(jnp.int32)


def strengthened(array, rng, source, target, parts, factor):
    def block_of(dim):
        return (jnp.arange(array.shape[dim]) // (array.shape[dim] // parts)).reshape((-1,) + (1,) * (array.ndim - 1 - dim))

    near = jax.random.permutation(rng, parts)[block_of(target)]
    far = (block_of(target) + parts // 2) % parts
    return jnp.where((block_of(source) == near) | (block_of(source) == far), factor * array, array)


def steps_of(own_key, extent, pieces, least, high):
    level, own = 1.0, jax.random.fold_in(own_key, 6)
    for axis_at, shards_of in pieces:
        draws = jnp.exp(jax.random.uniform(jax.random.fold_in(own, axis_at), (shards_of,), jnp.float32, least / len(pieces), high / len(pieces)))
        level = level * jnp.repeat(draws, extent[axis_at] // shards_of).reshape([-1 if axis == axis_at else 1 for axis in range(len(extent))])
    return level


def bell_draw(stream_key, dims, deviation, bound, shards=(), kind=jnp.bfloat16):
    array = jax.random.normal(stream_key, dims, jnp.float32) * deviation
    if len(shards) > 0:
        array = steps_of(stream_key, dims, shards, -0.22, 0.18) * array
    return jnp.clip(array, min=-bound, max=bound).astype(kind)


def heavy_noise(stream_key, extent, scale, most, pieces, heavy, kind=jnp.bfloat16):
    values = scale * jax.random.normal(stream_key, extent, jnp.float32)
    if pieces:
        values = values * steps_of(stream_key, extent, pieces, -0.22, 0.18)
    return jnp.clip(strengthened(values, jax.random.fold_in(stream_key, 3), *heavy), -most, most).astype(kind)


def setup_inputs(seed: int = 0) -> dict:
    splits = jax.random.split(jax.random.key(seed), 19)
    return {
        "inputs": heavy_noise(splits[0], (TOKENS, D), 1.0, 6.0, ((0, 32),), (0, 1, 32, 2.75)),
        "prefix": draw_prefix(jax.random.fold_in(splits[18], 71), 0),
        "cotangent": heavy_noise(splits[2], (TOKENS, D), 1.0, 6.0, ((0, 32),), (0, 1, 32, 2.75)),
        "w_query": bell_draw(splits[3], (D, D), (D // 2) ** -0.5, 0.3125, ((0, 8), (1, 4))),
        "w_key": bell_draw(splits[4], (D, D), (D // 2) ** -0.5, 0.3125, ((0, 8), (1, 4))),
        "w_value": bell_draw(splits[5], (D, D), D ** -0.5, 0.21875, ((0, 8), (1, 4))),
        "w_out": bell_draw(splits[6], (D, D), (D // 16) ** -0.5, 0.875, ((0, 4), (1, 8))),
        "w_up": bell_draw(splits[7], (D, FF), D ** -0.5, 0.21875, ((0, 8), (1, 4))),
        "w_down": bell_draw(splits[8], (FF, D), FF ** -0.5, 0.109375, ((0, 4), (1, 8))),
        "b_query": bell_draw(splits[9], (D,), 0.5, 3.0),
        "b_value": bell_draw(splits[10], (D,), 0.5, 3.0),
        "b_out": bell_draw(splits[11], (D,), 0.3, 2.0),
        "b_up": bell_draw(splits[12], (FF,), 0.5, 3.0),
        "b_down": bell_draw(splits[13], (D,), 0.3, 2.0),
        "gain_one": jnp.clip(1.0 + 0.15 * jax.random.normal(splits[14], (D,), jnp.float32), 0.25, 1.75).astype(jnp.bfloat16),
        "shift_one": bell_draw(splits[15], (D,), 0.3, 2.0),
        "gain_two": jnp.clip(1.0 + 0.15 * jax.random.normal(splits[16], (D,), jnp.float32), 0.25, 1.75).astype(jnp.bfloat16),
        "shift_two": bell_draw(splits[17], (D,), 0.3, 2.0),
    }


@jax.custom_vjp
def low(v):
    return lax.optimization_barrier(v.astype(jnp.bfloat16)).astype(jnp.float32)

@jax.custom_vjp
def low_back(v):
    return v

def low_keep(v):
    return (low(v), None)

def low_pass(kept, grad):
    return (grad,)

def back_keep(v):
    return (v, None)

def back_low(kept, grad):
    return (low(grad),)
low.defvjp(low_keep, low_pass)
low_back.defvjp(back_keep, back_low)
norm_eps = 1e-12
masked_score = -1e+30

def matmul(first_op, second_op):
    return jnp.dot(first_op, second_op, precision=lax.Precision.HIGHEST)

def layer_norm(values, norm_gain, norm_shift):
    center = values - lax.optimization_barrier(jnp.mean(values, axis=-1, keepdims=True))
    spread = lax.optimization_barrier(jnp.mean(center * center, axis=-1, keepdims=True))
    return center * lax.rsqrt(spread + norm_eps) * norm_gain + norm_shift

def attend_one(packed):
    queries, key_rows, value_rows, prefix_len = packed
    scaling = HEAD ** (-0.5)
    scores = jnp.einsum('qhe,khe->hqk', queries, key_rows, precision=lax.Precision.HIGHEST) * scaling
    row_index = jnp.arange(SEQ_LEN, dtype=jnp.int32)[:, None]
    col_index = jnp.arange(SEQ_LEN, dtype=jnp.int32)[None, :]
    visible = (col_index <= row_index) | (col_index < prefix_len)
    scores = low_back(jnp.where(visible[None], scores, masked_score))
    row_top = lax.optimization_barrier(jnp.max(scores, axis=-1, keepdims=True))
    exponent = jnp.exp(scores - row_top)
    probability = low(exponent / lax.optimization_barrier(jnp.sum(exponent, axis=-1, keepdims=True)))
    return jnp.einsum('hqk,khe->qhe', probability, value_rows, precision=lax.Precision.HIGHEST)
attend_checked = jax.checkpoint(attend_one)

def layer_forward(rows_in, weights, lengths):
    w_query, w_key, w_value, w_out, w_up, w_down, b_query, b_value, b_out, b_up, b_down, gain_one, shift_one, gain_two, shift_two = weights
    normed_one = low(layer_norm(rows_in, gain_one, shift_one))
    queries = low(low_back(matmul(normed_one, w_query) + b_query))
    key_rows = low(low_back(matmul(normed_one, w_key)))
    value_rows = low(low_back(matmul(normed_one, w_value) + b_value))
    shape_four = (lengths.shape[0], SEQ_LEN, HEADS, HEAD)
    attended = lax.map(attend_checked, (queries.reshape(shape_four), key_rows.reshape(shape_four), value_rows.reshape(shape_four), lengths))
    attended = low(low_back(attended.reshape(-1, D)))
    middle = rows_in + low_back(matmul(attended, w_out)) + b_out
    normed_two = low(layer_norm(middle, gain_two, shift_two))
    pre_act = low_back(matmul(normed_two, w_up) + b_up)
    activated = low(jax.nn.gelu(pre_act, approximate=False))
    return middle + low_back(matmul(activated, w_down)) + b_down

def reference(inputs, prefix, cotangent, w_query, w_key, w_value, w_out, w_up, w_down, b_query, b_value, b_out, b_up, b_down, gain_one, shift_one, gain_two, shift_two):
    params = tuple((weight.astype(jnp.float32) for weight in (w_query, w_key, w_value, w_out, w_up, w_down, b_query, b_value, b_out, b_up, b_down, gain_one, shift_one, gain_two, shift_two)))
    group_size = math.gcd(SEQS, max(1, 4096 // SEQ_LEN))
    group_count = SEQS // group_size
    inputs_grouped = inputs.astype(jnp.float32).reshape(group_count, group_size * SEQ_LEN, D)
    grads_grouped = cotangent.astype(jnp.float32).reshape(group_count, group_size * SEQ_LEN, D)
    prefix_grouped = prefix.reshape(group_count, group_size)

    def one_group(totals, group_item):
        rows_in, grad_rows, lengths = group_item

        def forward_fn(rows_value, *weights):
            return layer_forward(rows_value, weights, lengths)
        outcome, pull_back = jax.vjp(forward_fn, rows_in, *params)
        cotangents = pull_back(grad_rows)
        totals = tuple((total + grad for total, grad in zip(totals, cotangents[1:])))
        return (totals, (outcome.astype(jnp.bfloat16), cotangents[0]))
    initial = tuple((jnp.zeros_like(weight) for weight in params))
    totals, (outcomes, grad_inputs) = lax.scan(one_group, initial, (inputs_grouped, grads_grouped, prefix_grouped))
    return (outcomes.reshape(TOKENS, D), grad_inputs.reshape(TOKENS, D), totals[0], totals[1], totals[2], totals[3], totals[4], totals[5], totals[6], totals[7], totals[8], totals[9], totals[10], totals[11], totals[12], totals[13], totals[14])
```

```python
import jax
import jax.numpy as jnp
from jax import lax
from jax.sharding import PartitionSpec as P

HEAD = 64
SEQ_LEN = 1024

norm_eps = 1e-12
masked_score = -1e30


def layer_norm(values, norm_gain, norm_shift):
    center = values - jnp.mean(values, axis=-1, keepdims=True)
    spread = jnp.mean(center * center, axis=-1, keepdims=True)
    return center * lax.rsqrt(spread + norm_eps) * norm_gain + norm_shift


def gelu_exact(values):
    return jax.nn.gelu(values, approximate=False)


def dot_right(first_op, second_op):
    return jnp.dot(first_op, second_op, preferred_element_type=jnp.float32)


def dot_back(first_op, second_op):
    return lax.dot_general(
        first_op, second_op, (((1,), (1,)), ((), ())), preferred_element_type=jnp.float32
    )


def dot_over_rows(first_op, second_op):
    return lax.dot_general(
        first_op, second_op, (((0,), (0,)), ((), ())), preferred_element_type=jnp.float32
    )


AXES = ("dp", "tensor")


def gather_rows_cols(shard, dp, tp):
    r, c = shard.shape
    full = lax.all_gather(shard, AXES, axis=0, tiled=False)
    return full.reshape(dp, tp, r, c).transpose(0, 2, 1, 3).reshape(dp * r, tp * c)


def gather_cols_rows(shard, dp, tp):
    r, c = shard.shape
    full = lax.all_gather(shard, AXES, axis=0, tiled=False)
    return full.reshape(dp, tp, r, c).transpose(1, 2, 0, 3).reshape(tp * r, dp * c)


def blocks_rows_cols(grad, dp, tp):
    rows, cols = grad.shape
    r, c = rows // dp, cols // tp
    return grad.reshape(dp, r, tp, c).transpose(0, 2, 1, 3).reshape(dp * tp, r, c)


def blocks_cols_rows(grad, dp, tp):
    rows, cols = grad.shape
    r, c = rows // tp, cols // dp
    return grad.reshape(tp, r, dp, c).transpose(2, 0, 1, 3).reshape(dp * tp, r, c)


def scatter_blocks(blocks):
    return lax.psum_scatter(blocks, AXES, scatter_dimension=0, tiled=False)


def summed_everywhere(vectors):
    joined = jnp.concatenate(vectors)
    total = jnp.sum(lax.all_gather(joined, AXES, axis=0, tiled=False), axis=0)
    out = []
    start = 0
    for v in vectors:
        out.append(total[start : start + v.shape[0]])
        start += v.shape[0]
    return out


def scores_of(queries, key_rows, qpos, kpos, prefix_len):
    scaling = HEAD ** (-0.5)
    scores = jnp.einsum("qhe,khe->hqk", queries, key_rows, preferred_element_type=jnp.float32) * scaling
    visible = (kpos[None, :] <= qpos[:, None]) | (kpos[None, :] < prefix_len)
    return jnp.where(visible[None], scores, masked_score)


def body(
    inputs,
    prefix,
    cotangent,
    w_query,
    w_key,
    w_value,
    w_out,
    w_up,
    w_down,
    b_query,
    b_value,
    b_out,
    b_up,
    b_down,
    gain_one,
    shift_one,
    gain_two,
    shift_two,
):
    f32 = jnp.float32
    bf16 = jnp.bfloat16
    dp = lax.axis_size("dp")
    tp = lax.axis_size("tensor")
    t_index = lax.axis_index("tensor")
    rows = inputs.shape[0]
    pieces = SEQ_LEN // rows
    assert pieces == 2
    half = t_index % pieces
    seq_here = (t_index * rows) // SEQ_LEN
    prefix_len = lax.dynamic_index_in_dim(prefix, seq_here, keepdims=False)
    pos_own = half * rows + lax.iota(jnp.int32, rows)
    pos_oth = (1 - half) * rows + lax.iota(jnp.int32, rows)
    to_second = [(t, t + 1) for t in range(0, tp, 2)]
    to_first = [(t + 1, t) for t in range(0, tp, 2)]

    full_query = gather_rows_cols(w_query, dp, tp)
    full_key = gather_rows_cols(w_key, dp, tp)
    full_value = gather_rows_cols(w_value, dp, tp)
    full_out = gather_cols_rows(w_out, dp, tp)
    full_up = gather_rows_cols(w_up, dp, tp)
    full_down = gather_cols_rows(w_down, dp, tp)
    width = full_query.shape[1]
    heads = width // HEAD

    gain_first = gain_one.astype(f32)
    shift_first = shift_one.astype(f32)
    gain_second = gain_two.astype(f32)
    shift_second = shift_two.astype(f32)

    in_rows = inputs.astype(f32)
    normed_one = layer_norm(in_rows, gain_first, shift_first).astype(bf16)
    key_rows = dot_right(normed_one, full_key).astype(bf16)
    value_rows = (dot_right(normed_one, full_value) + b_value.astype(f32)).astype(bf16)
    queries = (dot_right(normed_one, full_query) + b_query.astype(f32)).astype(bf16)
    shape3 = (rows, heads, HEAD)
    q3 = queries.reshape(shape3)
    k3 = key_rows.reshape(shape3)
    v3 = value_rows.reshape(shape3)
    k_oth, v_oth = lax.ppermute((k3, v3), "tensor", to_second)

    s_own = scores_of(q3, k3, pos_own, pos_own, prefix_len)
    s_oth = scores_of(q3, k_oth, pos_own, pos_oth, prefix_len)
    row_top = jnp.maximum(jnp.max(s_own, axis=-1, keepdims=True), jnp.max(s_oth, axis=-1, keepdims=True))
    e_own = jnp.exp(s_own - row_top)
    e_oth = jnp.exp(s_oth - row_top)
    row_total = jnp.sum(e_own, axis=-1, keepdims=True) + jnp.sum(e_oth, axis=-1, keepdims=True)
    p_own = (e_own / row_total).astype(bf16)
    p_oth = (e_oth / row_total).astype(bf16)
    attended = jnp.einsum("hqk,khe->qhe", p_own, v3, preferred_element_type=f32) + jnp.einsum(
        "hqk,khe->qhe", p_oth, v_oth, preferred_element_type=f32
    )
    log_sums = row_top + jnp.log(row_total)
    attended = attended.reshape(rows, width).astype(bf16)
    q_rcv, lse_rcv = lax.ppermute((q3, log_sums), "tensor", to_first)

    middle = in_rows + dot_right(attended, full_out) + b_out.astype(f32)
    normed_two = layer_norm(middle, gain_second, shift_second).astype(bf16)
    pre_act = dot_right(normed_two, full_up) + b_up.astype(f32)
    activated = gelu_exact(pre_act).astype(bf16)
    result = (middle + dot_right(activated, full_down) + b_down.astype(f32)).astype(bf16)

    grad_result = cotangent.astype(f32)
    down_blocks = blocks_cols_rows(dot_over_rows(activated, cotangent), dp, tp)
    grad_act = dot_back(cotangent, full_down)
    down_blocks, grad_act = lax.optimization_barrier((down_blocks, grad_act))
    shard_down = scatter_blocks(down_blocks)
    grad_pre = jax.vjp(gelu_exact, pre_act)[1](grad_act)[0].astype(bf16)
    up_blocks = blocks_rows_cols(dot_over_rows(normed_two, grad_pre), dp, tp)
    grad_norm_two = dot_back(grad_pre, full_up)
    up_blocks, grad_norm_two = lax.optimization_barrier((up_blocks, grad_norm_two))
    shard_up = scatter_blocks(up_blocks)
    norm_two_back = jax.vjp(layer_norm, middle, gain_second, shift_second)[1](grad_norm_two)
    grad_middle = grad_result + norm_two_back[0]
    early_sums = summed_everywhere(
        [
            jnp.sum(grad_middle, axis=0),
            jnp.sum(grad_pre, axis=0, dtype=f32),
            jnp.sum(grad_result, axis=0),
            norm_two_back[1],
            norm_two_back[2],
        ]
    )
    grad_attn_rows = grad_middle.astype(bf16)
    out_blocks = blocks_cols_rows(dot_over_rows(attended, grad_attn_rows), dp, tp)
    grad_attended = dot_back(grad_attn_rows, full_out).astype(bf16)
    out_blocks, grad_attended = lax.optimization_barrier((out_blocks, grad_attended))
    shard_out = scatter_blocks(out_blocks)
    do3 = grad_attended.reshape(shape3)

    scaling = HEAD ** (-0.5)
    prob_own = jnp.exp(s_own - log_sums)
    prob_oth = jnp.exp(s_oth - log_sums)
    dp_own = jnp.einsum("qhe,khe->hqk", do3, v3, preferred_element_type=f32)
    dp_oth = jnp.einsum("qhe,khe->hqk", do3, v_oth, preferred_element_type=f32)
    delta = jnp.sum(prob_own * dp_own, axis=-1, keepdims=True) + jnp.sum(
        prob_oth * dp_oth, axis=-1, keepdims=True
    )
    do_rcv, delta_rcv = lax.ppermute((do3, delta), "tensor", to_first)
    ds_own = (prob_own * (dp_own - delta)).astype(bf16)
    ds_oth = (prob_oth * (dp_oth - delta)).astype(bf16)
    dq = (
        jnp.einsum("hqk,khe->qhe", ds_own, k3, preferred_element_type=f32)
        + jnp.einsum("hqk,khe->qhe", ds_oth, k_oth, preferred_element_type=f32)
    ) * scaling
    dk = jnp.einsum("hqk,qhe->khe", ds_own, q3, preferred_element_type=f32)
    dv = jnp.einsum("hqk,qhe->khe", prob_own.astype(bf16), do3, preferred_element_type=f32)
    s_x = scores_of(q_rcv, k3, pos_oth, pos_own, prefix_len)
    prob_x = jnp.exp(s_x - lse_rcv)
    dp_x = jnp.einsum("qhe,khe->hqk", do_rcv, v3, preferred_element_type=f32)
    ds_x = (prob_x * (dp_x - delta_rcv)).astype(bf16)
    dk = (dk + jnp.einsum("hqk,qhe->khe", ds_x, q_rcv, preferred_element_type=f32)) * scaling
    dv = dv + jnp.einsum("hqk,qhe->khe", prob_x.astype(bf16), do_rcv, preferred_element_type=f32)

    grad_q = dq.reshape(rows, width).astype(bf16)
    grad_k = dk.reshape(rows, width).astype(bf16)
    grad_v = dv.reshape(rows, width).astype(bf16)
    grad_wq = dot_over_rows(normed_one, grad_q)
    grad_wk = dot_over_rows(normed_one, grad_k)
    grad_wv = dot_over_rows(normed_one, grad_v)
    grad_norm_one = dot_back(grad_q, full_query) + dot_back(grad_k, full_key) + dot_back(grad_v, full_value)
    norm_one_back = jax.vjp(layer_norm, in_rows, gain_first, shift_first)[1](grad_norm_one)
    grad_input = grad_middle + norm_one_back[0]

    shard_query = scatter_blocks(blocks_rows_cols(grad_wq, dp, tp))
    shard_key = scatter_blocks(blocks_rows_cols(grad_wk, dp, tp))
    shard_value = scatter_blocks(blocks_rows_cols(grad_wv, dp, tp))
    late_sums = summed_everywhere(
        [
            jnp.sum(grad_q, axis=0, dtype=f32),
            jnp.sum(grad_v, axis=0, dtype=f32),
            norm_one_back[1],
            norm_one_back[2],
        ]
    )
    vector_sums = (
        late_sums[0],
        late_sums[1],
        early_sums[0],
        early_sums[1],
        early_sums[2],
        late_sums[2],
        late_sums[3],
        early_sums[3],
        early_sums[4],
    )
    return (
        result,
        grad_input,
        shard_query,
        shard_key,
        shard_value,
        shard_out,
        shard_up,
        shard_down,
    ) + tuple(vector_sums)


def solution(mesh):
    rows_spec = P(("dp", "tensor"), None)
    placed = (
        rows_spec,
        P("dp"),
        rows_spec,
        P("dp", "tensor"),
        P("dp", "tensor"),
        P("dp", "tensor"),
        P("tensor", "dp"),
        P("dp", "tensor"),
        P("tensor", "dp"),
    ) + (P(),) * 9
    return jax.shard_map(
        body,
        mesh=mesh,
        in_specs=placed,
        out_specs=(
            rows_spec,
            rows_spec,
            P("dp", "tensor"),
            P("dp", "tensor"),
            P("dp", "tensor"),
            P("tensor", "dp"),
            P("dp", "tensor"),
            P("tensor", "dp"),
        )
        + (P(),) * 9,
        check_vma=False,
    )
```

```python
import jax
import jax.numpy as jnp
from jax import lax
from jax.sharding import PartitionSpec as P


HEAD = 64
SEQ_LEN = 1024

norm_eps = 1e-12
masked_score = -1e30


def layer_norm(values, norm_gain, norm_shift):
    center = values - jnp.mean(values, axis=-1, keepdims=True)
    spread = jnp.mean(center * center, axis=-1, keepdims=True)
    return center * lax.rsqrt(spread + norm_eps) * norm_gain + norm_shift


def gelu_exact(values):
    return jax.nn.gelu(values, approximate=False)


def dot_right(first_op, second_op):
    return jnp.dot(first_op, second_op, preferred_element_type=jnp.float32)


def dot_back(first_op, second_op):
    return lax.dot_general(
        first_op, second_op, (((1,), (1,)), ((), ())), preferred_element_type=jnp.float32
    )


def dot_over_rows(first_op, second_op):
    return lax.dot_general(
        first_op, second_op, (((0,), (0,)), ((), ())), preferred_element_type=jnp.float32
    )


AXES = ("dp", "tensor")


def gather_joined(shards, dp, tp):
    r = shards[0].shape[0]
    joined = jnp.concatenate(shards, axis=1)
    full = lax.all_gather(joined, AXES, axis=0, tiled=False).reshape(dp, tp, r, -1)
    out = []
    start = 0
    for piece in shards:
        c = piece.shape[1]
        block = full[:, :, :, start : start + c]
        out.append(block.transpose(0, 2, 1, 3).reshape(dp * r, tp * c))
        start += c
    return out


def scatter_rows(grad):
    return lax.psum_scatter(grad, "dp", scatter_dimension=0, tiled=True)


def scatter_cols_joined(pieces, tp):
    parts = []
    for piece in pieces:
        r, c = piece.shape
        parts.append(piece.reshape(r, tp, c // tp).transpose(1, 0, 2))
    joined = jnp.concatenate(parts, axis=2)
    mine = lax.psum_scatter(joined, "tensor", scatter_dimension=0, tiled=False)
    out = []
    start = 0
    for piece in pieces:
        c = piece.shape[1] // tp
        out.append(mine[:, start : start + c])
        start += c
    return out


def scores_of(queries, key_rows, qpos, kpos, prefix_len):
    scaling = HEAD ** (-0.5)
    scores = jnp.einsum("qhe,khe->hqk", queries, key_rows, preferred_element_type=jnp.float32) * scaling
    visible = (kpos[None, :] <= qpos[:, None]) | (kpos[None, :] < prefix_len)
    return jnp.where(visible[None], scores, masked_score)


def layer(
    inputs,
    prefix,
    cotangent,
    w_query,
    w_key,
    w_value,
    w_out,
    w_up,
    w_down,
    b_query,
    b_value,
    b_out,
    b_up,
    b_down,
    gain_one,
    shift_one,
    gain_two,
    shift_two,
):
    f32 = jnp.float32
    bf16 = jnp.bfloat16
    dp = lax.axis_size("dp")
    tp = lax.axis_size("tensor")
    t_index = lax.axis_index("tensor")
    rows = inputs.shape[0]
    pieces = SEQ_LEN // rows
    assert pieces == 2
    half = t_index % pieces
    seq_here = (t_index * rows) // SEQ_LEN
    prefix_len = lax.dynamic_index_in_dim(prefix, seq_here, keepdims=False)
    pos_own = half * rows + lax.iota(jnp.int32, rows)
    pos_oth = (1 - half) * rows + lax.iota(jnp.int32, rows)
    to_second = [(t, t + 1) for t in range(0, tp, 2)]
    to_first = [(t + 1, t) for t in range(0, tp, 2)]

    full_query, full_key, full_value, out_t = gather_joined([w_query, w_key, w_value, w_out.T], dp, tp)
    full_out = out_t.T
    full_up, down_t = gather_joined([w_up, w_down.T], dp, tp)
    full_down = down_t.T
    width = full_query.shape[1]
    heads = width // HEAD

    gain_first = gain_one.astype(f32)
    shift_first = shift_one.astype(f32)
    gain_second = gain_two.astype(f32)
    shift_second = shift_two.astype(f32)

    in_rows = inputs.astype(f32)
    normed_one = layer_norm(in_rows, gain_first, shift_first).astype(bf16)
    key_rows = dot_right(normed_one, full_key).astype(bf16)
    value_rows = (dot_right(normed_one, full_value) + b_value.astype(f32)).astype(bf16)
    queries = (dot_right(normed_one, full_query) + b_query.astype(f32)).astype(bf16)
    shape3 = (rows, heads, HEAD)
    q3 = queries.reshape(shape3)
    k3 = key_rows.reshape(shape3)
    v3 = value_rows.reshape(shape3)
    k_oth, v_oth = lax.ppermute((k3, v3), "tensor", to_second)

    s_own = scores_of(q3, k3, pos_own, pos_own, prefix_len)
    s_oth = scores_of(q3, k_oth, pos_own, pos_oth, prefix_len)
    row_top = jnp.maximum(jnp.max(s_own, axis=-1, keepdims=True), jnp.max(s_oth, axis=-1, keepdims=True))
    e_own = jnp.exp(s_own - row_top)
    e_oth = jnp.exp(s_oth - row_top)
    row_total = jnp.sum(e_own, axis=-1, keepdims=True) + jnp.sum(e_oth, axis=-1, keepdims=True)
    p_own = (e_own / row_total).astype(bf16)
    p_oth = (e_oth / row_total).astype(bf16)
    attended = jnp.einsum("hqk,khe->qhe", p_own, v3, preferred_element_type=f32) + jnp.einsum(
        "hqk,khe->qhe", p_oth, v_oth, preferred_element_type=f32
    )
    log_sums = row_top + jnp.log(row_total)
    attended = attended.reshape(rows, width).astype(bf16)
    q_rcv, lse_rcv = lax.ppermute((q3, log_sums), "tensor", to_first)

    middle = in_rows + dot_right(attended, full_out) + b_out.astype(f32)
    normed_two = layer_norm(middle, gain_second, shift_second).astype(bf16)
    pre_act = dot_right(normed_two, full_up) + b_up.astype(f32)
    activated = gelu_exact(pre_act).astype(bf16)
    result = (middle + dot_right(activated, full_down) + b_down.astype(f32)).astype(bf16)

    grad_result = cotangent.astype(f32)
    down_t_grad = dot_over_rows(cotangent, activated)
    grad_act = dot_back(cotangent, full_down)
    down_t_grad, grad_act = lax.optimization_barrier((down_t_grad, grad_act))
    down_rows = scatter_rows(down_t_grad)
    grad_pre = jax.vjp(gelu_exact, pre_act)[1](grad_act)[0].astype(bf16)
    up_grad = dot_over_rows(normed_two, grad_pre)
    grad_norm_two = dot_back(grad_pre, full_up)
    up_grad, grad_norm_two = lax.optimization_barrier((up_grad, grad_norm_two))
    up_rows = scatter_rows(up_grad)
    norm_two_back = jax.vjp(layer_norm, middle, gain_second, shift_second)[1](grad_norm_two)
    grad_middle = grad_result + norm_two_back[0]
    grad_attn_rows = grad_middle.astype(bf16)
    out_t_grad = dot_over_rows(grad_attn_rows, attended)
    grad_attended = dot_back(grad_attn_rows, full_out).astype(bf16)
    out_t_grad, grad_attended = lax.optimization_barrier((out_t_grad, grad_attended))
    out_rows = scatter_rows(out_t_grad)
    do3 = grad_attended.reshape(shape3)

    scaling = HEAD ** (-0.5)
    prob_own = jnp.exp(s_own - log_sums)
    prob_oth = jnp.exp(s_oth - log_sums)
    dp_own = jnp.einsum("qhe,khe->hqk", do3, v3, preferred_element_type=f32)
    dp_oth = jnp.einsum("qhe,khe->hqk", do3, v_oth, preferred_element_type=f32)
    delta = jnp.sum(prob_own * dp_own, axis=-1, keepdims=True) + jnp.sum(
        prob_oth * dp_oth, axis=-1, keepdims=True
    )
    do_rcv, delta_rcv = lax.ppermute((do3, delta), "tensor", to_first)
    ds_own = (prob_own * (dp_own - delta)).astype(bf16)
    ds_oth = (prob_oth * (dp_oth - delta)).astype(bf16)
    dq = (
        jnp.einsum("hqk,khe->qhe", ds_own, k3, preferred_element_type=f32)
        + jnp.einsum("hqk,khe->qhe", ds_oth, k_oth, preferred_element_type=f32)
    ) * scaling
    dk = jnp.einsum("hqk,qhe->khe", ds_own, q3, preferred_element_type=f32)
    dv = jnp.einsum("hqk,qhe->khe", prob_own.astype(bf16), do3, preferred_element_type=f32)
    s_x = scores_of(q_rcv, k3, pos_oth, pos_own, prefix_len)
    prob_x = jnp.exp(s_x - lse_rcv)
    dp_x = jnp.einsum("qhe,khe->hqk", do_rcv, v3, preferred_element_type=f32)
    ds_x = (prob_x * (dp_x - delta_rcv)).astype(bf16)
    dk = (dk + jnp.einsum("hqk,qhe->khe", ds_x, q_rcv, preferred_element_type=f32)) * scaling
    dv = dv + jnp.einsum("hqk,qhe->khe", prob_x.astype(bf16), do_rcv, preferred_element_type=f32)

    grad_q = dq.reshape(rows, width).astype(bf16)
    grad_k = dk.reshape(rows, width).astype(bf16)
    grad_v = dv.reshape(rows, width).astype(bf16)
    grad_qkv = jnp.concatenate([grad_q, grad_k, grad_v], axis=1)
    qkv_rows = scatter_rows(dot_over_rows(normed_one, grad_qkv))
    grad_norm_one = dot_back(grad_q, full_query) + dot_back(grad_k, full_key) + dot_back(grad_v, full_value)
    norm_one_back = jax.vjp(layer_norm, in_rows, gain_first, shift_first)[1](grad_norm_one)
    grad_input = grad_middle + norm_one_back[0]

    shard_query, shard_key, shard_value, shard_out_t, shard_up, shard_down_t = scatter_cols_joined(
        [qkv_rows[:, :width], qkv_rows[:, width : 2 * width], qkv_rows[:, 2 * width :], out_rows, up_rows, down_rows],
        tp,
    )
    shard_out = shard_out_t.T
    shard_down = shard_down_t.T
    vector_sums = lax.psum(
        (
            jnp.sum(grad_q, axis=0, dtype=f32),
            jnp.sum(grad_v, axis=0, dtype=f32),
            jnp.sum(grad_middle, axis=0),
            jnp.sum(grad_pre, axis=0, dtype=f32),
            jnp.sum(grad_result, axis=0),
            norm_one_back[1],
            norm_one_back[2],
            norm_two_back[1],
            norm_two_back[2],
        ),
        AXES,
    )
    return (
        result,
        grad_input,
        shard_query,
        shard_key,
        shard_value,
        shard_out,
        shard_up,
        shard_down,
    ) + tuple(vector_sums)


def solution(mesh):
    rows_spec = P(("dp", "tensor"), None)
    placed = (
        rows_spec,
        P("dp"),
        rows_spec,
        P("dp", "tensor"),
        P("dp", "tensor"),
        P("dp", "tensor"),
        P("tensor", "dp"),
        P("dp", "tensor"),
        P("tensor", "dp"),
    ) + (P(),) * 9
    return jax.shard_map(
        layer,
        mesh=mesh,
        in_specs=placed,
        out_specs=(
            rows_spec,
            rows_spec,
            P("dp", "tensor"),
            P("dp", "tensor"),
            P("dp", "tensor"),
            P("tensor", "dp"),
            P("dp", "tensor"),
            P("tensor", "dp"),
        )
        + (P(),) * 9,
        check_vma=False,
    )
```

```python
import jax
import jax.numpy as jnp
from jax import lax
from jax.sharding import PartitionSpec as P


HEAD = 64
SEQ_LEN = 1024

norm_eps = 1e-12
masked_score = -1e30


def layer_norm(values, norm_gain, norm_shift):
    center = values - jnp.mean(values, axis=-1, keepdims=True)
    spread = jnp.mean(center * center, axis=-1, keepdims=True)
    return center * lax.rsqrt(spread + norm_eps) * norm_gain + norm_shift


def gelu_exact(values):
    return jax.nn.gelu(values, approximate=False)


def dot_right(first_op, second_op):
    return jnp.dot(first_op, second_op, preferred_element_type=jnp.float32)


def dot_back(first_op, second_op):
    return lax.dot_general(
        first_op, second_op, (((1,), (1,)), ((), ())), preferred_element_type=jnp.float32
    )


def dot_over_rows(first_op, second_op):
    return lax.dot_general(
        first_op, second_op, (((0,), (0,)), ((), ())), preferred_element_type=jnp.float32
    )


AXES = ("dp", "tensor")


def gather_joined(shards, dp, tp):
    r = shards[0].shape[0]
    joined = jnp.concatenate(shards, axis=1)
    full = lax.all_gather(joined, AXES, axis=0, tiled=False).reshape(dp, tp, r, -1)
    out = []
    start = 0
    for piece in shards:
        c = piece.shape[1]
        block = full[:, :, :, start : start + c]
        out.append(block.transpose(0, 2, 1, 3).reshape(dp * r, tp * c))
        start += c
    return out


LINK = jnp.bfloat16


def scatter_rows(grad, axis=0):
    return lax.psum_scatter(grad.astype(LINK), "dp", scatter_dimension=axis, tiled=True)


def scatter_cols_joined(pieces, tp):
    parts = []
    for piece in pieces:
        r, c = piece.shape
        parts.append(piece.reshape(r, tp, c // tp).transpose(1, 0, 2))
    joined = jnp.concatenate(parts, axis=2)
    mine = lax.psum_scatter(joined, "tensor", scatter_dimension=0, tiled=False).astype(jnp.float32)
    out = []
    start = 0
    for piece in pieces:
        c = piece.shape[1] // tp
        out.append(mine[:, start : start + c])
        start += c
    return out


def scores_of(queries, key_rows, qpos, kpos, prefix_len):
    scaling = HEAD ** (-0.5)
    scores = jnp.einsum("qhe,khe->hqk", queries, key_rows, preferred_element_type=jnp.float32) * scaling
    visible = (kpos[None, :] <= qpos[:, None]) | (kpos[None, :] < prefix_len)
    return jnp.where(visible[None], scores, masked_score)


def layer(
    inputs,
    prefix,
    cotangent,
    w_query,
    w_key,
    w_value,
    w_out,
    w_up,
    w_down,
    b_query,
    b_value,
    b_out,
    b_up,
    b_down,
    gain_one,
    shift_one,
    gain_two,
    shift_two,
):
    f32 = jnp.float32
    bf16 = jnp.bfloat16
    dp = lax.axis_size("dp")
    tp = lax.axis_size("tensor")
    t_index = lax.axis_index("tensor")
    rows = inputs.shape[0]
    pieces = SEQ_LEN // rows
    assert pieces == 2
    half = t_index % pieces
    seq_here = (t_index * rows) // SEQ_LEN
    prefix_len = lax.dynamic_index_in_dim(prefix, seq_here, keepdims=False)
    pos_own = half * rows + lax.iota(jnp.int32, rows)
    pos_oth = (1 - half) * rows + lax.iota(jnp.int32, rows)
    to_second = [(t, t + 1) for t in range(0, tp, 2)]
    to_first = [(t + 1, t) for t in range(0, tp, 2)]

    full_query, full_key, full_value, out_t = gather_joined([w_query, w_key, w_value, w_out.T], dp, tp)
    full_out = out_t.T
    full_up, down_t = gather_joined([w_up, w_down.T], dp, tp)
    full_down = down_t.T
    width = full_query.shape[1]
    heads = width // HEAD

    gain_first = gain_one.astype(f32)
    shift_first = shift_one.astype(f32)
    gain_second = gain_two.astype(f32)
    shift_second = shift_two.astype(f32)

    in_rows = inputs.astype(f32)
    normed_one = layer_norm(in_rows, gain_first, shift_first).astype(bf16)
    key_rows = dot_right(normed_one, full_key).astype(bf16)
    value_rows = (dot_right(normed_one, full_value) + b_value.astype(f32)).astype(bf16)
    queries = (dot_right(normed_one, full_query) + b_query.astype(f32)).astype(bf16)
    shape3 = (rows, heads, HEAD)
    q3 = queries.reshape(shape3)
    k3 = key_rows.reshape(shape3)
    v3 = value_rows.reshape(shape3)
    k_oth, v_oth = lax.ppermute((k3, v3), "tensor", to_second)

    s_own = scores_of(q3, k3, pos_own, pos_own, prefix_len)
    s_oth = scores_of(q3, k_oth, pos_own, pos_oth, prefix_len)
    row_top = jnp.maximum(jnp.max(s_own, axis=-1, keepdims=True), jnp.max(s_oth, axis=-1, keepdims=True))
    e_own = jnp.exp(s_own - row_top)
    e_oth = jnp.exp(s_oth - row_top)
    row_total = jnp.sum(e_own, axis=-1, keepdims=True) + jnp.sum(e_oth, axis=-1, keepdims=True)
    p_own = (e_own / row_total).astype(bf16)
    p_oth = (e_oth / row_total).astype(bf16)
    attended = jnp.einsum("hqk,khe->qhe", p_own, v3, preferred_element_type=f32) + jnp.einsum(
        "hqk,khe->qhe", p_oth, v_oth, preferred_element_type=f32
    )
    log_sums = row_top + jnp.log(row_total)
    attended = attended.reshape(rows, width).astype(bf16)
    q_rcv, lse_rcv = lax.ppermute((q3, log_sums), "tensor", to_first)

    middle = in_rows + dot_right(attended, full_out) + b_out.astype(f32)
    normed_two = layer_norm(middle, gain_second, shift_second).astype(bf16)
    pre_act = dot_right(normed_two, full_up) + b_up.astype(f32)
    activated = gelu_exact(pre_act).astype(bf16)
    result = (middle + dot_right(activated, full_down) + b_down.astype(f32)).astype(bf16)

    grad_result = cotangent.astype(f32)
    grad_act = dot_back(cotangent, full_down)
    grad_pre = jax.vjp(gelu_exact, pre_act)[1](grad_act)[0].astype(bf16)
    ffn_grad = lax.dot_general(
        jnp.stack([normed_two, cotangent]),
        jnp.stack([grad_pre, activated]),
        (((1,), (1,)), ((0,), (0,))),
        preferred_element_type=f32,
    )
    grad_norm_two = dot_back(grad_pre, full_up)
    ffn_grad, grad_norm_two = lax.optimization_barrier((ffn_grad, grad_norm_two))
    ffn_rows = scatter_rows(ffn_grad, axis=1)
    up_rows = ffn_rows[0]
    down_rows = ffn_rows[1]
    norm_two_back = jax.vjp(layer_norm, middle, gain_second, shift_second)[1](grad_norm_two)
    grad_middle = grad_result + norm_two_back[0]
    grad_attn_rows = grad_middle.astype(bf16)
    grad_attended = dot_back(grad_attn_rows, full_out).astype(bf16)
    do3 = grad_attended.reshape(shape3)

    scaling = HEAD ** (-0.5)
    prob_own = jnp.exp(s_own - log_sums)
    prob_oth = jnp.exp(s_oth - log_sums)
    dp_own = jnp.einsum("qhe,khe->hqk", do3, v3, preferred_element_type=f32)
    dp_oth = jnp.einsum("qhe,khe->hqk", do3, v_oth, preferred_element_type=f32)
    delta = jnp.sum(prob_own * dp_own, axis=-1, keepdims=True) + jnp.sum(
        prob_oth * dp_oth, axis=-1, keepdims=True
    )
    do_rcv, delta_rcv = lax.ppermute((do3, delta), "tensor", to_first)
    ds_own = (prob_own * (dp_own - delta)).astype(bf16)
    ds_oth = (prob_oth * (dp_oth - delta)).astype(bf16)
    dq = (
        jnp.einsum("hqk,khe->qhe", ds_own, k3, preferred_element_type=f32)
        + jnp.einsum("hqk,khe->qhe", ds_oth, k_oth, preferred_element_type=f32)
    ) * scaling
    dk = jnp.einsum("hqk,qhe->khe", ds_own, q3, preferred_element_type=f32)
    dv = jnp.einsum("hqk,qhe->khe", prob_own.astype(bf16), do3, preferred_element_type=f32)
    s_x = scores_of(q_rcv, k3, pos_oth, pos_own, prefix_len)
    prob_x = jnp.exp(s_x - lse_rcv)
    dp_x = jnp.einsum("qhe,khe->hqk", do_rcv, v3, preferred_element_type=f32)
    ds_x = (prob_x * (dp_x - delta_rcv)).astype(bf16)
    dk = (dk + jnp.einsum("hqk,qhe->khe", ds_x, q_rcv, preferred_element_type=f32)) * scaling
    dv = dv + jnp.einsum("hqk,qhe->khe", prob_x.astype(bf16), do_rcv, preferred_element_type=f32)

    grad_q = dq.reshape(rows, width).astype(bf16)
    grad_k = dk.reshape(rows, width).astype(bf16)
    grad_v = dv.reshape(rows, width).astype(bf16)
    grad_qkv = jnp.concatenate([grad_q, grad_k, grad_v], axis=1)
    attn_grad = jnp.concatenate(
        [dot_over_rows(normed_one, grad_qkv), dot_over_rows(grad_attn_rows, attended)], axis=1
    )
    attn_rows = scatter_rows(attn_grad)
    qkv_rows = attn_rows[:, : 3 * width]
    out_rows = attn_rows[:, 3 * width :]
    grad_norm_one = dot_back(grad_q, full_query) + dot_back(grad_k, full_key) + dot_back(grad_v, full_value)
    norm_one_back = jax.vjp(layer_norm, in_rows, gain_first, shift_first)[1](grad_norm_one)
    grad_input = grad_middle + norm_one_back[0]

    shard_query, shard_key, shard_value, shard_out_t, shard_up, shard_down_t = scatter_cols_joined(
        [qkv_rows[:, :width], qkv_rows[:, width : 2 * width], qkv_rows[:, 2 * width :], out_rows, up_rows, down_rows],
        tp,
    )
    shard_out = shard_out_t.T
    shard_down = shard_down_t.T
    vector_sums = lax.psum(
        (
        jnp.sum(grad_q, axis=0, dtype=f32),
        jnp.sum(grad_v, axis=0, dtype=f32),
        jnp.sum(grad_middle, axis=0),
        jnp.sum(grad_pre, axis=0, dtype=f32),
        jnp.sum(grad_result, axis=0),
        norm_one_back[1],
        norm_one_back[2],
        norm_two_back[1],
        norm_two_back[2],
        ),
        AXES,
    )
    return (
        result,
        grad_input,
        shard_query,
        shard_key,
        shard_value,
        shard_out,
        shard_up,
        shard_down,
    ) + tuple(vector_sums)


def solution(mesh):
    rows_spec = P(("dp", "tensor"), None)
    placed = (
        rows_spec,
        P("dp"),
        rows_spec,
        P("dp", "tensor"),
        P("dp", "tensor"),
        P("dp", "tensor"),
        P("tensor", "dp"),
        P("dp", "tensor"),
        P("tensor", "dp"),
    ) + (P(),) * 9
    return jax.shard_map(
        layer,
        mesh=mesh,
        in_specs=placed,
        out_specs=(
            rows_spec,
            rows_spec,
            P("dp", "tensor"),
            P("dp", "tensor"),
            P("dp", "tensor"),
            P("tensor", "dp"),
            P("dp", "tensor"),
            P("tensor", "dp"),
        )
        + (P(),) * 9,
        check_vma=False,
    )
```

```python
import jax
import jax.numpy as jnp
from jax import lax
from jax.sharding import PartitionSpec as P

from jax.experimental import pallas as pl
from jax.experimental.pallas import tpu as pltpu


HEAD = 64
SEQ_LEN = 1024

norm_eps = 1e-12
masked_score = -1e30


def layer_norm(values, norm_gain, norm_shift):
    center = values - jnp.mean(values, axis=-1, keepdims=True)
    spread = jnp.mean(center * center, axis=-1, keepdims=True)
    return center * lax.rsqrt(spread + norm_eps) * norm_gain + norm_shift


def gelu_exact(values):
    return jax.nn.gelu(values, approximate=False)


def dot_right(first_op, second_op):
    return jnp.dot(first_op, second_op, preferred_element_type=jnp.float32)


def dot_back(first_op, second_op):
    return lax.dot_general(
        first_op, second_op, (((1,), (1,)), ((), ())), preferred_element_type=jnp.float32
    )


def dot_over_rows(first_op, second_op):
    return lax.dot_general(
        first_op, second_op, (((0,), (0,)), ((), ())), preferred_element_type=jnp.float32
    )


AXES = ("dp", "tensor")


def gather_joined(shards, dp, tp):
    r = shards[0].shape[0]
    joined = jnp.concatenate(shards, axis=1)
    full = lax.all_gather(joined, AXES, axis=0, tiled=False).reshape(dp, tp, r, -1)
    out = []
    start = 0
    for piece in shards:
        c = piece.shape[1]
        block = full[:, :, :, start : start + c]
        out.append(block.transpose(0, 2, 1, 3).reshape(dp * r, tp * c))
        start += c
    return out


LINK = jnp.bfloat16


def scatter_rows(grad, axis=0):
    return lax.psum_scatter(grad.astype(LINK), "dp", scatter_dimension=axis, tiled=True)


def scatter_cols_joined(pieces, tp):
    parts = []
    for piece in pieces:
        r, c = piece.shape
        parts.append(piece.reshape(r, tp, c // tp).transpose(1, 0, 2))
    joined = jnp.concatenate(parts, axis=2)
    mine = lax.psum_scatter(joined, "tensor", scatter_dimension=0, tiled=False).astype(jnp.float32)
    out = []
    start = 0
    for piece in pieces:
        c = piece.shape[1] // tp
        out.append(mine[:, start : start + c])
        start += c
    return out


NT = (((1,), (1,)), ((), ()))
LANES = 128


def attn_fwd_kernel(meta_ref, q_ref, k_ref, v_ref, ko_ref, vo_ref, o_ref, of_ref, lse_ref):
    half = meta_ref[0]
    prefix_len = meta_ref[1]
    rows = q_ref.shape[1]
    scale = HEAD ** (-0.5)
    q = q_ref[0]
    s = lax.dot_general(q, k_ref[0], NT, preferred_element_type=jnp.float32) * scale
    row = lax.broadcasted_iota(jnp.int32, s.shape, 0)
    col = lax.broadcasted_iota(jnp.int32, s.shape, 1)
    visible = (col <= row) | (half * rows + col < prefix_len)
    s = jnp.where(visible, s, masked_score)
    so = lax.dot_general(q, ko_ref[0], NT, preferred_element_type=jnp.float32) * scale
    so = jnp.where(half == 1, so, masked_score)
    top = jnp.maximum(jnp.max(s, axis=1, keepdims=True), jnp.max(so, axis=1, keepdims=True))
    e = jnp.exp(s - top)
    eo = jnp.exp(so - top)
    total = jnp.sum(e, axis=1, keepdims=True) + jnp.sum(eo, axis=1, keepdims=True)
    inv = 1.0 / total
    p = (e * inv).astype(jnp.bfloat16)
    po = (eo * inv).astype(jnp.bfloat16)
    o = jnp.dot(p, v_ref[0], preferred_element_type=jnp.float32) + jnp.dot(
        po, vo_ref[0], preferred_element_type=jnp.float32
    )
    o_ref[0] = o.astype(o_ref.dtype)
    of_ref[0] = o
    lse_ref[0] = jnp.broadcast_to(top + jnp.log(total), (rows, LANES))


def attn_bwd_kernel(
    meta_ref, q_ref, k_ref, v_ref, do_ref, lse_ref, dl_ref, ko_ref, vo_ref, qr_ref, dor_ref, lser_ref, dlr_ref,
    dq_ref, dk_ref, dv_ref,
):
    f32 = jnp.float32
    bf16 = jnp.bfloat16
    half = meta_ref[0]
    prefix_len = meta_ref[1]
    rows = q_ref.shape[1]
    reps = rows // LANES
    scale = HEAD ** (-0.5)
    q = q_ref[0]
    k = k_ref[0]
    v = v_ref[0]
    do = do_ref[0]
    s = lax.dot_general(q, k, NT, preferred_element_type=f32) * scale
    row = lax.broadcasted_iota(jnp.int32, s.shape, 0)
    col = lax.broadcasted_iota(jnp.int32, s.shape, 1)
    visible = (col <= row) | (half * rows + col < prefix_len)
    s = jnp.where(visible, s, masked_score)
    p = jnp.exp(s - jnp.tile(lse_ref[0], (1, reps)))
    dp = lax.dot_general(do, v, NT, preferred_element_type=f32)
    ds = (p * (dp - jnp.tile(dl_ref[0], (1, reps)))).astype(bf16)
    dq = jnp.dot(ds, k, preferred_element_type=f32)
    dk = jnp.dot(ds.T, q, preferred_element_type=f32)
    dv = jnp.dot(p.astype(bf16).T, do, preferred_element_type=f32)
    second = half == 1
    xq = jnp.where(second, q, qr_ref[0])
    xdo = jnp.where(second, do, dor_ref[0])
    xlse = jnp.tile(jnp.where(second, lse_ref[0], lser_ref[0]), (1, reps))
    xdl = jnp.tile(jnp.where(second, dl_ref[0], dlr_ref[0]), (1, reps))
    xk = jnp.where(second, ko_ref[0], k)
    xv = jnp.where(second, vo_ref[0], v)
    s2 = lax.dot_general(xq, xk, NT, preferred_element_type=f32) * scale
    p2 = jnp.exp(s2 - xlse)
    dp2 = lax.dot_general(xdo, xv, NT, preferred_element_type=f32)
    ds2 = (p2 * (dp2 - xdl)).astype(bf16)
    dq_x = jnp.dot(ds2, xk, preferred_element_type=f32)
    dk_x = jnp.dot(ds2.T, xq, preferred_element_type=f32)
    dv_x = jnp.dot(p2.astype(bf16).T, xdo, preferred_element_type=f32)
    dq = dq + jnp.where(second, dq_x, 0.0)
    dk = dk + jnp.where(second, 0.0, dk_x)
    dv = dv + jnp.where(second, 0.0, dv_x)
    dq_ref[0] = (dq * scale).astype(dq_ref.dtype)
    dk_ref[0] = (dk * scale).astype(dk_ref.dtype)
    dv_ref[0] = dv.astype(dv_ref.dtype)


def head_spec(shape):
    return pl.BlockSpec((1,) + tuple(shape[1:]), lambda h, meta: (h, 0, 0))


def attention_forward(meta, q, k, v, ko, vo):
    heads, rows, size = q.shape
    spec = head_spec(q.shape)
    lse_spec = head_spec((heads, rows, LANES))
    return pl.pallas_call(
        attn_fwd_kernel,
        out_shape=(
            jax.ShapeDtypeStruct(q.shape, jnp.bfloat16),
            jax.ShapeDtypeStruct(q.shape, jnp.float32),
            jax.ShapeDtypeStruct((heads, rows, LANES), jnp.float32),
        ),
        grid_spec=pltpu.PrefetchScalarGridSpec(
            num_scalar_prefetch=1,
            grid=(heads,),
            in_specs=[spec] * 5,
            out_specs=(spec, spec, lse_spec),
        ),
        cost_estimate=pl.CostEstimate(
            flops=8 * heads * rows * rows * size,
            transcendentals=2 * heads * rows * rows,
            bytes_accessed=5 * q.size * 2 + q.size * 6 + heads * rows * LANES * 4,
        ),
    )(meta, q, k, v, ko, vo)


def attention_backward(meta, q, k, v, do, lse, dl, ko, vo, qr, dor, lser, dlr):
    heads, rows, size = q.shape
    spec = head_spec(q.shape)
    lse_spec = head_spec(lse.shape)
    return pl.pallas_call(
        attn_bwd_kernel,
        out_shape=tuple(jax.ShapeDtypeStruct(q.shape, jnp.bfloat16) for _ in range(3)),
        grid_spec=pltpu.PrefetchScalarGridSpec(
            num_scalar_prefetch=1,
            grid=(heads,),
            in_specs=[spec, spec, spec, spec, lse_spec, lse_spec, spec, spec, spec, spec, lse_spec, lse_spec],
            out_specs=(spec, spec, spec),
        ),
        cost_estimate=pl.CostEstimate(
            flops=20 * heads * rows * rows * size,
            transcendentals=2 * heads * rows * rows,
            bytes_accessed=11 * q.size * 2 + 4 * lse.size * 4,
        ),
    )(meta, q, k, v, do, lse, dl, ko, vo, qr, dor, lser, dlr)


def layer(
    inputs,
    prefix,
    cotangent,
    w_query,
    w_key,
    w_value,
    w_out,
    w_up,
    w_down,
    b_query,
    b_value,
    b_out,
    b_up,
    b_down,
    gain_one,
    shift_one,
    gain_two,
    shift_two,
):
    f32 = jnp.float32
    bf16 = jnp.bfloat16
    dp = lax.axis_size("dp")
    tp = lax.axis_size("tensor")
    t_index = lax.axis_index("tensor")
    rows = inputs.shape[0]
    pieces = SEQ_LEN // rows
    assert pieces == 2
    half = t_index % pieces
    seq_here = (t_index * rows) // SEQ_LEN
    prefix_len = lax.dynamic_index_in_dim(prefix, seq_here, keepdims=False)
    to_second = [(t, t + 1) for t in range(0, tp, 2)]
    to_first = [(t + 1, t) for t in range(0, tp, 2)]

    full_query, full_key, full_value, out_t = gather_joined([w_query, w_key, w_value, w_out.T], dp, tp)
    full_out = out_t.T
    full_up, down_t = gather_joined([w_up, w_down.T], dp, tp)
    full_down = down_t.T
    width = full_query.shape[1]
    heads = width // HEAD

    gain_first = gain_one.astype(f32)
    shift_first = shift_one.astype(f32)
    gain_second = gain_two.astype(f32)
    shift_second = shift_two.astype(f32)

    in_rows = inputs.astype(f32)
    normed_one = layer_norm(in_rows, gain_first, shift_first).astype(bf16)
    key_rows = dot_right(normed_one, full_key).astype(bf16)
    value_rows = (dot_right(normed_one, full_value) + b_value.astype(f32)).astype(bf16)
    queries = (dot_right(normed_one, full_query) + b_query.astype(f32)).astype(bf16)

    def by_heads(x):
        return x.reshape(rows, heads, HEAD).transpose(1, 0, 2)

    meta = jnp.stack([half, prefix_len]).astype(jnp.int32)
    q3 = by_heads(queries)
    k3 = by_heads(key_rows)
    v3 = by_heads(value_rows)
    k_oth, v_oth = lax.ppermute((k3, v3), "tensor", to_second)
    o_heads, o_full, lse_wide = attention_forward(meta, q3, k3, v3, k_oth, v_oth)
    attended = o_heads.transpose(1, 0, 2).reshape(rows, width)
    q_rcv, lse_rcv = lax.ppermute((q3, lse_wide[:, :, 0]), "tensor", to_first)

    middle = in_rows + dot_right(attended, full_out) + b_out.astype(f32)
    normed_two = layer_norm(middle, gain_second, shift_second).astype(bf16)
    pre_act = dot_right(normed_two, full_up) + b_up.astype(f32)
    activated = gelu_exact(pre_act).astype(bf16)
    result = (middle + dot_right(activated, full_down) + b_down.astype(f32)).astype(bf16)

    grad_result = cotangent.astype(f32)
    grad_act = dot_back(cotangent, full_down)
    grad_pre = jax.vjp(gelu_exact, pre_act)[1](grad_act)[0].astype(bf16)
    ffn_grad = lax.dot_general(
        jnp.stack([normed_two, cotangent]),
        jnp.stack([grad_pre, activated]),
        (((1,), (1,)), ((0,), (0,))),
        preferred_element_type=f32,
    )
    grad_norm_two = dot_back(grad_pre, full_up)
    ffn_grad, grad_norm_two = lax.optimization_barrier((ffn_grad, grad_norm_two))
    ffn_rows = scatter_rows(ffn_grad, axis=1)
    up_rows = ffn_rows[0]
    down_rows = ffn_rows[1]
    norm_two_back = jax.vjp(layer_norm, middle, gain_second, shift_second)[1](grad_norm_two)
    grad_middle = grad_result + norm_two_back[0]
    grad_attn_rows = grad_middle.astype(bf16)
    grad_attended = dot_back(grad_attn_rows, full_out).astype(bf16)

    do3 = by_heads(grad_attended)
    delta = jnp.sum(do3.astype(f32) * o_full, axis=-1)
    do_rcv, delta_rcv = lax.ppermute((do3, delta), "tensor", to_first)

    def wide(x):
        return jnp.broadcast_to(x[:, :, None], x.shape + (LANES,))

    dq3, dk3, dv3 = attention_backward(
        meta, q3, k3, v3, do3, lse_wide, wide(delta), k_oth, v_oth, q_rcv, do_rcv, wide(lse_rcv), wide(delta_rcv)
    )

    def by_rows(x):
        return x.transpose(1, 0, 2).reshape(rows, width)

    grad_q = by_rows(dq3)
    grad_k = by_rows(dk3)
    grad_v = by_rows(dv3)
    grad_qkv = jnp.concatenate([grad_q, grad_k, grad_v], axis=1)
    attn_grad = jnp.concatenate(
        [dot_over_rows(normed_one, grad_qkv), dot_over_rows(grad_attn_rows, attended)], axis=1
    )
    attn_rows = scatter_rows(attn_grad)
    qkv_rows = attn_rows[:, : 3 * width]
    out_rows = attn_rows[:, 3 * width :]
    grad_norm_one = dot_back(grad_q, full_query) + dot_back(grad_k, full_key) + dot_back(grad_v, full_value)
    norm_one_back = jax.vjp(layer_norm, in_rows, gain_first, shift_first)[1](grad_norm_one)
    grad_input = grad_middle + norm_one_back[0]

    shard_query, shard_key, shard_value, shard_out_t, shard_up, shard_down_t = scatter_cols_joined(
        [qkv_rows[:, :width], qkv_rows[:, width : 2 * width], qkv_rows[:, 2 * width :], out_rows, up_rows, down_rows],
        tp,
    )
    shard_out = shard_out_t.T
    shard_down = shard_down_t.T
    vector_sums = lax.psum(
        (
        jnp.sum(grad_q, axis=0, dtype=f32),
        jnp.sum(grad_v, axis=0, dtype=f32),
        jnp.sum(grad_middle, axis=0),
        jnp.sum(grad_pre, axis=0, dtype=f32),
        jnp.sum(grad_result, axis=0),
        norm_one_back[1],
        norm_one_back[2],
        norm_two_back[1],
        norm_two_back[2],
        ),
        AXES,
    )
    return (
        result,
        grad_input,
        shard_query,
        shard_key,
        shard_value,
        shard_out,
        shard_up,
        shard_down,
    ) + tuple(vector_sums)


def solution(mesh):
    rows_spec = P(("dp", "tensor"), None)
    placed = (
        rows_spec,
        P("dp"),
        rows_spec,
        P("dp", "tensor"),
        P("dp", "tensor"),
        P("dp", "tensor"),
        P("tensor", "dp"),
        P("dp", "tensor"),
        P("tensor", "dp"),
    ) + (P(),) * 9
    return jax.shard_map(
        layer,
        mesh=mesh,
        in_specs=placed,
        out_specs=(
            rows_spec,
            rows_spec,
            P("dp", "tensor"),
            P("dp", "tensor"),
            P("dp", "tensor"),
            P("tensor", "dp"),
            P("dp", "tensor"),
            P("tensor", "dp"),
        )
        + (P(),) * 9,
        check_vma=False,
    )
```

```python
import jax
import jax.numpy as jnp
from jax import lax
from jax.sharding import PartitionSpec as P

from jax.experimental import pallas as pl
from jax.experimental.pallas import tpu as pltpu


HEAD = 64
SEQ_LEN = 1024

norm_eps = 1e-12
masked_score = -1e30


def layer_norm(values, norm_gain, norm_shift):
    center = values - jnp.mean(values, axis=-1, keepdims=True)
    spread = jnp.mean(center * center, axis=-1, keepdims=True)
    return center * lax.rsqrt(spread + norm_eps) * norm_gain + norm_shift


def gelu_exact(values):
    return jax.nn.gelu(values, approximate=False)


def dot_right(first_op, second_op):
    return jnp.dot(first_op, second_op, preferred_element_type=jnp.float32)


def dot_back(first_op, second_op):
    return lax.dot_general(
        first_op, second_op, (((1,), (1,)), ((), ())), preferred_element_type=jnp.float32
    )


def dot_over_rows(first_op, second_op):
    return lax.dot_general(
        first_op, second_op, (((0,), (0,)), ((), ())), preferred_element_type=jnp.float32
    )


AXES = ("dp", "tensor")


def gather_joined(shards, dp, tp):
    r = shards[0].shape[0]
    joined = jnp.concatenate(shards, axis=1)
    full = lax.all_gather(joined, AXES, axis=0, tiled=False).reshape(dp, tp, r, -1)
    out = []
    start = 0
    for piece in shards:
        c = piece.shape[1]
        block = full[:, :, :, start : start + c]
        out.append(block.transpose(0, 2, 1, 3).reshape(dp * r, tp * c))
        start += c
    return out


LINK = jnp.bfloat16


def scatter_rows(grad, axis=0):
    return lax.psum_scatter(grad.astype(LINK), "dp", scatter_dimension=axis, tiled=True)


def scatter_cols_joined(pieces, tp):
    parts = []
    for piece in pieces:
        r, c = piece.shape
        parts.append(piece.reshape(r, tp, c // tp).transpose(1, 0, 2))
    joined = jnp.concatenate(parts, axis=2)
    mine = lax.psum_scatter(joined, "tensor", scatter_dimension=0, tiled=False).astype(jnp.float32)
    out = []
    start = 0
    for piece in pieces:
        c = piece.shape[1] // tp
        out.append(mine[:, start : start + c])
        start += c
    return out


NT = (((1,), (1,)), ((), ()))
LANES = 128


def attn_fwd_kernel(meta_ref, q_ref, k_ref, v_ref, ko_ref, vo_ref, o_ref, of_ref, lse_ref):
    half = meta_ref[0]
    prefix_len = meta_ref[1]
    rows = q_ref.shape[1]
    scale = HEAD ** (-0.5)
    q = q_ref[0]
    s = lax.dot_general(q, k_ref[0], NT, preferred_element_type=jnp.float32) * scale
    row = lax.broadcasted_iota(jnp.int32, s.shape, 0)
    col = lax.broadcasted_iota(jnp.int32, s.shape, 1)
    visible = (col <= row) | (half * rows + col < prefix_len)
    s = jnp.where(visible, s, masked_score)
    so = lax.dot_general(q, ko_ref[0], NT, preferred_element_type=jnp.float32) * scale
    so = jnp.where(half == 1, so, masked_score)
    top = jnp.maximum(jnp.max(s, axis=1, keepdims=True), jnp.max(so, axis=1, keepdims=True))
    e = jnp.exp(s - top)
    eo = jnp.exp(so - top)
    total = jnp.sum(e, axis=1, keepdims=True) + jnp.sum(eo, axis=1, keepdims=True)
    inv = 1.0 / total
    p = (e * inv).astype(jnp.bfloat16)
    po = (eo * inv).astype(jnp.bfloat16)
    o = jnp.dot(p, v_ref[0], preferred_element_type=jnp.float32) + jnp.dot(
        po, vo_ref[0], preferred_element_type=jnp.float32
    )
    o_ref[0] = o.astype(o_ref.dtype)
    of_ref[0] = o
    lse_ref[0] = jnp.broadcast_to(top + jnp.log(total), (rows, LANES))


def attn_bwd_kernel(
    meta_ref, q_ref, k_ref, v_ref, do_ref, lse_ref, dl_ref, ko_ref, vo_ref, qr_ref, dor_ref, lser_ref, dlr_ref,
    dq_ref, dk_ref, dv_ref,
):
    f32 = jnp.float32
    bf16 = jnp.bfloat16
    half = meta_ref[0]
    prefix_len = meta_ref[1]
    rows = q_ref.shape[1]
    reps = rows // LANES
    scale = HEAD ** (-0.5)
    q = q_ref[0]
    k = k_ref[0]
    v = v_ref[0]
    do = do_ref[0]
    s = lax.dot_general(q, k, NT, preferred_element_type=f32) * scale
    row = lax.broadcasted_iota(jnp.int32, s.shape, 0)
    col = lax.broadcasted_iota(jnp.int32, s.shape, 1)
    visible = (col <= row) | (half * rows + col < prefix_len)
    s = jnp.where(visible, s, masked_score)
    p = jnp.exp(s - jnp.tile(lse_ref[0], (1, reps)))
    dp = lax.dot_general(do, v, NT, preferred_element_type=f32)
    ds = (p * (dp - jnp.tile(dl_ref[0], (1, reps)))).astype(bf16)
    dq = jnp.dot(ds, k, preferred_element_type=f32)
    dk = jnp.dot(ds.T, q, preferred_element_type=f32)
    dv = jnp.dot(p.astype(bf16).T, do, preferred_element_type=f32)
    second = half == 1
    xq = jnp.where(second, q, qr_ref[0])
    xdo = jnp.where(second, do, dor_ref[0])
    xlse = jnp.tile(jnp.where(second, lse_ref[0], lser_ref[0]), (1, reps))
    xdl = jnp.tile(jnp.where(second, dl_ref[0], dlr_ref[0]), (1, reps))
    xk = jnp.where(second, ko_ref[0], k)
    xv = jnp.where(second, vo_ref[0], v)
    s2 = lax.dot_general(xq, xk, NT, preferred_element_type=f32) * scale
    p2 = jnp.exp(s2 - xlse)
    dp2 = lax.dot_general(xdo, xv, NT, preferred_element_type=f32)
    ds2 = (p2 * (dp2 - xdl)).astype(bf16)
    dq_x = jnp.dot(ds2, xk, preferred_element_type=f32)
    dk_x = jnp.dot(ds2.T, xq, preferred_element_type=f32)
    dv_x = jnp.dot(p2.astype(bf16).T, xdo, preferred_element_type=f32)
    dq = dq + jnp.where(second, dq_x, 0.0)
    dk = dk + jnp.where(second, 0.0, dk_x)
    dv = dv + jnp.where(second, 0.0, dv_x)
    dq_ref[0] = (dq * scale).astype(dq_ref.dtype)
    dk_ref[0] = (dk * scale).astype(dk_ref.dtype)
    dv_ref[0] = dv.astype(dv_ref.dtype)


def head_spec(shape):
    return pl.BlockSpec((1,) + tuple(shape[1:]), lambda h, meta: (h, 0, 0))


def attention_forward(meta, q, k, v, ko, vo):
    heads, rows, size = q.shape
    spec = head_spec(q.shape)
    lse_spec = head_spec((heads, rows, LANES))
    return pl.pallas_call(
        attn_fwd_kernel,
        out_shape=(
            jax.ShapeDtypeStruct(q.shape, jnp.bfloat16),
            jax.ShapeDtypeStruct(q.shape, jnp.float32),
            jax.ShapeDtypeStruct((heads, rows, LANES), jnp.float32),
        ),
        grid_spec=pltpu.PrefetchScalarGridSpec(
            num_scalar_prefetch=1,
            grid=(heads,),
            in_specs=[spec] * 5,
            out_specs=(spec, spec, lse_spec),
        ),
        cost_estimate=pl.CostEstimate(
            flops=8 * heads * rows * rows * size,
            transcendentals=2 * heads * rows * rows,
            bytes_accessed=5 * q.size * 2 + q.size * 6 + heads * rows * LANES * 4,
        ),
    )(meta, q, k, v, ko, vo)


def attention_backward(meta, q, k, v, do, lse, dl, ko, vo, qr, dor, lser, dlr):
    heads, rows, size = q.shape
    spec = head_spec(q.shape)
    lse_spec = head_spec(lse.shape)
    return pl.pallas_call(
        attn_bwd_kernel,
        out_shape=tuple(jax.ShapeDtypeStruct(q.shape, jnp.bfloat16) for _ in range(3)),
        grid_spec=pltpu.PrefetchScalarGridSpec(
            num_scalar_prefetch=1,
            grid=(heads,),
            in_specs=[spec, spec, spec, spec, lse_spec, lse_spec, spec, spec, spec, spec, lse_spec, lse_spec],
            out_specs=(spec, spec, spec),
        ),
        cost_estimate=pl.CostEstimate(
            flops=20 * heads * rows * rows * size,
            transcendentals=2 * heads * rows * rows,
            bytes_accessed=11 * q.size * 2 + 4 * lse.size * 4,
        ),
    )(meta, q, k, v, do, lse, dl, ko, vo, qr, dor, lser, dlr)


def layer(
    inputs,
    prefix,
    cotangent,
    w_query,
    w_key,
    w_value,
    w_out,
    w_up,
    w_down,
    b_query,
    b_value,
    b_out,
    b_up,
    b_down,
    gain_one,
    shift_one,
    gain_two,
    shift_two,
):
    f32 = jnp.float32
    bf16 = jnp.bfloat16
    dp = lax.axis_size("dp")
    tp = lax.axis_size("tensor")
    t_index = lax.axis_index("tensor")
    rows = inputs.shape[0]
    pieces = SEQ_LEN // rows
    assert pieces == 2
    half = t_index % pieces
    seq_here = (t_index * rows) // SEQ_LEN
    prefix_len = lax.dynamic_index_in_dim(prefix, seq_here, keepdims=False)
    to_second = [(t, t + 1) for t in range(0, tp, 2)]
    to_first = [(t + 1, t) for t in range(0, tp, 2)]

    full_query, full_key, full_value = gather_joined([w_query, w_key, w_value], dp, tp)
    out_t, full_up, down_t = gather_joined([w_out.T, w_up, w_down.T], dp, tp)
    full_out = out_t.T
    full_down = down_t.T
    width = full_query.shape[1]
    heads = width // HEAD

    gain_first = gain_one.astype(f32)
    shift_first = shift_one.astype(f32)
    gain_second = gain_two.astype(f32)
    shift_second = shift_two.astype(f32)

    in_rows = inputs.astype(f32)
    normed_one = layer_norm(in_rows, gain_first, shift_first).astype(bf16)
    key_rows = dot_right(normed_one, full_key).astype(bf16)
    value_rows = (dot_right(normed_one, full_value) + b_value.astype(f32)).astype(bf16)
    queries = (dot_right(normed_one, full_query) + b_query.astype(f32)).astype(bf16)

    def by_heads(x):
        return x.reshape(rows, heads, HEAD).transpose(1, 0, 2)

    meta = jnp.stack([half, prefix_len]).astype(jnp.int32)
    q3 = by_heads(queries)
    k3 = by_heads(key_rows)
    v3 = by_heads(value_rows)
    k_oth, v_oth = lax.ppermute((k3, v3), "tensor", to_second)
    o_heads, o_full, lse_wide = attention_forward(meta, q3, k3, v3, k_oth, v_oth)
    attended = o_heads.transpose(1, 0, 2).reshape(rows, width)
    q_rcv, lse_rcv = lax.ppermute((q3, lse_wide[:, :, 0]), "tensor", to_first)

    middle = in_rows + dot_right(attended, full_out) + b_out.astype(f32)
    normed_two = layer_norm(middle, gain_second, shift_second).astype(bf16)
    pre_act = dot_right(normed_two, full_up) + b_up.astype(f32)
    activated = gelu_exact(pre_act).astype(bf16)
    result = (middle + dot_right(activated, full_down) + b_down.astype(f32)).astype(bf16)

    grad_result = cotangent.astype(f32)
    grad_act = dot_back(cotangent, full_down)
    grad_pre = jax.vjp(gelu_exact, pre_act)[1](grad_act)[0].astype(bf16)
    ffn_grad = lax.dot_general(
        jnp.stack([normed_two, cotangent]),
        jnp.stack([grad_pre, activated]),
        (((1,), (1,)), ((0,), (0,))),
        preferred_element_type=f32,
    )
    grad_norm_two = dot_back(grad_pre, full_up)
    ffn_grad, grad_norm_two = lax.optimization_barrier((ffn_grad, grad_norm_two))
    ffn_rows = scatter_rows(ffn_grad, axis=1)
    up_rows = ffn_rows[0]
    down_rows = ffn_rows[1]
    norm_two_back = jax.vjp(layer_norm, middle, gain_second, shift_second)[1](grad_norm_two)
    grad_middle = grad_result + norm_two_back[0]
    grad_attn_rows = grad_middle.astype(bf16)
    grad_attended = dot_back(grad_attn_rows, full_out).astype(bf16)

    do3 = by_heads(grad_attended)
    delta = jnp.sum(do3.astype(f32) * o_full, axis=-1)
    do_rcv, delta_rcv = lax.ppermute((do3, delta), "tensor", to_first)

    def wide(x):
        return jnp.broadcast_to(x[:, :, None], x.shape + (LANES,))

    dq3, dk3, dv3 = attention_backward(
        meta, q3, k3, v3, do3, lse_wide, wide(delta), k_oth, v_oth, q_rcv, do_rcv, wide(lse_rcv), wide(delta_rcv)
    )

    def by_rows(x):
        return x.transpose(1, 0, 2).reshape(rows, width)

    grad_q = by_rows(dq3)
    grad_k = by_rows(dk3)
    grad_v = by_rows(dv3)
    grad_qkv = jnp.concatenate([grad_q, grad_k, grad_v], axis=1)
    attn_grad = jnp.concatenate(
        [dot_over_rows(normed_one, grad_qkv), dot_over_rows(grad_attn_rows, attended)], axis=1
    )
    attn_rows = scatter_rows(attn_grad)
    qkv_rows = attn_rows[:, : 3 * width]
    out_rows = attn_rows[:, 3 * width :]
    grad_norm_one = dot_back(grad_q, full_query) + dot_back(grad_k, full_key) + dot_back(grad_v, full_value)
    norm_one_back = jax.vjp(layer_norm, in_rows, gain_first, shift_first)[1](grad_norm_one)
    grad_input = grad_middle + norm_one_back[0]

    shard_query, shard_key, shard_value, shard_out_t, shard_up, shard_down_t = scatter_cols_joined(
        [qkv_rows[:, :width], qkv_rows[:, width : 2 * width], qkv_rows[:, 2 * width :], out_rows, up_rows, down_rows],
        tp,
    )
    shard_out = shard_out_t.T
    shard_down = shard_down_t.T
    vector_sums = lax.psum(
        (
        jnp.sum(grad_q, axis=0, dtype=f32),
        jnp.sum(grad_v, axis=0, dtype=f32),
        jnp.sum(grad_middle, axis=0),
        jnp.sum(grad_pre, axis=0, dtype=f32),
        jnp.sum(grad_result, axis=0),
        norm_one_back[1],
        norm_one_back[2],
        norm_two_back[1],
        norm_two_back[2],
        ),
        "tensor",
    )
    vector_sums = lax.psum(vector_sums, "dp")
    return (
        result,
        grad_input,
        shard_query,
        shard_key,
        shard_value,
        shard_out,
        shard_up,
        shard_down,
    ) + tuple(vector_sums)


def solution(mesh):
    rows_spec = P(("dp", "tensor"), None)
    placed = (
        rows_spec,
        P("dp"),
        rows_spec,
        P("dp", "tensor"),
        P("dp", "tensor"),
        P("dp", "tensor"),
        P("tensor", "dp"),
        P("dp", "tensor"),
        P("tensor", "dp"),
    ) + (P(),) * 9
    return jax.shard_map(
        layer,
        mesh=mesh,
        in_specs=placed,
        out_specs=(
            rows_spec,
            rows_spec,
            P("dp", "tensor"),
            P("dp", "tensor"),
            P("dp", "tensor"),
            P("tensor", "dp"),
            P("dp", "tensor"),
            P("tensor", "dp"),
        )
        + (P(),) * 9,
        check_vma=False,
    )
```

```python
import jax
import jax.numpy as jnp
from jax import lax
from jax.sharding import PartitionSpec as P

from jax.experimental import pallas as pl
from jax.experimental.pallas import tpu as pltpu


HEAD = 64
SEQ_LEN = 1024

norm_eps = 1e-12
masked_score = -1e30


def layer_norm(values, norm_gain, norm_shift):
    center = values - jnp.mean(values, axis=-1, keepdims=True)
    spread = jnp.mean(center * center, axis=-1, keepdims=True)
    return center * lax.rsqrt(spread + norm_eps) * norm_gain + norm_shift


def gelu_exact(values):
    return jax.nn.gelu(values, approximate=False)


def dot_right(first_op, second_op):
    return jnp.dot(first_op, second_op, preferred_element_type=jnp.float32)


def dot_back(first_op, second_op):
    return lax.dot_general(
        first_op, second_op, (((1,), (1,)), ((), ())), preferred_element_type=jnp.float32
    )


def dot_over_rows(first_op, second_op):
    return lax.dot_general(
        first_op, second_op, (((0,), (0,)), ((), ())), preferred_element_type=jnp.float32
    )


AXES = ("dp", "tensor")


def gather_joined(shards, dp, tp):
    r = shards[0].shape[0]
    joined = jnp.concatenate(shards, axis=1)
    pieces = [joined] + [
        lax.ppermute(joined, "tensor", [(i, (i + step) % tp) for i in range(tp)]) for step in range(1, tp)
    ]
    t_index = lax.axis_index("tensor")
    order = (t_index - jnp.arange(tp, dtype=jnp.int32)) % tp
    by_tensor = jnp.take(jnp.stack(pieces), order, axis=0)
    full = lax.all_gather(by_tensor, "dp", axis=0, tiled=False)
    out = []
    start = 0
    for piece in shards:
        c = piece.shape[1]
        block = full[:, :, :, start : start + c]
        out.append(block.transpose(0, 2, 1, 3).reshape(dp * r, tp * c))
        start += c
    return out


LINK = jnp.bfloat16


def scatter_rows(grad, axis=0):
    return lax.psum_scatter(grad.astype(LINK), "dp", scatter_dimension=axis, tiled=True)


def scatter_cols_joined(pieces, tp):
    parts = []
    for piece in pieces:
        r, c = piece.shape
        parts.append(piece.reshape(r, tp, c // tp).transpose(1, 0, 2))
    joined = jnp.concatenate(parts, axis=2)
    mine = lax.psum_scatter(joined, "tensor", scatter_dimension=0, tiled=False).astype(jnp.float32)
    out = []
    start = 0
    for piece in pieces:
        c = piece.shape[1] // tp
        out.append(mine[:, start : start + c])
        start += c
    return out


NT = (((1,), (1,)), ((), ()))
LANES = 128


def attn_fwd_kernel(meta_ref, q_ref, k_ref, v_ref, ko_ref, vo_ref, o_ref, of_ref, lse_ref):
    half = meta_ref[0]
    prefix_len = meta_ref[1]
    rows = q_ref.shape[1]
    scale = HEAD ** (-0.5)
    q = q_ref[0]
    s = lax.dot_general(q, k_ref[0], NT, preferred_element_type=jnp.float32) * scale
    row = lax.broadcasted_iota(jnp.int32, s.shape, 0)
    col = lax.broadcasted_iota(jnp.int32, s.shape, 1)
    visible = (col <= row) | (half * rows + col < prefix_len)
    s = jnp.where(visible, s, masked_score)
    so = lax.dot_general(q, ko_ref[0], NT, preferred_element_type=jnp.float32) * scale
    so = jnp.where(half == 1, so, masked_score)
    top = jnp.maximum(jnp.max(s, axis=1, keepdims=True), jnp.max(so, axis=1, keepdims=True))
    e = jnp.exp(s - top)
    eo = jnp.exp(so - top)
    total = jnp.sum(e, axis=1, keepdims=True) + jnp.sum(eo, axis=1, keepdims=True)
    inv = 1.0 / total
    p = (e * inv).astype(jnp.bfloat16)
    po = (eo * inv).astype(jnp.bfloat16)
    o = jnp.dot(p, v_ref[0], preferred_element_type=jnp.float32) + jnp.dot(
        po, vo_ref[0], preferred_element_type=jnp.float32
    )
    o_ref[0] = o.astype(o_ref.dtype)
    of_ref[0] = o
    lse_ref[0] = jnp.broadcast_to(top + jnp.log(total), (rows, LANES))


def attn_bwd_kernel(
    meta_ref, q_ref, k_ref, v_ref, do_ref, lse_ref, dl_ref, ko_ref, vo_ref, qr_ref, dor_ref, lser_ref, dlr_ref,
    dq_ref, dk_ref, dv_ref,
):
    f32 = jnp.float32
    bf16 = jnp.bfloat16
    half = meta_ref[0]
    prefix_len = meta_ref[1]
    rows = q_ref.shape[1]
    reps = rows // LANES
    scale = HEAD ** (-0.5)
    q = q_ref[0]
    k = k_ref[0]
    v = v_ref[0]
    do = do_ref[0]
    s = lax.dot_general(q, k, NT, preferred_element_type=f32) * scale
    row = lax.broadcasted_iota(jnp.int32, s.shape, 0)
    col = lax.broadcasted_iota(jnp.int32, s.shape, 1)
    visible = (col <= row) | (half * rows + col < prefix_len)
    s = jnp.where(visible, s, masked_score)
    p = jnp.exp(s - jnp.tile(lse_ref[0], (1, reps)))
    dp = lax.dot_general(do, v, NT, preferred_element_type=f32)
    ds = (p * (dp - jnp.tile(dl_ref[0], (1, reps)))).astype(bf16)
    dq = jnp.dot(ds, k, preferred_element_type=f32)
    dk = jnp.dot(ds.T, q, preferred_element_type=f32)
    dv = jnp.dot(p.astype(bf16).T, do, preferred_element_type=f32)
    second = half == 1
    xq = jnp.where(second, q, qr_ref[0])
    xdo = jnp.where(second, do, dor_ref[0])
    xlse = jnp.tile(jnp.where(second, lse_ref[0], lser_ref[0]), (1, reps))
    xdl = jnp.tile(jnp.where(second, dl_ref[0], dlr_ref[0]), (1, reps))
    xk = jnp.where(second, ko_ref[0], k)
    xv = jnp.where(second, vo_ref[0], v)
    s2 = lax.dot_general(xq, xk, NT, preferred_element_type=f32) * scale
    p2 = jnp.exp(s2 - xlse)
    dp2 = lax.dot_general(xdo, xv, NT, preferred_element_type=f32)
    ds2 = (p2 * (dp2 - xdl)).astype(bf16)
    dq_x = jnp.dot(ds2, xk, preferred_element_type=f32)
    dk_x = jnp.dot(ds2.T, xq, preferred_element_type=f32)
    dv_x = jnp.dot(p2.astype(bf16).T, xdo, preferred_element_type=f32)
    dq = dq + jnp.where(second, dq_x, 0.0)
    dk = dk + jnp.where(second, 0.0, dk_x)
    dv = dv + jnp.where(second, 0.0, dv_x)
    dq_ref[0] = (dq * scale).astype(dq_ref.dtype)
    dk_ref[0] = (dk * scale).astype(dk_ref.dtype)
    dv_ref[0] = dv.astype(dv_ref.dtype)


def head_spec(shape):
    return pl.BlockSpec((1,) + tuple(shape[1:]), lambda h, meta: (h, 0, 0))


def attention_forward(meta, q, k, v, ko, vo):
    heads, rows, size = q.shape
    spec = head_spec(q.shape)
    lse_spec = head_spec((heads, rows, LANES))
    return pl.pallas_call(
        attn_fwd_kernel,
        out_shape=(
            jax.ShapeDtypeStruct(q.shape, jnp.bfloat16),
            jax.ShapeDtypeStruct(q.shape, jnp.float32),
            jax.ShapeDtypeStruct((heads, rows, LANES), jnp.float32),
        ),
        grid_spec=pltpu.PrefetchScalarGridSpec(
            num_scalar_prefetch=1,
            grid=(heads,),
            in_specs=[spec] * 5,
            out_specs=(spec, spec, lse_spec),
        ),
        cost_estimate=pl.CostEstimate(
            flops=8 * heads * rows * rows * size,
            transcendentals=2 * heads * rows * rows,
            bytes_accessed=5 * q.size * 2 + q.size * 6 + heads * rows * LANES * 4,
        ),
    )(meta, q, k, v, ko, vo)


def attention_backward(meta, q, k, v, do, lse, dl, ko, vo, qr, dor, lser, dlr):
    heads, rows, size = q.shape
    spec = head_spec(q.shape)
    lse_spec = head_spec(lse.shape)
    return pl.pallas_call(
        attn_bwd_kernel,
        out_shape=tuple(jax.ShapeDtypeStruct(q.shape, jnp.bfloat16) for _ in range(3)),
        grid_spec=pltpu.PrefetchScalarGridSpec(
            num_scalar_prefetch=1,
            grid=(heads,),
            in_specs=[spec, spec, spec, spec, lse_spec, lse_spec, spec, spec, spec, spec, lse_spec, lse_spec],
            out_specs=(spec, spec, spec),
        ),
        cost_estimate=pl.CostEstimate(
            flops=20 * heads * rows * rows * size,
            transcendentals=2 * heads * rows * rows,
            bytes_accessed=11 * q.size * 2 + 4 * lse.size * 4,
        ),
    )(meta, q, k, v, do, lse, dl, ko, vo, qr, dor, lser, dlr)


def layer(
    inputs,
    prefix,
    cotangent,
    w_query,
    w_key,
    w_value,
    w_out,
    w_up,
    w_down,
    b_query,
    b_value,
    b_out,
    b_up,
    b_down,
    gain_one,
    shift_one,
    gain_two,
    shift_two,
):
    f32 = jnp.float32
    bf16 = jnp.bfloat16
    dp = lax.axis_size("dp")
    tp = lax.axis_size("tensor")
    t_index = lax.axis_index("tensor")
    rows = inputs.shape[0]
    pieces = SEQ_LEN // rows
    assert pieces == 2
    half = t_index % pieces
    seq_here = (t_index * rows) // SEQ_LEN
    prefix_len = lax.dynamic_index_in_dim(prefix, seq_here, keepdims=False)
    to_second = [(t, t + 1) for t in range(0, tp, 2)]
    to_first = [(t + 1, t) for t in range(0, tp, 2)]

    full_query, full_key, full_value, out_t = gather_joined([w_query, w_key, w_value, w_out.T], dp, tp)
    full_out = out_t.T
    full_up, down_t = gather_joined([w_up, w_down.T], dp, tp)
    full_down = down_t.T
    width = full_query.shape[1]
    heads = width // HEAD

    gain_first = gain_one.astype(f32)
    shift_first = shift_one.astype(f32)
    gain_second = gain_two.astype(f32)
    shift_second = shift_two.astype(f32)

    in_rows = inputs.astype(f32)
    normed_one = layer_norm(in_rows, gain_first, shift_first).astype(bf16)
    key_rows = dot_right(normed_one, full_key).astype(bf16)
    value_rows = (dot_right(normed_one, full_value) + b_value.astype(f32)).astype(bf16)
    queries = (dot_right(normed_one, full_query) + b_query.astype(f32)).astype(bf16)

    def by_heads(x):
        return x.reshape(rows, heads, HEAD).transpose(1, 0, 2)

    meta = jnp.stack([half, prefix_len]).astype(jnp.int32)
    q3 = by_heads(queries)
    k3 = by_heads(key_rows)
    v3 = by_heads(value_rows)
    k_oth, v_oth = lax.ppermute((k3, v3), "tensor", to_second)
    o_heads, o_full, lse_wide = attention_forward(meta, q3, k3, v3, k_oth, v_oth)
    attended = o_heads.transpose(1, 0, 2).reshape(rows, width)
    q_rcv, lse_rcv = lax.ppermute((q3, lse_wide[:, :, 0]), "tensor", to_first)

    middle = in_rows + dot_right(attended, full_out) + b_out.astype(f32)
    normed_two = layer_norm(middle, gain_second, shift_second).astype(bf16)
    pre_act = dot_right(normed_two, full_up) + b_up.astype(f32)
    activated = gelu_exact(pre_act).astype(bf16)
    result = (middle + dot_right(activated, full_down) + b_down.astype(f32)).astype(bf16)

    grad_result = cotangent.astype(f32)
    grad_act = dot_back(cotangent, full_down)
    grad_pre = jax.vjp(gelu_exact, pre_act)[1](grad_act)[0].astype(bf16)
    ffn_grad = lax.dot_general(
        jnp.stack([normed_two, cotangent]),
        jnp.stack([grad_pre, activated]),
        (((1,), (1,)), ((0,), (0,))),
        preferred_element_type=f32,
    )
    grad_norm_two = dot_back(grad_pre, full_up)
    ffn_grad, grad_norm_two = lax.optimization_barrier((ffn_grad, grad_norm_two))
    ffn_rows = scatter_rows(ffn_grad, axis=1)
    up_rows = ffn_rows[0]
    down_rows = ffn_rows[1]
    norm_two_back = jax.vjp(layer_norm, middle, gain_second, shift_second)[1](grad_norm_two)
    grad_middle = grad_result + norm_two_back[0]
    grad_attn_rows = grad_middle.astype(bf16)
    grad_attended = dot_back(grad_attn_rows, full_out).astype(bf16)

    do3 = by_heads(grad_attended)
    delta = jnp.sum(do3.astype(f32) * o_full, axis=-1)
    do_rcv, delta_rcv = lax.ppermute((do3, delta), "tensor", to_first)

    def wide(x):
        return jnp.broadcast_to(x[:, :, None], x.shape + (LANES,))

    dq3, dk3, dv3 = attention_backward(
        meta, q3, k3, v3, do3, lse_wide, wide(delta), k_oth, v_oth, q_rcv, do_rcv, wide(lse_rcv), wide(delta_rcv)
    )

    def by_rows(x):
        return x.transpose(1, 0, 2).reshape(rows, width)

    grad_q = by_rows(dq3)
    grad_k = by_rows(dk3)
    grad_v = by_rows(dv3)
    grad_qkv = jnp.concatenate([grad_q, grad_k, grad_v], axis=1)
    attn_grad = jnp.concatenate(
        [dot_over_rows(normed_one, grad_qkv), dot_over_rows(grad_attn_rows, attended)], axis=1
    )
    attn_rows = scatter_rows(attn_grad)
    qkv_rows = attn_rows[:, : 3 * width]
    out_rows = attn_rows[:, 3 * width :]
    grad_norm_one = dot_back(grad_q, full_query) + dot_back(grad_k, full_key) + dot_back(grad_v, full_value)
    norm_one_back = jax.vjp(layer_norm, in_rows, gain_first, shift_first)[1](grad_norm_one)
    grad_input = grad_middle + norm_one_back[0]

    shard_query, shard_key, shard_value, shard_out_t, shard_up, shard_down_t = scatter_cols_joined(
        [qkv_rows[:, :width], qkv_rows[:, width : 2 * width], qkv_rows[:, 2 * width :], out_rows, up_rows, down_rows],
        tp,
    )
    shard_out = shard_out_t.T
    shard_down = shard_down_t.T
    vector_sums = lax.psum(
        (
        jnp.sum(grad_q, axis=0, dtype=f32),
        jnp.sum(grad_v, axis=0, dtype=f32),
        jnp.sum(grad_middle, axis=0),
        jnp.sum(grad_pre, axis=0, dtype=f32),
        jnp.sum(grad_result, axis=0),
        norm_one_back[1],
        norm_one_back[2],
        norm_two_back[1],
        norm_two_back[2],
        ),
        AXES,
    )
    return (
        result,
        grad_input,
        shard_query,
        shard_key,
        shard_value,
        shard_out,
        shard_up,
        shard_down,
    ) + tuple(vector_sums)


def solution(mesh):
    rows_spec = P(("dp", "tensor"), None)
    placed = (
        rows_spec,
        P("dp"),
        rows_spec,
        P("dp", "tensor"),
        P("dp", "tensor"),
        P("dp", "tensor"),
        P("tensor", "dp"),
        P("dp", "tensor"),
        P("tensor", "dp"),
    ) + (P(),) * 9
    return jax.shard_map(
        layer,
        mesh=mesh,
        in_specs=placed,
        out_specs=(
            rows_spec,
            rows_spec,
            P("dp", "tensor"),
            P("dp", "tensor"),
            P("dp", "tensor"),
            P("tensor", "dp"),
            P("dp", "tensor"),
            P("tensor", "dp"),
        )
        + (P(),) * 9,
        check_vma=False,
    )
```

```python
import jax
import jax.numpy as jnp
from jax import lax
from jax.sharding import PartitionSpec as P

from jax.experimental import pallas as pl
from jax.experimental.pallas import tpu as pltpu


HEAD = 64
SEQ_LEN = 1024

norm_eps = 1e-12
masked_score = -1e30


def layer_norm(values, norm_gain, norm_shift):
    center = values - jnp.mean(values, axis=-1, keepdims=True)
    spread = jnp.mean(center * center, axis=-1, keepdims=True)
    return center * lax.rsqrt(spread + norm_eps) * norm_gain + norm_shift


def gelu_exact(values):
    return jax.nn.gelu(values, approximate=False)


def dot_right(first_op, second_op):
    return jnp.dot(first_op, second_op, preferred_element_type=jnp.float32)


def dot_back(first_op, second_op):
    return lax.dot_general(
        first_op, second_op, (((1,), (1,)), ((), ())), preferred_element_type=jnp.float32
    )


def dot_over_rows(first_op, second_op):
    return lax.dot_general(
        first_op, second_op, (((0,), (0,)), ((), ())), preferred_element_type=jnp.float32
    )


AXES = ("dp", "tensor")


def gather_joined(shards, dp, tp):
    r = shards[0].shape[0]
    joined = jnp.concatenate(shards, axis=1)
    pieces = [joined] + [
        lax.ppermute(joined, "tensor", [(i, (i + step) % tp) for i in range(tp)]) for step in range(1, tp)
    ]
    t_index = lax.axis_index("tensor")
    order = (t_index - jnp.arange(tp, dtype=jnp.int32)) % tp
    by_tensor = jnp.take(jnp.stack(pieces), order, axis=0)
    full = lax.all_gather(by_tensor, "dp", axis=0, tiled=False)
    out = []
    start = 0
    for piece in shards:
        c = piece.shape[1]
        block = full[:, :, :, start : start + c]
        out.append(block.transpose(0, 2, 1, 3).reshape(dp * r, tp * c))
        start += c
    return out


LINK = jnp.bfloat16


def scatter_rows(grad, axis=0):
    return lax.psum_scatter(grad.astype(LINK), "dp", scatter_dimension=axis, tiled=True)


def sum_over_tensor(pieces, tp):
    parts = []
    for piece in pieces:
        r, c = piece.shape
        parts.append(piece.reshape(r, tp, c // tp).transpose(1, 0, 2))
    joined = jnp.concatenate(parts, axis=2)
    t_index = lax.axis_index("tensor")
    mine = lax.dynamic_index_in_dim(joined, t_index, keepdims=False).astype(jnp.float32)
    for step in range(1, tp):
        sent = lax.dynamic_index_in_dim(joined, (t_index + step) % tp, keepdims=False)
        mine = mine + lax.ppermute(sent, "tensor", [(i, (i + step) % tp) for i in range(tp)]).astype(jnp.float32)
    out = []
    start = 0
    for piece in pieces:
        c = piece.shape[1] // tp
        out.append(mine[:, start : start + c])
        start += c
    return out


NT = (((1,), (1,)), ((), ()))
LANES = 128


def attn_fwd_kernel(meta_ref, q_ref, k_ref, v_ref, ko_ref, vo_ref, o_ref, of_ref, lse_ref):
    half = meta_ref[0]
    prefix_len = meta_ref[1]
    rows = q_ref.shape[1]
    scale = HEAD ** (-0.5)
    q = q_ref[0]
    s = lax.dot_general(q, k_ref[0], NT, preferred_element_type=jnp.float32) * scale
    row = lax.broadcasted_iota(jnp.int32, s.shape, 0)
    col = lax.broadcasted_iota(jnp.int32, s.shape, 1)
    visible = (col <= row) | (half * rows + col < prefix_len)
    s = jnp.where(visible, s, masked_score)
    so = lax.dot_general(q, ko_ref[0], NT, preferred_element_type=jnp.float32) * scale
    so = jnp.where(half == 1, so, masked_score)
    top = jnp.maximum(jnp.max(s, axis=1, keepdims=True), jnp.max(so, axis=1, keepdims=True))
    e = jnp.exp(s - top)
    eo = jnp.exp(so - top)
    total = jnp.sum(e, axis=1, keepdims=True) + jnp.sum(eo, axis=1, keepdims=True)
    inv = 1.0 / total
    p = (e * inv).astype(jnp.bfloat16)
    po = (eo * inv).astype(jnp.bfloat16)
    o = jnp.dot(p, v_ref[0], preferred_element_type=jnp.float32) + jnp.dot(
        po, vo_ref[0], preferred_element_type=jnp.float32
    )
    o_ref[0] = o.astype(o_ref.dtype)
    of_ref[0] = o
    lse_ref[0] = jnp.broadcast_to(top + jnp.log(total), (rows, LANES))


def attn_bwd_kernel(
    meta_ref, q_ref, k_ref, v_ref, do_ref, lse_ref, dl_ref, ko_ref, vo_ref, qr_ref, dor_ref, lser_ref, dlr_ref,
    dq_ref, dk_ref, dv_ref,
):
    f32 = jnp.float32
    bf16 = jnp.bfloat16
    half = meta_ref[0]
    prefix_len = meta_ref[1]
    rows = q_ref.shape[1]
    reps = rows // LANES
    scale = HEAD ** (-0.5)
    q = q_ref[0]
    k = k_ref[0]
    v = v_ref[0]
    do = do_ref[0]
    s = lax.dot_general(q, k, NT, preferred_element_type=f32) * scale
    row = lax.broadcasted_iota(jnp.int32, s.shape, 0)
    col = lax.broadcasted_iota(jnp.int32, s.shape, 1)
    visible = (col <= row) | (half * rows + col < prefix_len)
    s = jnp.where(visible, s, masked_score)
    p = jnp.exp(s - jnp.tile(lse_ref[0], (1, reps)))
    dp = lax.dot_general(do, v, NT, preferred_element_type=f32)
    ds = (p * (dp - jnp.tile(dl_ref[0], (1, reps)))).astype(bf16)
    dq = jnp.dot(ds, k, preferred_element_type=f32)
    dk = jnp.dot(ds.T, q, preferred_element_type=f32)
    dv = jnp.dot(p.astype(bf16).T, do, preferred_element_type=f32)
    second = half == 1
    xq = jnp.where(second, q, qr_ref[0])
    xdo = jnp.where(second, do, dor_ref[0])
    xlse = jnp.tile(jnp.where(second, lse_ref[0], lser_ref[0]), (1, reps))
    xdl = jnp.tile(jnp.where(second, dl_ref[0], dlr_ref[0]), (1, reps))
    xk = jnp.where(second, ko_ref[0], k)
    xv = jnp.where(second, vo_ref[0], v)
    s2 = lax.dot_general(xq, xk, NT, preferred_element_type=f32) * scale
    p2 = jnp.exp(s2 - xlse)
    dp2 = lax.dot_general(xdo, xv, NT, preferred_element_type=f32)
    ds2 = (p2 * (dp2 - xdl)).astype(bf16)
    dq_x = jnp.dot(ds2, xk, preferred_element_type=f32)
    dk_x = jnp.dot(ds2.T, xq, preferred_element_type=f32)
    dv_x = jnp.dot(p2.astype(bf16).T, xdo, preferred_element_type=f32)
    dq = dq + jnp.where(second, dq_x, 0.0)
    dk = dk + jnp.where(second, 0.0, dk_x)
    dv = dv + jnp.where(second, 0.0, dv_x)
    dq_ref[0] = (dq * scale).astype(dq_ref.dtype)
    dk_ref[0] = (dk * scale).astype(dk_ref.dtype)
    dv_ref[0] = dv.astype(dv_ref.dtype)


def head_spec(shape):
    return pl.BlockSpec((1,) + tuple(shape[1:]), lambda h, meta: (h, 0, 0))


def attention_forward(meta, q, k, v, ko, vo):
    heads, rows, size = q.shape
    spec = head_spec(q.shape)
    lse_spec = head_spec((heads, rows, LANES))
    return pl.pallas_call(
        attn_fwd_kernel,
        out_shape=(
            jax.ShapeDtypeStruct(q.shape, jnp.bfloat16),
            jax.ShapeDtypeStruct(q.shape, jnp.float32),
            jax.ShapeDtypeStruct((heads, rows, LANES), jnp.float32),
        ),
        grid_spec=pltpu.PrefetchScalarGridSpec(
            num_scalar_prefetch=1,
            grid=(heads,),
            in_specs=[spec] * 5,
            out_specs=(spec, spec, lse_spec),
        ),
        cost_estimate=pl.CostEstimate(
            flops=8 * heads * rows * rows * size,
            transcendentals=2 * heads * rows * rows,
            bytes_accessed=5 * q.size * 2 + q.size * 6 + heads * rows * LANES * 4,
        ),
    )(meta, q, k, v, ko, vo)


def attention_backward(meta, q, k, v, do, lse, dl, ko, vo, qr, dor, lser, dlr):
    heads, rows, size = q.shape
    spec = head_spec(q.shape)
    lse_spec = head_spec(lse.shape)
    return pl.pallas_call(
        attn_bwd_kernel,
        out_shape=tuple(jax.ShapeDtypeStruct(q.shape, jnp.bfloat16) for _ in range(3)),
        grid_spec=pltpu.PrefetchScalarGridSpec(
            num_scalar_prefetch=1,
            grid=(heads,),
            in_specs=[spec, spec, spec, spec, lse_spec, lse_spec, spec, spec, spec, spec, lse_spec, lse_spec],
            out_specs=(spec, spec, spec),
        ),
        cost_estimate=pl.CostEstimate(
            flops=20 * heads * rows * rows * size,
            transcendentals=2 * heads * rows * rows,
            bytes_accessed=11 * q.size * 2 + 4 * lse.size * 4,
        ),
    )(meta, q, k, v, do, lse, dl, ko, vo, qr, dor, lser, dlr)


def layer(
    inputs,
    prefix,
    cotangent,
    w_query,
    w_key,
    w_value,
    w_out,
    w_up,
    w_down,
    b_query,
    b_value,
    b_out,
    b_up,
    b_down,
    gain_one,
    shift_one,
    gain_two,
    shift_two,
):
    f32 = jnp.float32
    bf16 = jnp.bfloat16
    dp = lax.axis_size("dp")
    tp = lax.axis_size("tensor")
    t_index = lax.axis_index("tensor")
    rows = inputs.shape[0]
    pieces = SEQ_LEN // rows
    assert pieces == 2
    half = t_index % pieces
    seq_here = (t_index * rows) // SEQ_LEN
    prefix_len = lax.dynamic_index_in_dim(prefix, seq_here, keepdims=False)
    to_second = [(t, t + 1) for t in range(0, tp, 2)]
    to_first = [(t + 1, t) for t in range(0, tp, 2)]

    full_query, full_key, full_value, out_t = gather_joined([w_query, w_key, w_value, w_out.T], dp, tp)
    full_out = out_t.T
    full_up, down_t = gather_joined([w_up, w_down.T], dp, tp)
    full_down = down_t.T
    width = full_query.shape[1]
    heads = width // HEAD

    gain_first = gain_one.astype(f32)
    shift_first = shift_one.astype(f32)
    gain_second = gain_two.astype(f32)
    shift_second = shift_two.astype(f32)

    in_rows = inputs.astype(f32)
    normed_one = layer_norm(in_rows, gain_first, shift_first).astype(bf16)
    key_rows = dot_right(normed_one, full_key).astype(bf16)
    value_rows = (dot_right(normed_one, full_value) + b_value.astype(f32)).astype(bf16)
    queries = (dot_right(normed_one, full_query) + b_query.astype(f32)).astype(bf16)

    def by_heads(x):
        return x.reshape(rows, heads, HEAD).transpose(1, 0, 2)

    meta = jnp.stack([half, prefix_len]).astype(jnp.int32)
    q3 = by_heads(queries)
    k3 = by_heads(key_rows)
    v3 = by_heads(value_rows)
    k_oth, v_oth = lax.ppermute((k3, v3), "tensor", to_second)
    o_heads, o_full, lse_wide = attention_forward(meta, q3, k3, v3, k_oth, v_oth)
    attended = o_heads.transpose(1, 0, 2).reshape(rows, width)
    q_rcv, lse_rcv = lax.ppermute((q3, lse_wide[:, :, 0]), "tensor", to_first)

    middle = in_rows + dot_right(attended, full_out) + b_out.astype(f32)
    normed_two = layer_norm(middle, gain_second, shift_second).astype(bf16)
    pre_act = dot_right(normed_two, full_up) + b_up.astype(f32)
    activated = gelu_exact(pre_act).astype(bf16)
    result = (middle + dot_right(activated, full_down) + b_down.astype(f32)).astype(bf16)

    grad_result = cotangent.astype(f32)
    grad_act = dot_back(cotangent, full_down)
    grad_pre = jax.vjp(gelu_exact, pre_act)[1](grad_act)[0].astype(bf16)
    ffn_grad = lax.dot_general(
        jnp.stack([normed_two, cotangent]),
        jnp.stack([grad_pre, activated]),
        (((1,), (1,)), ((0,), (0,))),
        preferred_element_type=f32,
    )
    grad_norm_two = dot_back(grad_pre, full_up)
    ffn_grad, grad_norm_two = lax.optimization_barrier((ffn_grad, grad_norm_two))
    ffn_rows = scatter_rows(ffn_grad, axis=1)
    up_rows = ffn_rows[0]
    down_rows = ffn_rows[1]
    norm_two_back = jax.vjp(layer_norm, middle, gain_second, shift_second)[1](grad_norm_two)
    grad_middle = grad_result + norm_two_back[0]
    grad_attn_rows = grad_middle.astype(bf16)
    grad_attended = dot_back(grad_attn_rows, full_out).astype(bf16)

    do3 = by_heads(grad_attended)
    delta = jnp.sum(do3.astype(f32) * o_full, axis=-1)
    do_rcv, delta_rcv = lax.ppermute((do3, delta), "tensor", to_first)

    def wide(x):
        return jnp.broadcast_to(x[:, :, None], x.shape + (LANES,))

    dq3, dk3, dv3 = attention_backward(
        meta, q3, k3, v3, do3, lse_wide, wide(delta), k_oth, v_oth, q_rcv, do_rcv, wide(lse_rcv), wide(delta_rcv)
    )

    def by_rows(x):
        return x.transpose(1, 0, 2).reshape(rows, width)

    grad_q = by_rows(dq3)
    grad_k = by_rows(dk3)
    grad_v = by_rows(dv3)
    grad_qkv = jnp.concatenate([grad_q, grad_k, grad_v], axis=1)
    attn_grad = jnp.concatenate(
        [dot_over_rows(normed_one, grad_qkv), dot_over_rows(grad_attn_rows, attended)], axis=1
    )
    attn_rows = scatter_rows(attn_grad)
    qkv_rows = attn_rows[:, : 3 * width]
    out_rows = attn_rows[:, 3 * width :]
    grad_norm_one = dot_back(grad_q, full_query) + dot_back(grad_k, full_key) + dot_back(grad_v, full_value)
    norm_one_back = jax.vjp(layer_norm, in_rows, gain_first, shift_first)[1](grad_norm_one)
    grad_input = grad_middle + norm_one_back[0]

    shard_up, shard_down_t = sum_over_tensor([up_rows, down_rows], tp)
    shard_query, shard_key, shard_value, shard_out_t = sum_over_tensor(
        [qkv_rows[:, :width], qkv_rows[:, width : 2 * width], qkv_rows[:, 2 * width :], out_rows], tp
    )
    shard_out = shard_out_t.T
    shard_down = shard_down_t.T
    vector_sums = lax.psum(
        (
        jnp.sum(grad_q, axis=0, dtype=f32),
        jnp.sum(grad_v, axis=0, dtype=f32),
        jnp.sum(grad_middle, axis=0),
        jnp.sum(grad_pre, axis=0, dtype=f32),
        jnp.sum(grad_result, axis=0),
        norm_one_back[1],
        norm_one_back[2],
        norm_two_back[1],
        norm_two_back[2],
        ),
        AXES,
    )
    return (
        result,
        grad_input,
        shard_query,
        shard_key,
        shard_value,
        shard_out,
        shard_up,
        shard_down,
    ) + tuple(vector_sums)


def solution(mesh):
    rows_spec = P(("dp", "tensor"), None)
    placed = (
        rows_spec,
        P("dp"),
        rows_spec,
        P("dp", "tensor"),
        P("dp", "tensor"),
        P("dp", "tensor"),
        P("tensor", "dp"),
        P("dp", "tensor"),
        P("tensor", "dp"),
    ) + (P(),) * 9
    return jax.shard_map(
        layer,
        mesh=mesh,
        in_specs=placed,
        out_specs=(
            rows_spec,
            rows_spec,
            P("dp", "tensor"),
            P("dp", "tensor"),
            P("dp", "tensor"),
            P("tensor", "dp"),
            P("dp", "tensor"),
            P("tensor", "dp"),
        )
        + (P(),) * 9,
        check_vma=False,
    )
```

```python
import jax
import jax.numpy as jnp
from jax import lax
from jax.sharding import PartitionSpec as P

from jax.experimental import pallas as pl
from jax.experimental.pallas import tpu as pltpu


HEAD = 64
SEQ_LEN = 1024

norm_eps = 1e-12
masked_score = -1e30


def layer_norm(values, norm_gain, norm_shift):
    center = values - jnp.mean(values, axis=-1, keepdims=True)
    spread = jnp.mean(center * center, axis=-1, keepdims=True)
    return center * lax.rsqrt(spread + norm_eps) * norm_gain + norm_shift


def gelu_exact(values):
    return jax.nn.gelu(values, approximate=False)


def dot_right(first_op, second_op):
    return jnp.dot(first_op, second_op, preferred_element_type=jnp.float32)


def dot_back(first_op, second_op):
    return lax.dot_general(
        first_op, second_op, (((1,), (1,)), ((), ())), preferred_element_type=jnp.float32
    )


def dot_over_rows(first_op, second_op):
    return lax.dot_general(
        first_op, second_op, (((0,), (0,)), ((), ())), preferred_element_type=jnp.float32
    )


def gather_joined(shards, dp, tp):
    r = shards[0].shape[0]
    joined = jnp.concatenate(shards, axis=1)
    pieces = [joined] + [
        lax.ppermute(joined, "tensor", [(i, (i + step) % tp) for i in range(tp)]) for step in range(1, tp)
    ]
    t_index = lax.axis_index("tensor")
    order = (t_index - jnp.arange(tp, dtype=jnp.int32)) % tp
    by_tensor = jnp.take(jnp.stack(pieces), order, axis=0)
    full = lax.all_gather(by_tensor, "dp", axis=0, tiled=False)
    out = []
    start = 0
    for piece in shards:
        c = piece.shape[1]
        block = full[:, :, :, start : start + c]
        out.append(block.transpose(0, 2, 1, 3).reshape(dp * r, tp * c))
        start += c
    return out


LINK = jnp.bfloat16


def scatter_rows(grad, axis=0):
    return lax.psum_scatter(grad.astype(LINK), "dp", scatter_dimension=axis, tiled=True)


def sum_over_tensor(pieces, tp):
    parts = []
    for piece in pieces:
        r, c = piece.shape
        parts.append(piece.reshape(r, tp, c // tp).transpose(1, 0, 2))
    joined = jnp.concatenate(parts, axis=2)
    t_index = lax.axis_index("tensor")
    mine = lax.dynamic_index_in_dim(joined, t_index, keepdims=False).astype(jnp.float32)
    for step in range(1, tp):
        sent = lax.dynamic_index_in_dim(joined, (t_index + step) % tp, keepdims=False)
        mine = mine + lax.ppermute(sent, "tensor", [(i, (i + step) % tp) for i in range(tp)]).astype(jnp.float32)
    out = []
    start = 0
    for piece in pieces:
        c = piece.shape[1] // tp
        out.append(mine[:, start : start + c])
        start += c
    return out


NT = (((1,), (1,)), ((), ()))
LANES = 128


def attn_fwd_kernel(meta_ref, q_ref, k_ref, v_ref, ko_ref, vo_ref, o_ref, of_ref, lse_ref):
    half = meta_ref[0]
    prefix_len = meta_ref[1]
    rows = q_ref.shape[1]
    scale = HEAD ** (-0.5)
    q = q_ref[0]
    s = lax.dot_general(q, k_ref[0], NT, preferred_element_type=jnp.float32) * scale
    row = lax.broadcasted_iota(jnp.int32, s.shape, 0)
    col = lax.broadcasted_iota(jnp.int32, s.shape, 1)
    visible = (col <= row) | (half * rows + col < prefix_len)
    s = jnp.where(visible, s, masked_score)
    so = lax.dot_general(q, ko_ref[0], NT, preferred_element_type=jnp.float32) * scale
    so = jnp.where(half == 1, so, masked_score)
    top = jnp.maximum(jnp.max(s, axis=1, keepdims=True), jnp.max(so, axis=1, keepdims=True))
    e = jnp.exp(s - top)
    eo = jnp.exp(so - top)
    total = jnp.sum(e, axis=1, keepdims=True) + jnp.sum(eo, axis=1, keepdims=True)
    inv = 1.0 / total
    p = (e * inv).astype(jnp.bfloat16)
    po = (eo * inv).astype(jnp.bfloat16)
    o = jnp.dot(p, v_ref[0], preferred_element_type=jnp.float32) + jnp.dot(
        po, vo_ref[0], preferred_element_type=jnp.float32
    )
    o_ref[0] = o.astype(o_ref.dtype)
    of_ref[0] = o
    lse_ref[0] = jnp.broadcast_to(top + jnp.log(total), (rows, LANES))


def attn_bwd_kernel(
    meta_ref, q_ref, k_ref, v_ref, do_ref, lse_ref, dl_ref, ko_ref, vo_ref, qr_ref, dor_ref, lser_ref, dlr_ref,
    dq_ref, dk_ref, dv_ref,
):
    f32 = jnp.float32
    bf16 = jnp.bfloat16
    half = meta_ref[0]
    prefix_len = meta_ref[1]
    rows = q_ref.shape[1]
    reps = rows // LANES
    scale = HEAD ** (-0.5)
    q = q_ref[0]
    k = k_ref[0]
    v = v_ref[0]
    do = do_ref[0]
    s = lax.dot_general(q, k, NT, preferred_element_type=f32) * scale
    row = lax.broadcasted_iota(jnp.int32, s.shape, 0)
    col = lax.broadcasted_iota(jnp.int32, s.shape, 1)
    visible = (col <= row) | (half * rows + col < prefix_len)
    s = jnp.where(visible, s, masked_score)
    p = jnp.exp(s - jnp.tile(lse_ref[0], (1, reps)))
    dp = lax.dot_general(do, v, NT, preferred_element_type=f32)
    ds = (p * (dp - jnp.tile(dl_ref[0], (1, reps)))).astype(bf16)
    dq = jnp.dot(ds, k, preferred_element_type=f32)
    dk = jnp.dot(ds.T, q, preferred_element_type=f32)
    dv = jnp.dot(p.astype(bf16).T, do, preferred_element_type=f32)
    second = half == 1
    xq = jnp.where(second, q, qr_ref[0])
    xdo = jnp.where(second, do, dor_ref[0])
    xlse = jnp.tile(jnp.where(second, lse_ref[0], lser_ref[0]), (1, reps))
    xdl = jnp.tile(jnp.where(second, dl_ref[0], dlr_ref[0]), (1, reps))
    xk = jnp.where(second, ko_ref[0], k)
    xv = jnp.where(second, vo_ref[0], v)
    s2 = lax.dot_general(xq, xk, NT, preferred_element_type=f32) * scale
    p2 = jnp.exp(s2 - xlse)
    dp2 = lax.dot_general(xdo, xv, NT, preferred_element_type=f32)
    ds2 = (p2 * (dp2 - xdl)).astype(bf16)
    dq_x = jnp.dot(ds2, xk, preferred_element_type=f32)
    dk_x = jnp.dot(ds2.T, xq, preferred_element_type=f32)
    dv_x = jnp.dot(p2.astype(bf16).T, xdo, preferred_element_type=f32)
    dq = dq + jnp.where(second, dq_x, 0.0)
    dk = dk + jnp.where(second, 0.0, dk_x)
    dv = dv + jnp.where(second, 0.0, dv_x)
    dq_ref[0] = (dq * scale).astype(dq_ref.dtype)
    dk_ref[0] = (dk * scale).astype(dk_ref.dtype)
    dv_ref[0] = dv.astype(dv_ref.dtype)


def head_spec(shape):
    return pl.BlockSpec((1,) + tuple(shape[1:]), lambda h, meta: (h, 0, 0))


def attention_forward(meta, q, k, v, ko, vo):
    heads, rows, size = q.shape
    spec = head_spec(q.shape)
    lse_spec = head_spec((heads, rows, LANES))
    return pl.pallas_call(
        attn_fwd_kernel,
        out_shape=(
            jax.ShapeDtypeStruct(q.shape, jnp.bfloat16),
            jax.ShapeDtypeStruct(q.shape, jnp.float32),
            jax.ShapeDtypeStruct((heads, rows, LANES), jnp.float32),
        ),
        grid_spec=pltpu.PrefetchScalarGridSpec(
            num_scalar_prefetch=1,
            grid=(heads,),
            in_specs=[spec] * 5,
            out_specs=(spec, spec, lse_spec),
        ),
        cost_estimate=pl.CostEstimate(
            flops=8 * heads * rows * rows * size,
            transcendentals=2 * heads * rows * rows,
            bytes_accessed=5 * q.size * 2 + q.size * 6 + heads * rows * LANES * 4,
        ),
    )(meta, q, k, v, ko, vo)


def attention_backward(meta, q, k, v, do, lse, dl, ko, vo, qr, dor, lser, dlr):
    heads, rows, size = q.shape
    spec = head_spec(q.shape)
    lse_spec = head_spec(lse.shape)
    return pl.pallas_call(
        attn_bwd_kernel,
        out_shape=tuple(jax.ShapeDtypeStruct(q.shape, jnp.bfloat16) for _ in range(3)),
        grid_spec=pltpu.PrefetchScalarGridSpec(
            num_scalar_prefetch=1,
            grid=(heads,),
            in_specs=[spec, spec, spec, spec, lse_spec, lse_spec, spec, spec, spec, spec, lse_spec, lse_spec],
            out_specs=(spec, spec, spec),
        ),
        cost_estimate=pl.CostEstimate(
            flops=20 * heads * rows * rows * size,
            transcendentals=2 * heads * rows * rows,
            bytes_accessed=11 * q.size * 2 + 4 * lse.size * 4,
        ),
    )(meta, q, k, v, do, lse, dl, ko, vo, qr, dor, lser, dlr)


def layer(
    inputs,
    prefix,
    cotangent,
    w_query,
    w_key,
    w_value,
    w_out,
    w_up,
    w_down,
    b_query,
    b_value,
    b_out,
    b_up,
    b_down,
    gain_one,
    shift_one,
    gain_two,
    shift_two,
):
    f32 = jnp.float32
    bf16 = jnp.bfloat16
    dp = lax.axis_size("dp")
    tp = lax.axis_size("tensor")
    t_index = lax.axis_index("tensor")
    rows = inputs.shape[0]
    pieces = SEQ_LEN // rows
    assert pieces == 2
    half = t_index % pieces
    seq_here = (t_index * rows) // SEQ_LEN
    prefix_len = lax.dynamic_index_in_dim(prefix, seq_here, keepdims=False)
    to_second = [(t, t + 1) for t in range(0, tp, 2)]
    to_first = [(t + 1, t) for t in range(0, tp, 2)]

    full_query, full_key, full_value, out_t = gather_joined([w_query, w_key, w_value, w_out.T], dp, tp)
    full_out = out_t.T
    full_up, down_t = gather_joined([w_up, w_down.T], dp, tp)
    full_down = down_t.T
    width = full_query.shape[1]
    heads = width // HEAD

    gain_first = gain_one.astype(f32)
    shift_first = shift_one.astype(f32)
    gain_second = gain_two.astype(f32)
    shift_second = shift_two.astype(f32)

    in_rows = inputs.astype(f32)
    normed_one = layer_norm(in_rows, gain_first, shift_first).astype(bf16)
    key_rows = dot_right(normed_one, full_key).astype(bf16)
    value_rows = (dot_right(normed_one, full_value) + b_value.astype(f32)).astype(bf16)
    queries = (dot_right(normed_one, full_query) + b_query.astype(f32)).astype(bf16)

    def by_heads(x):
        return x.reshape(rows, heads, HEAD).transpose(1, 0, 2)

    meta = jnp.stack([half, prefix_len]).astype(jnp.int32)
    q3 = by_heads(queries)
    k3 = by_heads(key_rows)
    v3 = by_heads(value_rows)
    k_oth, v_oth = lax.ppermute((k3, v3), "tensor", to_second)
    o_heads, o_full, lse_wide = attention_forward(meta, q3, k3, v3, k_oth, v_oth)
    attended = o_heads.transpose(1, 0, 2).reshape(rows, width)
    q_rcv, lse_rcv = lax.ppermute((q3, lse_wide[:, :, 0]), "tensor", to_first)

    middle = in_rows + dot_right(attended, full_out) + b_out.astype(f32)
    normed_two = layer_norm(middle, gain_second, shift_second).astype(bf16)
    pre_act = dot_right(normed_two, full_up) + b_up.astype(f32)
    activated = gelu_exact(pre_act).astype(bf16)
    result = (middle + dot_right(activated, full_down) + b_down.astype(f32)).astype(bf16)

    grad_result = cotangent.astype(f32)
    grad_act = dot_back(cotangent, full_down)
    grad_pre = jax.vjp(gelu_exact, pre_act)[1](grad_act)[0].astype(bf16)
    ffn_grad = lax.dot_general(
        jnp.stack([normed_two, cotangent]),
        jnp.stack([grad_pre, activated]),
        (((1,), (1,)), ((0,), (0,))),
        preferred_element_type=f32,
    )
    grad_norm_two = dot_back(grad_pre, full_up)
    ffn_grad, grad_norm_two = lax.optimization_barrier((ffn_grad, grad_norm_two))
    ffn_rows = scatter_rows(ffn_grad, axis=1)
    up_rows = ffn_rows[0]
    down_rows = ffn_rows[1]
    norm_two_back = jax.vjp(layer_norm, middle, gain_second, shift_second)[1](grad_norm_two)
    grad_middle = grad_result + norm_two_back[0]
    grad_attn_rows = grad_middle.astype(bf16)
    grad_attended = dot_back(grad_attn_rows, full_out).astype(bf16)

    do3 = by_heads(grad_attended)
    delta = jnp.sum(do3.astype(f32) * o_full, axis=-1)
    do_rcv, delta_rcv = lax.ppermute((do3, delta), "tensor", to_first)

    def wide(x):
        return jnp.broadcast_to(x[:, :, None], x.shape + (LANES,))

    dq3, dk3, dv3 = attention_backward(
        meta, q3, k3, v3, do3, lse_wide, wide(delta), k_oth, v_oth, q_rcv, do_rcv, wide(lse_rcv), wide(delta_rcv)
    )

    def by_rows(x):
        return x.transpose(1, 0, 2).reshape(rows, width)

    grad_q = by_rows(dq3)
    grad_k = by_rows(dk3)
    grad_v = by_rows(dv3)
    grad_qkv = jnp.concatenate([grad_q, grad_k, grad_v], axis=1)
    attn_grad = jnp.concatenate(
        [dot_over_rows(normed_one, grad_qkv), dot_over_rows(grad_attn_rows, attended)], axis=1
    )
    attn_rows = scatter_rows(attn_grad)
    qkv_rows = attn_rows[:, : 3 * width]
    out_rows = attn_rows[:, 3 * width :]
    grad_norm_one = dot_back(grad_q, full_query) + dot_back(grad_k, full_key) + dot_back(grad_v, full_value)
    norm_one_back = jax.vjp(layer_norm, in_rows, gain_first, shift_first)[1](grad_norm_one)
    grad_input = grad_middle + norm_one_back[0]

    shard_up, shard_down_t = sum_over_tensor([up_rows, down_rows], tp)
    shard_query, shard_key, shard_value, shard_out_t = sum_over_tensor(
        [qkv_rows[:, :width], qkv_rows[:, width : 2 * width], qkv_rows[:, 2 * width :], out_rows], tp
    )
    shard_out = shard_out_t.T
    shard_down = shard_down_t.T
    vectors = [
        jnp.sum(grad_q, axis=0, dtype=f32),
        jnp.sum(grad_v, axis=0, dtype=f32),
        jnp.sum(grad_middle, axis=0),
        jnp.sum(grad_pre, axis=0, dtype=f32),
        jnp.sum(grad_result, axis=0),
        norm_one_back[1],
        norm_one_back[2],
        norm_two_back[1],
        norm_two_back[2],
    ]
    joined = lax.psum(jnp.concatenate(vectors), "dp")
    total = joined
    for step in range(1, tp):
        total = total + lax.ppermute(joined, "tensor", [(i, (i + step) % tp) for i in range(tp)])
    vector_sums = []
    start = 0
    for v in vectors:
        vector_sums.append(total[start : start + v.shape[0]])
        start += v.shape[0]
    return (
        result,
        grad_input,
        shard_query,
        shard_key,
        shard_value,
        shard_out,
        shard_up,
        shard_down,
    ) + tuple(vector_sums)


def solution(mesh):
    rows_spec = P(("dp", "tensor"), None)
    placed = (
        rows_spec,
        P("dp"),
        rows_spec,
        P("dp", "tensor"),
        P("dp", "tensor"),
        P("dp", "tensor"),
        P("tensor", "dp"),
        P("dp", "tensor"),
        P("tensor", "dp"),
    ) + (P(),) * 9
    return jax.shard_map(
        layer,
        mesh=mesh,
        in_specs=placed,
        out_specs=(
            rows_spec,
            rows_spec,
            P("dp", "tensor"),
            P("dp", "tensor"),
            P("dp", "tensor"),
            P("tensor", "dp"),
            P("dp", "tensor"),
            P("tensor", "dp"),
        )
        + (P(),) * 9,
        check_vma=False,
    )
```

```python
import jax
import jax.numpy as jnp
from jax import lax
from jax.sharding import PartitionSpec as P

from jax.experimental import pallas as pl
from jax.experimental.pallas import tpu as pltpu


HEAD = 64
SEQ_LEN = 1024

norm_eps = 1e-12
masked_score = -1e30


def layer_norm(values, norm_gain, norm_shift):
    center = values - jnp.mean(values, axis=-1, keepdims=True)
    spread = jnp.mean(center * center, axis=-1, keepdims=True)
    return center * lax.rsqrt(spread + norm_eps) * norm_gain + norm_shift


def gelu_exact(values):
    return jax.nn.gelu(values, approximate=False)


def dot_right(first_op, second_op):
    return jnp.dot(first_op, second_op, preferred_element_type=jnp.float32)


def dot_back(first_op, second_op):
    return lax.dot_general(
        first_op, second_op, (((1,), (1,)), ((), ())), preferred_element_type=jnp.float32
    )


def dot_over_rows(first_op, second_op):
    return lax.dot_general(
        first_op, second_op, (((0,), (0,)), ((), ())), preferred_element_type=jnp.float32
    )


def gather_joined(shards, dp, tp):
    r = shards[0].shape[0]
    joined = jnp.concatenate(shards, axis=1)
    pieces = [joined] + [
        lax.ppermute(joined, "tensor", [(i, (i + step) % tp) for i in range(tp)]) for step in range(1, tp)
    ]
    t_index = lax.axis_index("tensor")
    order = (t_index - jnp.arange(tp, dtype=jnp.int32)) % tp
    by_tensor = jnp.take(jnp.stack(pieces), order, axis=0)
    full = lax.all_gather(by_tensor, "dp", axis=0, tiled=False)
    out = []
    start = 0
    for piece in shards:
        c = piece.shape[1]
        block = full[:, :, :, start : start + c]
        out.append(block.transpose(0, 2, 1, 3).reshape(dp * r, tp * c))
        start += c
    return out


LINK = jnp.bfloat16


def scatter_rows(grad, axis=0):
    return lax.psum_scatter(grad.astype(LINK), "dp", scatter_dimension=axis, tiled=True)


def sum_over_tensor(pieces, tp):
    parts = []
    for piece in pieces:
        r, c = piece.shape
        parts.append(piece.reshape(r, tp, c // tp).transpose(1, 0, 2))
    joined = jnp.concatenate(parts, axis=2)
    t_index = lax.axis_index("tensor")
    mine = lax.dynamic_index_in_dim(joined, t_index, keepdims=False).astype(jnp.float32)
    for step in range(1, tp):
        sent = lax.dynamic_index_in_dim(joined, (t_index + step) % tp, keepdims=False)
        mine = mine + lax.ppermute(sent, "tensor", [(i, (i + step) % tp) for i in range(tp)]).astype(jnp.float32)
    out = []
    start = 0
    for piece in pieces:
        c = piece.shape[1] // tp
        out.append(mine[:, start : start + c])
        start += c
    return out


NT = (((1,), (1,)), ((), ()))
LANES = 128


def attn_fwd_kernel(meta_ref, q_ref, k_ref, v_ref, ko_ref, vo_ref, o_ref, of_ref, lse_ref):
    half = meta_ref[0]
    prefix_len = meta_ref[1]
    rows = q_ref.shape[0]
    scale = HEAD ** (-0.5)
    q_all = q_ref[...]
    k_all = k_ref[...]
    v_all = v_ref[...]
    ko_all = ko_ref[...]
    vo_all = vo_ref[...]
    outs = []
    for j in range(q_all.shape[1] // HEAD):
        cols = slice(j * HEAD, (j + 1) * HEAD)
        q = q_all[:, cols]
        s = lax.dot_general(q, k_all[:, cols], NT, preferred_element_type=jnp.float32) * scale
        row = lax.broadcasted_iota(jnp.int32, s.shape, 0)
        col = lax.broadcasted_iota(jnp.int32, s.shape, 1)
        visible = (col <= row) | (half * rows + col < prefix_len)
        s = jnp.where(visible, s, masked_score)
        so = lax.dot_general(q, ko_all[:, cols], NT, preferred_element_type=jnp.float32) * scale
        so = jnp.where(half == 1, so, masked_score)
        top = jnp.maximum(jnp.max(s, axis=1, keepdims=True), jnp.max(so, axis=1, keepdims=True))
        e = jnp.exp(s - top)
        eo = jnp.exp(so - top)
        total = jnp.sum(e, axis=1, keepdims=True) + jnp.sum(eo, axis=1, keepdims=True)
        inv = 1.0 / total
        p = (e * inv).astype(jnp.bfloat16)
        po = (eo * inv).astype(jnp.bfloat16)
        o = jnp.dot(p, v_all[:, cols], preferred_element_type=jnp.float32) + jnp.dot(
            po, vo_all[:, cols], preferred_element_type=jnp.float32
        )
        outs.append(o)
        lse_ref[j] = jnp.broadcast_to(top + jnp.log(total), (rows, LANES))
    o = jnp.concatenate(outs, axis=1)
    o_ref[...] = o.astype(o_ref.dtype)
    of_ref[...] = o


def attn_bwd_kernel(
    meta_ref, q_ref, k_ref, v_ref, do_ref, lse_ref, dl_ref, ko_ref, vo_ref, qr_ref, dor_ref, lser_ref, dlr_ref,
    dq_ref, dk_ref, dv_ref,
):
    f32 = jnp.float32
    bf16 = jnp.bfloat16
    half = meta_ref[0]
    prefix_len = meta_ref[1]
    rows = q_ref.shape[0]
    reps = rows // LANES
    scale = HEAD ** (-0.5)
    second = half == 1
    q_all = q_ref[...]
    k_all = k_ref[...]
    v_all = v_ref[...]
    do_all = do_ref[...]
    xq_all = jnp.where(second, q_all, qr_ref[...])
    xdo_all = jnp.where(second, do_all, dor_ref[...])
    xk_all = jnp.where(second, ko_ref[...], k_all)
    xv_all = jnp.where(second, vo_ref[...], v_all)
    dqs, dks, dvs = [], [], []
    for j in range(q_all.shape[1] // HEAD):
        cols = slice(j * HEAD, (j + 1) * HEAD)
        q = q_all[:, cols]
        k = k_all[:, cols]
        v = v_all[:, cols]
        do = do_all[:, cols]
        lse = lse_ref[j]
        dl = dl_ref[j]
        s = lax.dot_general(q, k, NT, preferred_element_type=f32) * scale
        row = lax.broadcasted_iota(jnp.int32, s.shape, 0)
        col = lax.broadcasted_iota(jnp.int32, s.shape, 1)
        visible = (col <= row) | (half * rows + col < prefix_len)
        s = jnp.where(visible, s, masked_score)
        p = jnp.exp(s - jnp.tile(lse, (1, reps)))
        dp = lax.dot_general(do, v, NT, preferred_element_type=f32)
        ds = (p * (dp - jnp.tile(dl, (1, reps)))).astype(bf16)
        dq = jnp.dot(ds, k, preferred_element_type=f32)
        dk = jnp.dot(ds.T, q, preferred_element_type=f32)
        dv = jnp.dot(p.astype(bf16).T, do, preferred_element_type=f32)
        xq = xq_all[:, cols]
        xdo = xdo_all[:, cols]
        xk = xk_all[:, cols]
        xv = xv_all[:, cols]
        xlse = jnp.tile(jnp.where(second, lse, lser_ref[j]), (1, reps))
        xdl = jnp.tile(jnp.where(second, dl, dlr_ref[j]), (1, reps))
        s2 = lax.dot_general(xq, xk, NT, preferred_element_type=f32) * scale
        p2 = jnp.exp(s2 - xlse)
        dp2 = lax.dot_general(xdo, xv, NT, preferred_element_type=f32)
        ds2 = (p2 * (dp2 - xdl)).astype(bf16)
        dq_x = jnp.dot(ds2, xk, preferred_element_type=f32)
        dk_x = jnp.dot(ds2.T, xq, preferred_element_type=f32)
        dv_x = jnp.dot(p2.astype(bf16).T, xdo, preferred_element_type=f32)
        dqs.append((dq + jnp.where(second, dq_x, 0.0)) * scale)
        dks.append((dk + jnp.where(second, 0.0, dk_x)) * scale)
        dvs.append(dv + jnp.where(second, 0.0, dv_x))
    dq_ref[...] = jnp.concatenate(dqs, axis=1).astype(dq_ref.dtype)
    dk_ref[...] = jnp.concatenate(dks, axis=1).astype(dk_ref.dtype)
    dv_ref[...] = jnp.concatenate(dvs, axis=1).astype(dv_ref.dtype)


PAIR = 2 * HEAD


def row_spec(rows):
    return pl.BlockSpec((rows, PAIR), lambda g, meta: (0, g))


def wide_spec(rows):
    return pl.BlockSpec((2, rows, LANES), lambda g, meta: (g, 0, 0))


def attention_forward(meta, q, k, v, ko, vo):
    rows, width = q.shape
    heads = width // HEAD
    spec = row_spec(rows)
    return pl.pallas_call(
        attn_fwd_kernel,
        out_shape=(
            jax.ShapeDtypeStruct(q.shape, jnp.bfloat16),
            jax.ShapeDtypeStruct(q.shape, jnp.float32),
            jax.ShapeDtypeStruct((heads, rows, LANES), jnp.float32),
        ),
        grid_spec=pltpu.PrefetchScalarGridSpec(
            num_scalar_prefetch=1,
            grid=(width // PAIR,),
            in_specs=[spec] * 5,
            out_specs=(spec, spec, wide_spec(rows)),
        ),
        cost_estimate=pl.CostEstimate(
            flops=8 * heads * rows * rows * HEAD,
            transcendentals=2 * heads * rows * rows,
            bytes_accessed=5 * q.size * 2 + q.size * 6 + heads * rows * LANES * 4,
        ),
    )(meta, q, k, v, ko, vo)


def attention_backward(meta, q, k, v, do, lse, dl, ko, vo, qr, dor, lser, dlr):
    rows, width = q.shape
    heads = width // HEAD
    spec = row_spec(rows)
    wspec = wide_spec(rows)
    return pl.pallas_call(
        attn_bwd_kernel,
        out_shape=tuple(jax.ShapeDtypeStruct(q.shape, jnp.bfloat16) for _ in range(3)),
        grid_spec=pltpu.PrefetchScalarGridSpec(
            num_scalar_prefetch=1,
            grid=(width // PAIR,),
            in_specs=[spec, spec, spec, spec, wspec, wspec, spec, spec, spec, spec, wspec, wspec],
            out_specs=(spec, spec, spec),
        ),
        cost_estimate=pl.CostEstimate(
            flops=20 * heads * rows * rows * HEAD,
            transcendentals=2 * heads * rows * rows,
            bytes_accessed=11 * q.size * 2 + 4 * lse.size * 4,
        ),
    )(meta, q, k, v, do, lse, dl, ko, vo, qr, dor, lser, dlr)


def layer(
    inputs,
    prefix,
    cotangent,
    w_query,
    w_key,
    w_value,
    w_out,
    w_up,
    w_down,
    b_query,
    b_value,
    b_out,
    b_up,
    b_down,
    gain_one,
    shift_one,
    gain_two,
    shift_two,
):
    f32 = jnp.float32
    bf16 = jnp.bfloat16
    dp = lax.axis_size("dp")
    tp = lax.axis_size("tensor")
    t_index = lax.axis_index("tensor")
    rows = inputs.shape[0]
    pieces = SEQ_LEN // rows
    assert pieces == 2
    half = t_index % pieces
    seq_here = (t_index * rows) // SEQ_LEN
    prefix_len = lax.dynamic_index_in_dim(prefix, seq_here, keepdims=False)
    to_second = [(t, t + 1) for t in range(0, tp, 2)]
    to_first = [(t + 1, t) for t in range(0, tp, 2)]

    full_query, full_key, full_value, out_t = gather_joined([w_query, w_key, w_value, w_out.T], dp, tp)
    full_out = out_t.T
    full_up, down_t = gather_joined([w_up, w_down.T], dp, tp)
    full_down = down_t.T
    width = full_query.shape[1]
    heads = width // HEAD

    gain_first = gain_one.astype(f32)
    shift_first = shift_one.astype(f32)
    gain_second = gain_two.astype(f32)
    shift_second = shift_two.astype(f32)

    in_rows = inputs.astype(f32)
    normed_one = layer_norm(in_rows, gain_first, shift_first).astype(bf16)
    key_rows = dot_right(normed_one, full_key).astype(bf16)
    value_rows = (dot_right(normed_one, full_value) + b_value.astype(f32)).astype(bf16)
    queries = (dot_right(normed_one, full_query) + b_query.astype(f32)).astype(bf16)
    meta = jnp.stack([half, prefix_len]).astype(jnp.int32)
    k_oth, v_oth = lax.ppermute((key_rows, value_rows), "tensor", to_second)
    attended, o_full, lse_wide = attention_forward(meta, queries, key_rows, value_rows, k_oth, v_oth)
    q_rcv, lse_rcv = lax.ppermute((queries, lse_wide[:, :, 0]), "tensor", to_first)

    middle = in_rows + dot_right(attended, full_out) + b_out.astype(f32)
    normed_two = layer_norm(middle, gain_second, shift_second).astype(bf16)
    pre_act = dot_right(normed_two, full_up) + b_up.astype(f32)
    activated = gelu_exact(pre_act).astype(bf16)
    result = (middle + dot_right(activated, full_down) + b_down.astype(f32)).astype(bf16)

    grad_result = cotangent.astype(f32)
    grad_act = dot_back(cotangent, full_down)
    grad_pre = jax.vjp(gelu_exact, pre_act)[1](grad_act)[0].astype(bf16)
    ffn_grad = lax.dot_general(
        jnp.stack([normed_two, cotangent]),
        jnp.stack([grad_pre, activated]),
        (((1,), (1,)), ((0,), (0,))),
        preferred_element_type=f32,
    )
    grad_norm_two = dot_back(grad_pre, full_up)
    ffn_grad, grad_norm_two = lax.optimization_barrier((ffn_grad, grad_norm_two))
    ffn_rows = scatter_rows(ffn_grad, axis=1)
    up_rows = ffn_rows[0]
    down_rows = ffn_rows[1]
    norm_two_back = jax.vjp(layer_norm, middle, gain_second, shift_second)[1](grad_norm_two)
    grad_middle = grad_result + norm_two_back[0]
    grad_attn_rows = grad_middle.astype(bf16)
    grad_attended = dot_back(grad_attn_rows, full_out).astype(bf16)

    delta = jnp.sum((grad_attended.astype(f32) * o_full).reshape(rows, heads, HEAD), axis=-1).T
    do_rcv, delta_rcv = lax.ppermute((grad_attended, delta), "tensor", to_first)

    def wide(x):
        return jnp.broadcast_to(x[:, :, None], x.shape + (LANES,))

    grad_q, grad_k, grad_v = attention_backward(
        meta, queries, key_rows, value_rows, grad_attended, lse_wide, wide(delta), k_oth, v_oth,
        q_rcv, do_rcv, wide(lse_rcv), wide(delta_rcv),
    )
    grad_qkv = jnp.concatenate([grad_q, grad_k, grad_v], axis=1)
    attn_grad = jnp.concatenate(
        [dot_over_rows(normed_one, grad_qkv), dot_over_rows(grad_attn_rows, attended)], axis=1
    )
    attn_rows = scatter_rows(attn_grad)
    qkv_rows = attn_rows[:, : 3 * width]
    out_rows = attn_rows[:, 3 * width :]
    grad_norm_one = dot_back(grad_q, full_query) + dot_back(grad_k, full_key) + dot_back(grad_v, full_value)
    norm_one_back = jax.vjp(layer_norm, in_rows, gain_first, shift_first)[1](grad_norm_one)
    grad_input = grad_middle + norm_one_back[0]

    shard_up, shard_down_t = sum_over_tensor([up_rows, down_rows], tp)
    shard_query, shard_key, shard_value, shard_out_t = sum_over_tensor(
        [qkv_rows[:, :width], qkv_rows[:, width : 2 * width], qkv_rows[:, 2 * width :], out_rows], tp
    )
    shard_out = shard_out_t.T
    shard_down = shard_down_t.T
    vectors = [
        jnp.sum(grad_q, axis=0, dtype=f32),
        jnp.sum(grad_v, axis=0, dtype=f32),
        jnp.sum(grad_middle, axis=0),
        jnp.sum(grad_pre, axis=0, dtype=f32),
        jnp.sum(grad_result, axis=0),
        norm_one_back[1],
        norm_one_back[2],
        norm_two_back[1],
        norm_two_back[2],
    ]
    joined = lax.psum(jnp.concatenate(vectors), "dp")
    total = joined
    for step in range(1, tp):
        total = total + lax.ppermute(joined, "tensor", [(i, (i + step) % tp) for i in range(tp)])
    vector_sums = []
    start = 0
    for v in vectors:
        vector_sums.append(total[start : start + v.shape[0]])
        start += v.shape[0]
    return (
        result,
        grad_input,
        shard_query,
        shard_key,
        shard_value,
        shard_out,
        shard_up,
        shard_down,
    ) + tuple(vector_sums)


def solution(mesh):
    rows_spec = P(("dp", "tensor"), None)
    placed = (
        rows_spec,
        P("dp"),
        rows_spec,
        P("dp", "tensor"),
        P("dp", "tensor"),
        P("dp", "tensor"),
        P("tensor", "dp"),
        P("dp", "tensor"),
        P("tensor", "dp"),
    ) + (P(),) * 9
    return jax.shard_map(
        layer,
        mesh=mesh,
        in_specs=placed,
        out_specs=(
            rows_spec,
            rows_spec,
            P("dp", "tensor"),
            P("dp", "tensor"),
            P("dp", "tensor"),
            P("tensor", "dp"),
            P("dp", "tensor"),
            P("tensor", "dp"),
        )
        + (P(),) * 9,
        check_vma=False,
    )
```

```python
import jax
import jax.numpy as jnp
from jax import lax
from jax.sharding import PartitionSpec as P

from jax.experimental import pallas as pl
from jax.experimental.pallas import tpu as pltpu


HEAD = 64
SEQ_LEN = 1024

norm_eps = 1e-12
masked_score = -1e30


def layer_norm(values, norm_gain, norm_shift):
    center = values - jnp.mean(values, axis=-1, keepdims=True)
    spread = jnp.mean(center * center, axis=-1, keepdims=True)
    return center * lax.rsqrt(spread + norm_eps) * norm_gain + norm_shift


def gelu_exact(values):
    return jax.nn.gelu(values, approximate=False)


def dot_right(first_op, second_op):
    return jnp.dot(first_op, second_op, preferred_element_type=jnp.float32)


def dot_back(first_op, second_op):
    return lax.dot_general(
        first_op, second_op, (((1,), (1,)), ((), ())), preferred_element_type=jnp.float32
    )


def dot_over_rows(first_op, second_op):
    return lax.dot_general(
        first_op, second_op, (((0,), (0,)), ((), ())), preferred_element_type=jnp.float32
    )


def gather_joined(shards, dp, tp):
    r = shards[0].shape[0]
    joined = jnp.concatenate(shards, axis=1)
    pieces = [joined] + [
        lax.ppermute(joined, "tensor", [(i, (i + step) % tp) for i in range(tp)]) for step in range(1, tp)
    ]
    t_index = lax.axis_index("tensor")
    order = (t_index - jnp.arange(tp, dtype=jnp.int32)) % tp
    by_tensor = jnp.take(jnp.stack(pieces), order, axis=0)
    full = lax.all_gather(by_tensor, "dp", axis=0, tiled=False)
    out = []
    start = 0
    for piece in shards:
        c = piece.shape[1]
        block = full[:, :, :, start : start + c]
        out.append(block.transpose(1, 3, 0, 2).reshape(tp * c, dp * r))
        start += c
    return out


LINK = jnp.bfloat16


def scatter_rows(grad, axis=0):
    return lax.psum_scatter(grad.astype(LINK), "dp", scatter_dimension=axis, tiled=True)


def sum_over_tensor(pieces, tp):
    parts = []
    for piece in pieces:
        r, c = piece.shape
        parts.append(piece.reshape(r, tp, c // tp).transpose(1, 0, 2))
    joined = jnp.concatenate(parts, axis=2)
    t_index = lax.axis_index("tensor")
    mine = lax.dynamic_index_in_dim(joined, t_index, keepdims=False).astype(jnp.float32)
    for step in range(1, tp):
        sent = lax.dynamic_index_in_dim(joined, (t_index + step) % tp, keepdims=False)
        mine = mine + lax.ppermute(sent, "tensor", [(i, (i + step) % tp) for i in range(tp)]).astype(jnp.float32)
    out = []
    start = 0
    for piece in pieces:
        c = piece.shape[1] // tp
        out.append(mine[:, start : start + c])
        start += c
    return out


NT = (((1,), (1,)), ((), ()))
LANES = 128


def attn_fwd_kernel(meta_ref, q_ref, k_ref, v_ref, ko_ref, vo_ref, o_ref, of_ref, lse_ref):
    half = meta_ref[0]
    prefix_len = meta_ref[1]
    rows = q_ref.shape[0]
    scale = HEAD ** (-0.5)
    q_all = q_ref[...]
    k_all = k_ref[...]
    v_all = v_ref[...]
    ko_all = ko_ref[...]
    vo_all = vo_ref[...]
    outs = []
    for j in range(q_all.shape[1] // HEAD):
        cols = slice(j * HEAD, (j + 1) * HEAD)
        q = q_all[:, cols]
        s = lax.dot_general(q, k_all[:, cols], NT, preferred_element_type=jnp.float32) * scale
        row = lax.broadcasted_iota(jnp.int32, s.shape, 0)
        col = lax.broadcasted_iota(jnp.int32, s.shape, 1)
        visible = (col <= row) | (half * rows + col < prefix_len)
        s = jnp.where(visible, s, masked_score)
        so = lax.dot_general(q, ko_all[:, cols], NT, preferred_element_type=jnp.float32) * scale
        so = jnp.where(half == 1, so, masked_score)
        top = jnp.maximum(jnp.max(s, axis=1, keepdims=True), jnp.max(so, axis=1, keepdims=True))
        e = jnp.exp(s - top)
        eo = jnp.exp(so - top)
        total = jnp.sum(e, axis=1, keepdims=True) + jnp.sum(eo, axis=1, keepdims=True)
        inv = 1.0 / total
        p = (e * inv).astype(jnp.bfloat16)
        po = (eo * inv).astype(jnp.bfloat16)
        o = jnp.dot(p, v_all[:, cols], preferred_element_type=jnp.float32) + jnp.dot(
            po, vo_all[:, cols], preferred_element_type=jnp.float32
        )
        outs.append(o)
        lse_ref[j] = jnp.broadcast_to(top + jnp.log(total), (rows, LANES))
    o = jnp.concatenate(outs, axis=1)
    o_ref[...] = o.astype(o_ref.dtype)
    of_ref[...] = o


def attn_bwd_kernel(
    meta_ref, q_ref, k_ref, v_ref, do_ref, lse_ref, dl_ref, ko_ref, vo_ref, qr_ref, dor_ref, lser_ref, dlr_ref,
    dq_ref, dk_ref, dv_ref,
):
    f32 = jnp.float32
    bf16 = jnp.bfloat16
    half = meta_ref[0]
    prefix_len = meta_ref[1]
    rows = q_ref.shape[0]
    reps = rows // LANES
    scale = HEAD ** (-0.5)
    second = half == 1
    q_all = q_ref[...]
    k_all = k_ref[...]
    v_all = v_ref[...]
    do_all = do_ref[...]
    xq_all = jnp.where(second, q_all, qr_ref[...])
    xdo_all = jnp.where(second, do_all, dor_ref[...])
    xk_all = jnp.where(second, ko_ref[...], k_all)
    xv_all = jnp.where(second, vo_ref[...], v_all)
    dqs, dks, dvs = [], [], []
    for j in range(q_all.shape[1] // HEAD):
        cols = slice(j * HEAD, (j + 1) * HEAD)
        q = q_all[:, cols]
        k = k_all[:, cols]
        v = v_all[:, cols]
        do = do_all[:, cols]
        lse = lse_ref[j]
        dl = dl_ref[j]
        s = lax.dot_general(q, k, NT, preferred_element_type=f32) * scale
        row = lax.broadcasted_iota(jnp.int32, s.shape, 0)
        col = lax.broadcasted_iota(jnp.int32, s.shape, 1)
        visible = (col <= row) | (half * rows + col < prefix_len)
        s = jnp.where(visible, s, masked_score)
        p = jnp.exp(s - jnp.tile(lse, (1, reps)))
        dp = lax.dot_general(do, v, NT, preferred_element_type=f32)
        ds = (p * (dp - jnp.tile(dl, (1, reps)))).astype(bf16)
        dq = jnp.dot(ds, k, preferred_element_type=f32)
        dk = jnp.dot(ds.T, q, preferred_element_type=f32)
        dv = jnp.dot(p.astype(bf16).T, do, preferred_element_type=f32)
        xq = xq_all[:, cols]
        xdo = xdo_all[:, cols]
        xk = xk_all[:, cols]
        xv = xv_all[:, cols]
        xlse = jnp.tile(jnp.where(second, lse, lser_ref[j]), (1, reps))
        xdl = jnp.tile(jnp.where(second, dl, dlr_ref[j]), (1, reps))
        s2 = lax.dot_general(xq, xk, NT, preferred_element_type=f32) * scale
        p2 = jnp.exp(s2 - xlse)
        dp2 = lax.dot_general(xdo, xv, NT, preferred_element_type=f32)
        ds2 = (p2 * (dp2 - xdl)).astype(bf16)
        dq_x = jnp.dot(ds2, xk, preferred_element_type=f32)
        dk_x = jnp.dot(ds2.T, xq, preferred_element_type=f32)
        dv_x = jnp.dot(p2.astype(bf16).T, xdo, preferred_element_type=f32)
        dqs.append((dq + jnp.where(second, dq_x, 0.0)) * scale)
        dks.append((dk + jnp.where(second, 0.0, dk_x)) * scale)
        dvs.append(dv + jnp.where(second, 0.0, dv_x))
    dq_ref[...] = jnp.concatenate(dqs, axis=1).astype(dq_ref.dtype)
    dk_ref[...] = jnp.concatenate(dks, axis=1).astype(dk_ref.dtype)
    dv_ref[...] = jnp.concatenate(dvs, axis=1).astype(dv_ref.dtype)


PAIR = 2 * HEAD


def row_spec(rows):
    return pl.BlockSpec((rows, PAIR), lambda g, meta: (0, g))


def wide_spec(rows):
    return pl.BlockSpec((2, rows, LANES), lambda g, meta: (g, 0, 0))


def attention_forward(meta, q, k, v, ko, vo):
    rows, width = q.shape
    heads = width // HEAD
    spec = row_spec(rows)
    return pl.pallas_call(
        attn_fwd_kernel,
        out_shape=(
            jax.ShapeDtypeStruct(q.shape, jnp.bfloat16),
            jax.ShapeDtypeStruct(q.shape, jnp.float32),
            jax.ShapeDtypeStruct((heads, rows, LANES), jnp.float32),
        ),
        grid_spec=pltpu.PrefetchScalarGridSpec(
            num_scalar_prefetch=1,
            grid=(width // PAIR,),
            in_specs=[spec] * 5,
            out_specs=(spec, spec, wide_spec(rows)),
        ),
        cost_estimate=pl.CostEstimate(
            flops=8 * heads * rows * rows * HEAD,
            transcendentals=2 * heads * rows * rows,
            bytes_accessed=5 * q.size * 2 + q.size * 6 + heads * rows * LANES * 4,
        ),
    )(meta, q, k, v, ko, vo)


def attention_backward(meta, q, k, v, do, lse, dl, ko, vo, qr, dor, lser, dlr):
    rows, width = q.shape
    heads = width // HEAD
    spec = row_spec(rows)
    wspec = wide_spec(rows)
    return pl.pallas_call(
        attn_bwd_kernel,
        out_shape=tuple(jax.ShapeDtypeStruct(q.shape, jnp.bfloat16) for _ in range(3)),
        grid_spec=pltpu.PrefetchScalarGridSpec(
            num_scalar_prefetch=1,
            grid=(width // PAIR,),
            in_specs=[spec, spec, spec, spec, wspec, wspec, spec, spec, spec, spec, wspec, wspec],
            out_specs=(spec, spec, spec),
        ),
        cost_estimate=pl.CostEstimate(
            flops=20 * heads * rows * rows * HEAD,
            transcendentals=2 * heads * rows * rows,
            bytes_accessed=11 * q.size * 2 + 4 * lse.size * 4,
        ),
    )(meta, q, k, v, do, lse, dl, ko, vo, qr, dor, lser, dlr)


def layer(
    inputs,
    prefix,
    cotangent,
    w_query,
    w_key,
    w_value,
    w_out,
    w_up,
    w_down,
    b_query,
    b_value,
    b_out,
    b_up,
    b_down,
    gain_one,
    shift_one,
    gain_two,
    shift_two,
):
    f32 = jnp.float32
    bf16 = jnp.bfloat16
    dp = lax.axis_size("dp")
    tp = lax.axis_size("tensor")
    t_index = lax.axis_index("tensor")
    rows = inputs.shape[0]
    pieces = SEQ_LEN // rows
    assert pieces == 2
    half = t_index % pieces
    seq_here = (t_index * rows) // SEQ_LEN
    prefix_len = lax.dynamic_index_in_dim(prefix, seq_here, keepdims=False)
    to_second = [(t, t + 1) for t in range(0, tp, 2)]
    to_first = [(t + 1, t) for t in range(0, tp, 2)]

    query_t, key_t, value_t, full_out = gather_joined([w_query, w_key, w_value, w_out.T], dp, tp)
    up_t, full_down = gather_joined([w_up, w_down.T], dp, tp)
    width = query_t.shape[0]
    heads = width // HEAD

    gain_first = gain_one.astype(f32)
    shift_first = shift_one.astype(f32)
    gain_second = gain_two.astype(f32)
    shift_second = shift_two.astype(f32)

    in_rows = inputs.astype(f32)
    normed_one = layer_norm(in_rows, gain_first, shift_first).astype(bf16)
    key_rows = dot_back(normed_one, key_t).astype(bf16)
    value_rows = (dot_back(normed_one, value_t) + b_value.astype(f32)).astype(bf16)
    queries = (dot_back(normed_one, query_t) + b_query.astype(f32)).astype(bf16)
    meta = jnp.stack([half, prefix_len]).astype(jnp.int32)
    k_oth, v_oth = lax.ppermute((key_rows, value_rows), "tensor", to_second)
    attended, o_full, lse_wide = attention_forward(meta, queries, key_rows, value_rows, k_oth, v_oth)
    q_rcv, lse_rcv = lax.ppermute((queries, lse_wide[:, :, 0]), "tensor", to_first)

    middle = in_rows + dot_right(attended, full_out) + b_out.astype(f32)
    normed_two = layer_norm(middle, gain_second, shift_second).astype(bf16)
    pre_act = dot_back(normed_two, up_t) + b_up.astype(f32)
    activated = gelu_exact(pre_act).astype(bf16)
    result = (middle + dot_right(activated, full_down) + b_down.astype(f32)).astype(bf16)

    grad_result = cotangent.astype(f32)
    grad_act = dot_back(cotangent, full_down)
    grad_pre = jax.vjp(gelu_exact, pre_act)[1](grad_act)[0].astype(bf16)
    ffn_grad = lax.dot_general(
        jnp.stack([normed_two, cotangent]),
        jnp.stack([grad_pre, activated]),
        (((1,), (1,)), ((0,), (0,))),
        preferred_element_type=f32,
    )
    grad_norm_two = dot_right(grad_pre, up_t)
    ffn_grad, grad_norm_two = lax.optimization_barrier((ffn_grad, grad_norm_two))
    ffn_rows = scatter_rows(ffn_grad, axis=1)
    up_rows = ffn_rows[0]
    down_rows = ffn_rows[1]
    norm_two_back = jax.vjp(layer_norm, middle, gain_second, shift_second)[1](grad_norm_two)
    grad_middle = grad_result + norm_two_back[0]
    grad_attn_rows = grad_middle.astype(bf16)
    grad_attended = dot_back(grad_attn_rows, full_out).astype(bf16)

    delta = jnp.sum((grad_attended.astype(f32) * o_full).reshape(rows, heads, HEAD), axis=-1).T
    do_rcv, delta_rcv = lax.ppermute((grad_attended, delta), "tensor", to_first)

    def wide(x):
        return jnp.broadcast_to(x[:, :, None], x.shape + (LANES,))

    grad_q, grad_k, grad_v = attention_backward(
        meta, queries, key_rows, value_rows, grad_attended, lse_wide, wide(delta), k_oth, v_oth,
        q_rcv, do_rcv, wide(lse_rcv), wide(delta_rcv),
    )
    grad_qkv = jnp.concatenate([grad_q, grad_k, grad_v], axis=1)
    attn_grad = jnp.concatenate(
        [dot_over_rows(normed_one, grad_qkv), dot_over_rows(grad_attn_rows, attended)], axis=1
    )
    attn_rows = scatter_rows(attn_grad)
    qkv_rows = attn_rows[:, : 3 * width]
    out_rows = attn_rows[:, 3 * width :]
    grad_norm_one = dot_right(grad_q, query_t) + dot_right(grad_k, key_t) + dot_right(grad_v, value_t)
    norm_one_back = jax.vjp(layer_norm, in_rows, gain_first, shift_first)[1](grad_norm_one)
    grad_input = grad_middle + norm_one_back[0]

    shard_up, shard_down_t = sum_over_tensor([up_rows, down_rows], tp)
    shard_query, shard_key, shard_value, shard_out_t = sum_over_tensor(
        [qkv_rows[:, :width], qkv_rows[:, width : 2 * width], qkv_rows[:, 2 * width :], out_rows], tp
    )
    shard_out = shard_out_t.T
    shard_down = shard_down_t.T
    vectors = [
        jnp.sum(grad_q, axis=0, dtype=f32),
        jnp.sum(grad_v, axis=0, dtype=f32),
        jnp.sum(grad_middle, axis=0),
        jnp.sum(grad_pre, axis=0, dtype=f32),
        jnp.sum(grad_result, axis=0),
        norm_one_back[1],
        norm_one_back[2],
        norm_two_back[1],
        norm_two_back[2],
    ]
    joined = lax.psum(jnp.concatenate(vectors), "dp")
    total = joined
    for step in range(1, tp):
        total = total + lax.ppermute(joined, "tensor", [(i, (i + step) % tp) for i in range(tp)])
    vector_sums = []
    start = 0
    for v in vectors:
        vector_sums.append(total[start : start + v.shape[0]])
        start += v.shape[0]
    return (
        result,
        grad_input,
        shard_query,
        shard_key,
        shard_value,
        shard_out,
        shard_up,
        shard_down,
    ) + tuple(vector_sums)


def solution(mesh):
    rows_spec = P(("dp", "tensor"), None)
    placed = (
        rows_spec,
        P("dp"),
        rows_spec,
        P("dp", "tensor"),
        P("dp", "tensor"),
        P("dp", "tensor"),
        P("tensor", "dp"),
        P("dp", "tensor"),
        P("tensor", "dp"),
    ) + (P(),) * 9
    return jax.shard_map(
        layer,
        mesh=mesh,
        in_specs=placed,
        out_specs=(
            rows_spec,
            rows_spec,
            P("dp", "tensor"),
            P("dp", "tensor"),
            P("dp", "tensor"),
            P("tensor", "dp"),
            P("dp", "tensor"),
            P("tensor", "dp"),
        )
        + (P(),) * 9,
        check_vma=False,
    )
```

```python
import jax
import jax.numpy as jnp
from jax import lax
from jax.sharding import PartitionSpec as P

from jax.experimental import pallas as pl
from jax.experimental.pallas import tpu as pltpu


HEAD = 64
SEQ_LEN = 1024

norm_eps = 1e-12
masked_score = -1e30


def layer_norm(values, norm_gain, norm_shift):
    center = values - jnp.mean(values, axis=-1, keepdims=True)
    spread = jnp.mean(center * center, axis=-1, keepdims=True)
    return center * lax.rsqrt(spread + norm_eps) * norm_gain + norm_shift


def gelu_exact(values):
    return jax.nn.gelu(values, approximate=False)


def dot_right(first_op, second_op):
    return jnp.dot(first_op, second_op, preferred_element_type=jnp.float32)


def dot_back(first_op, second_op):
    return lax.dot_general(
        first_op, second_op, (((1,), (1,)), ((), ())), preferred_element_type=jnp.float32
    )


def dot_over_rows(first_op, second_op):
    return lax.dot_general(
        first_op, second_op, (((0,), (0,)), ((), ())), preferred_element_type=jnp.float32
    )


def gather_joined(shards, tp):
    r = shards[0].shape[0]
    joined = jnp.concatenate(shards, axis=1)
    pieces = [joined] + [
        lax.ppermute(joined, "tensor", [(i, (i + step) % tp) for i in range(tp)]) for step in range(1, tp)
    ]
    t_index = lax.axis_index("tensor")
    order = (t_index - jnp.arange(tp, dtype=jnp.int32)) % tp
    by_tensor = jnp.take(jnp.stack(pieces), order, axis=0)
    strips = []
    start = 0
    for piece in shards:
        c = piece.shape[1]
        strips.append(by_tensor[:, :, start : start + c].transpose(1, 0, 2).reshape(r, tp * c))
        start += c
    full = lax.all_gather(jnp.concatenate(strips, axis=1), "dp", axis=0, tiled=True)
    out = []
    start = 0
    for piece in shards:
        c = tp * piece.shape[1]
        out.append(full[:, start : start + c])
        start += c
    return out


LINK = jnp.bfloat16


def scatter_rows(grad, axis=0):
    return lax.psum_scatter(grad.astype(LINK), "dp", scatter_dimension=axis, tiled=True)


def sum_over_tensor(pieces, tp):
    parts = []
    for piece in pieces:
        r, c = piece.shape
        parts.append(piece.reshape(r, tp, c // tp).transpose(1, 0, 2))
    joined = jnp.concatenate(parts, axis=2)
    t_index = lax.axis_index("tensor")
    mine = lax.dynamic_index_in_dim(joined, t_index, keepdims=False).astype(jnp.float32)
    for step in range(1, tp):
        sent = lax.dynamic_index_in_dim(joined, (t_index + step) % tp, keepdims=False)
        mine = mine + lax.ppermute(sent, "tensor", [(i, (i + step) % tp) for i in range(tp)]).astype(jnp.float32)
    out = []
    start = 0
    for piece in pieces:
        c = piece.shape[1] // tp
        out.append(mine[:, start : start + c])
        start += c
    return out


NT = (((1,), (1,)), ((), ()))
LANES = 128


def attn_fwd_kernel(meta_ref, q_ref, k_ref, v_ref, ko_ref, vo_ref, o_ref, of_ref, lse_ref):
    half = meta_ref[0]
    prefix_len = meta_ref[1]
    rows = q_ref.shape[0]
    scale = HEAD ** (-0.5)
    q_all = q_ref[...]
    k_all = k_ref[...]
    v_all = v_ref[...]
    ko_all = ko_ref[...]
    vo_all = vo_ref[...]
    outs = []
    for j in range(q_all.shape[1] // HEAD):
        cols = slice(j * HEAD, (j + 1) * HEAD)
        q = q_all[:, cols]
        s = lax.dot_general(q, k_all[:, cols], NT, preferred_element_type=jnp.float32) * scale
        row = lax.broadcasted_iota(jnp.int32, s.shape, 0)
        col = lax.broadcasted_iota(jnp.int32, s.shape, 1)
        visible = (col <= row) | (half * rows + col < prefix_len)
        s = jnp.where(visible, s, masked_score)
        so = lax.dot_general(q, ko_all[:, cols], NT, preferred_element_type=jnp.float32) * scale
        so = jnp.where(half == 1, so, masked_score)
        top = jnp.maximum(jnp.max(s, axis=1, keepdims=True), jnp.max(so, axis=1, keepdims=True))
        e = jnp.exp(s - top)
        eo = jnp.exp(so - top)
        total = jnp.sum(e, axis=1, keepdims=True) + jnp.sum(eo, axis=1, keepdims=True)
        inv = 1.0 / total
        p = (e * inv).astype(jnp.bfloat16)
        po = (eo * inv).astype(jnp.bfloat16)
        o = jnp.dot(p, v_all[:, cols], preferred_element_type=jnp.float32) + jnp.dot(
            po, vo_all[:, cols], preferred_element_type=jnp.float32
        )
        outs.append(o)
        lse_ref[j] = jnp.broadcast_to(top + jnp.log(total), (rows, LANES))
    o = jnp.concatenate(outs, axis=1)
    o_ref[...] = o.astype(o_ref.dtype)
    of_ref[...] = o


def attn_bwd_kernel(
    meta_ref, q_ref, k_ref, v_ref, do_ref, lse_ref, dl_ref, ko_ref, vo_ref, qr_ref, dor_ref, lser_ref, dlr_ref,
    dq_ref, dk_ref, dv_ref,
):
    f32 = jnp.float32
    bf16 = jnp.bfloat16
    half = meta_ref[0]
    prefix_len = meta_ref[1]
    rows = q_ref.shape[0]
    reps = rows // LANES
    scale = HEAD ** (-0.5)
    second = half == 1
    q_all = q_ref[...]
    k_all = k_ref[...]
    v_all = v_ref[...]
    do_all = do_ref[...]
    xq_all = jnp.where(second, q_all, qr_ref[...])
    xdo_all = jnp.where(second, do_all, dor_ref[...])
    xk_all = jnp.where(second, ko_ref[...], k_all)
    xv_all = jnp.where(second, vo_ref[...], v_all)
    dqs, dks, dvs = [], [], []
    for j in range(q_all.shape[1] // HEAD):
        cols = slice(j * HEAD, (j + 1) * HEAD)
        q = q_all[:, cols]
        k = k_all[:, cols]
        v = v_all[:, cols]
        do = do_all[:, cols]
        lse = lse_ref[j]
        dl = dl_ref[j]
        s = lax.dot_general(q, k, NT, preferred_element_type=f32) * scale
        row = lax.broadcasted_iota(jnp.int32, s.shape, 0)
        col = lax.broadcasted_iota(jnp.int32, s.shape, 1)
        visible = (col <= row) | (half * rows + col < prefix_len)
        s = jnp.where(visible, s, masked_score)
        p = jnp.exp(s - jnp.tile(lse, (1, reps)))
        dp = lax.dot_general(do, v, NT, preferred_element_type=f32)
        ds = (p * (dp - jnp.tile(dl, (1, reps)))).astype(bf16)
        dq = jnp.dot(ds, k, preferred_element_type=f32)
        dk = jnp.dot(ds.T, q, preferred_element_type=f32)
        dv = jnp.dot(p.astype(bf16).T, do, preferred_element_type=f32)
        xq = xq_all[:, cols]
        xdo = xdo_all[:, cols]
        xk = xk_all[:, cols]
        xv = xv_all[:, cols]
        xlse = jnp.tile(jnp.where(second, lse, lser_ref[j]), (1, reps))
        xdl = jnp.tile(jnp.where(second, dl, dlr_ref[j]), (1, reps))
        s2 = lax.dot_general(xq, xk, NT, preferred_element_type=f32) * scale
        p2 = jnp.exp(s2 - xlse)
        dp2 = lax.dot_general(xdo, xv, NT, preferred_element_type=f32)
        ds2 = (p2 * (dp2 - xdl)).astype(bf16)
        dq_x = jnp.dot(ds2, xk, preferred_element_type=f32)
        dk_x = jnp.dot(ds2.T, xq, preferred_element_type=f32)
        dv_x = jnp.dot(p2.astype(bf16).T, xdo, preferred_element_type=f32)
        dqs.append((dq + jnp.where(second, dq_x, 0.0)) * scale)
        dks.append((dk + jnp.where(second, 0.0, dk_x)) * scale)
        dvs.append(dv + jnp.where(second, 0.0, dv_x))
    dq_ref[...] = jnp.concatenate(dqs, axis=1).astype(dq_ref.dtype)
    dk_ref[...] = jnp.concatenate(dks, axis=1).astype(dk_ref.dtype)
    dv_ref[...] = jnp.concatenate(dvs, axis=1).astype(dv_ref.dtype)


PAIR = 2 * HEAD


def row_spec(rows):
    return pl.BlockSpec((rows, PAIR), lambda g, meta: (0, g))


def wide_spec(rows):
    return pl.BlockSpec((2, rows, LANES), lambda g, meta: (g, 0, 0))


def attention_forward(meta, q, k, v, ko, vo):
    rows, width = q.shape
    heads = width // HEAD
    spec = row_spec(rows)
    return pl.pallas_call(
        attn_fwd_kernel,
        out_shape=(
            jax.ShapeDtypeStruct(q.shape, jnp.bfloat16),
            jax.ShapeDtypeStruct(q.shape, jnp.float32),
            jax.ShapeDtypeStruct((heads, rows, LANES), jnp.float32),
        ),
        grid_spec=pltpu.PrefetchScalarGridSpec(
            num_scalar_prefetch=1,
            grid=(width // PAIR,),
            in_specs=[spec] * 5,
            out_specs=(spec, spec, wide_spec(rows)),
        ),
        cost_estimate=pl.CostEstimate(
            flops=8 * heads * rows * rows * HEAD,
            transcendentals=2 * heads * rows * rows,
            bytes_accessed=5 * q.size * 2 + q.size * 6 + heads * rows * LANES * 4,
        ),
    )(meta, q, k, v, ko, vo)


def attention_backward(meta, q, k, v, do, lse, dl, ko, vo, qr, dor, lser, dlr):
    rows, width = q.shape
    heads = width // HEAD
    spec = row_spec(rows)
    wspec = wide_spec(rows)
    return pl.pallas_call(
        attn_bwd_kernel,
        out_shape=tuple(jax.ShapeDtypeStruct(q.shape, jnp.bfloat16) for _ in range(3)),
        grid_spec=pltpu.PrefetchScalarGridSpec(
            num_scalar_prefetch=1,
            grid=(width // PAIR,),
            in_specs=[spec, spec, spec, spec, wspec, wspec, spec, spec, spec, spec, wspec, wspec],
            out_specs=(spec, spec, spec),
        ),
        cost_estimate=pl.CostEstimate(
            flops=20 * heads * rows * rows * HEAD,
            transcendentals=2 * heads * rows * rows,
            bytes_accessed=11 * q.size * 2 + 4 * lse.size * 4,
        ),
    )(meta, q, k, v, do, lse, dl, ko, vo, qr, dor, lser, dlr)


def layer(
    inputs,
    prefix,
    cotangent,
    w_query,
    w_key,
    w_value,
    w_out,
    w_up,
    w_down,
    b_query,
    b_value,
    b_out,
    b_up,
    b_down,
    gain_one,
    shift_one,
    gain_two,
    shift_two,
):
    f32 = jnp.float32
    bf16 = jnp.bfloat16
    tp = lax.axis_size("tensor")
    t_index = lax.axis_index("tensor")
    rows = inputs.shape[0]
    pieces = SEQ_LEN // rows
    assert pieces == 2
    half = t_index % pieces
    seq_here = (t_index * rows) // SEQ_LEN
    prefix_len = lax.dynamic_index_in_dim(prefix, seq_here, keepdims=False)
    to_second = [(t, t + 1) for t in range(0, tp, 2)]
    to_first = [(t + 1, t) for t in range(0, tp, 2)]

    full_query, full_key, full_value, out_t = gather_joined([w_query, w_key, w_value, w_out.T], tp)
    full_up, down_t = gather_joined([w_up, w_down.T], tp)
    width = full_query.shape[1]
    heads = width // HEAD

    gain_first = gain_one.astype(f32)
    shift_first = shift_one.astype(f32)
    gain_second = gain_two.astype(f32)
    shift_second = shift_two.astype(f32)

    in_rows = inputs.astype(f32)
    normed_one = layer_norm(in_rows, gain_first, shift_first).astype(bf16)
    key_rows = dot_right(normed_one, full_key).astype(bf16)
    value_rows = (dot_right(normed_one, full_value) + b_value.astype(f32)).astype(bf16)
    queries = (dot_right(normed_one, full_query) + b_query.astype(f32)).astype(bf16)
    meta = jnp.stack([half, prefix_len]).astype(jnp.int32)
    k_oth, v_oth = lax.ppermute((key_rows, value_rows), "tensor", to_second)
    attended, o_full, lse_wide = attention_forward(meta, queries, key_rows, value_rows, k_oth, v_oth)
    q_rcv, lse_rcv = lax.ppermute((queries, lse_wide[:, :, 0]), "tensor", to_first)

    middle = in_rows + dot_back(attended, out_t) + b_out.astype(f32)
    normed_two = layer_norm(middle, gain_second, shift_second).astype(bf16)
    pre_act = dot_right(normed_two, full_up) + b_up.astype(f32)
    activated = gelu_exact(pre_act).astype(bf16)
    result = (middle + dot_back(activated, down_t) + b_down.astype(f32)).astype(bf16)

    grad_result = cotangent.astype(f32)
    grad_act = dot_right(cotangent, down_t)
    grad_pre = jax.vjp(gelu_exact, pre_act)[1](grad_act)[0].astype(bf16)
    ffn_grad = lax.dot_general(
        jnp.stack([normed_two, cotangent]),
        jnp.stack([grad_pre, activated]),
        (((1,), (1,)), ((0,), (0,))),
        preferred_element_type=f32,
    )
    grad_norm_two = dot_back(grad_pre, full_up)
    ffn_grad, grad_norm_two = lax.optimization_barrier((ffn_grad, grad_norm_two))
    ffn_rows = scatter_rows(ffn_grad, axis=1)
    up_rows = ffn_rows[0]
    down_rows = ffn_rows[1]
    norm_two_back = jax.vjp(layer_norm, middle, gain_second, shift_second)[1](grad_norm_two)
    grad_middle = grad_result + norm_two_back[0]
    grad_attn_rows = grad_middle.astype(bf16)
    grad_attended = dot_right(grad_attn_rows, out_t).astype(bf16)

    delta = jnp.sum((grad_attended.astype(f32) * o_full).reshape(rows, heads, HEAD), axis=-1).T
    do_rcv, delta_rcv = lax.ppermute((grad_attended, delta), "tensor", to_first)

    def wide(x):
        return jnp.broadcast_to(x[:, :, None], x.shape + (LANES,))

    grad_q, grad_k, grad_v = attention_backward(
        meta, queries, key_rows, value_rows, grad_attended, lse_wide, wide(delta), k_oth, v_oth,
        q_rcv, do_rcv, wide(lse_rcv), wide(delta_rcv),
    )
    grad_qkv = jnp.concatenate([grad_q, grad_k, grad_v], axis=1)
    attn_grad = jnp.concatenate(
        [dot_over_rows(normed_one, grad_qkv), dot_over_rows(grad_attn_rows, attended)], axis=1
    )
    attn_rows = scatter_rows(attn_grad)
    qkv_rows = attn_rows[:, : 3 * width]
    out_rows = attn_rows[:, 3 * width :]
    grad_norm_one = dot_back(grad_q, full_query) + dot_back(grad_k, full_key) + dot_back(grad_v, full_value)
    norm_one_back = jax.vjp(layer_norm, in_rows, gain_first, shift_first)[1](grad_norm_one)
    grad_input = grad_middle + norm_one_back[0]

    shard_up, shard_down_t = sum_over_tensor([up_rows, down_rows], tp)
    shard_query, shard_key, shard_value, shard_out_t = sum_over_tensor(
        [qkv_rows[:, :width], qkv_rows[:, width : 2 * width], qkv_rows[:, 2 * width :], out_rows], tp
    )
    shard_out = shard_out_t.T
    shard_down = shard_down_t.T
    vectors = [
        jnp.sum(grad_q, axis=0, dtype=f32),
        jnp.sum(grad_v, axis=0, dtype=f32),
        jnp.sum(grad_middle, axis=0),
        jnp.sum(grad_pre, axis=0, dtype=f32),
        jnp.sum(grad_result, axis=0),
        norm_one_back[1],
        norm_one_back[2],
        norm_two_back[1],
        norm_two_back[2],
    ]
    joined = lax.psum(jnp.concatenate(vectors), "dp")
    total = joined
    for step in range(1, tp):
        total = total + lax.ppermute(joined, "tensor", [(i, (i + step) % tp) for i in range(tp)])
    vector_sums = []
    start = 0
    for v in vectors:
        vector_sums.append(total[start : start + v.shape[0]])
        start += v.shape[0]
    return (
        result,
        grad_input,
        shard_query,
        shard_key,
        shard_value,
        shard_out,
        shard_up,
        shard_down,
    ) + tuple(vector_sums)


def solution(mesh):
    rows_spec = P(("dp", "tensor"), None)
    placed = (
        rows_spec,
        P("dp"),
        rows_spec,
        P("dp", "tensor"),
        P("dp", "tensor"),
        P("dp", "tensor"),
        P("tensor", "dp"),
        P("dp", "tensor"),
        P("tensor", "dp"),
    ) + (P(),) * 9
    return jax.shard_map(
        layer,
        mesh=mesh,
        in_specs=placed,
        out_specs=(
            rows_spec,
            rows_spec,
            P("dp", "tensor"),
            P("dp", "tensor"),
            P("dp", "tensor"),
            P("tensor", "dp"),
            P("dp", "tensor"),
            P("tensor", "dp"),
        )
        + (P(),) * 9,
        check_vma=False,
    )
```

```python
import jax
import jax.numpy as jnp
from jax import lax
from jax.sharding import PartitionSpec as P

from jax.experimental import pallas as pl
from jax.experimental.pallas import tpu as pltpu


HEAD = 64
SEQ_LEN = 1024

norm_eps = 1e-12
masked_score = -1e30


def layer_norm(values, norm_gain, norm_shift):
    center = values - jnp.mean(values, axis=-1, keepdims=True)
    spread = jnp.mean(center * center, axis=-1, keepdims=True)
    return center * lax.rsqrt(spread + norm_eps) * norm_gain + norm_shift


def gelu_exact(values):
    return jax.nn.gelu(values, approximate=False)


def dot_right(first_op, second_op):
    return jnp.dot(first_op, second_op, preferred_element_type=jnp.float32)


def dot_back(first_op, second_op):
    return lax.dot_general(
        first_op, second_op, (((1,), (1,)), ((), ())), preferred_element_type=jnp.float32
    )


def dot_over_rows(first_op, second_op):
    return lax.dot_general(
        first_op, second_op, (((0,), (0,)), ((), ())), preferred_element_type=jnp.float32
    )


def gather_joined(shards, tp):
    r = shards[0].shape[0]
    joined = jnp.concatenate(shards, axis=1)
    pieces = [joined] + [
        lax.ppermute(joined, "tensor", [(i, (i + step) % tp) for i in range(tp)]) for step in range(1, tp)
    ]
    t_index = lax.axis_index("tensor")
    order = (t_index - jnp.arange(tp, dtype=jnp.int32)) % tp
    by_tensor = jnp.take(jnp.stack(pieces), order, axis=0)
    strips = []
    start = 0
    for piece in shards:
        c = piece.shape[1]
        strips.append(by_tensor[:, :, start : start + c].transpose(1, 0, 2).reshape(r, tp * c))
        start += c
    full = lax.all_gather(jnp.concatenate(strips, axis=1), "dp", axis=0, tiled=True)
    out = []
    start = 0
    for piece in shards:
        c = tp * piece.shape[1]
        out.append(full[:, start : start + c])
        start += c
    return out


LINK = jnp.bfloat16


def scatter_rows(grad, axis=0):
    return lax.psum_scatter(grad.astype(LINK), "dp", scatter_dimension=axis, tiled=True)


def sum_over_tensor(pieces, tp):
    parts = []
    for piece in pieces:
        r, c = piece.shape
        parts.append(piece.reshape(r, tp, c // tp).transpose(1, 0, 2))
    joined = jnp.concatenate(parts, axis=2)
    t_index = lax.axis_index("tensor")
    mine = lax.dynamic_index_in_dim(joined, t_index, keepdims=False).astype(jnp.float32)
    for step in range(1, tp):
        sent = lax.dynamic_index_in_dim(joined, (t_index + step) % tp, keepdims=False)
        mine = mine + lax.ppermute(sent, "tensor", [(i, (i + step) % tp) for i in range(tp)]).astype(jnp.float32)
    out = []
    start = 0
    for piece in pieces:
        c = piece.shape[1] // tp
        out.append(mine[:, start : start + c])
        start += c
    return out


NT = (((1,), (1,)), ((), ()))
LANES = 128


def attn_fwd_kernel(meta_ref, q_ref, k_ref, v_ref, ko_ref, vo_ref, o_ref, of_ref, lse_ref):
    half = meta_ref[0]
    prefix_len = meta_ref[1]
    rows = q_ref.shape[0]
    scale = HEAD ** (-0.5)
    q_all = q_ref[...]
    k_all = k_ref[...]
    v_all = v_ref[...]
    ko_all = ko_ref[...]
    vo_all = vo_ref[...]
    outs = []
    for j in range(q_all.shape[1] // HEAD):
        cols = slice(j * HEAD, (j + 1) * HEAD)
        q = q_all[:, cols]
        s = lax.dot_general(q, k_all[:, cols], NT, preferred_element_type=jnp.float32) * scale
        row = lax.broadcasted_iota(jnp.int32, s.shape, 0)
        col = lax.broadcasted_iota(jnp.int32, s.shape, 1)
        visible = (col <= row) | (half * rows + col < prefix_len)
        s = jnp.where(visible, s, masked_score)
        so = lax.dot_general(q, ko_all[:, cols], NT, preferred_element_type=jnp.float32) * scale
        so = jnp.where(half == 1, so, masked_score)
        top = jnp.maximum(jnp.max(s, axis=1, keepdims=True), jnp.max(so, axis=1, keepdims=True))
        e = jnp.exp(s - top)
        eo = jnp.exp(so - top)
        total = jnp.sum(e, axis=1, keepdims=True) + jnp.sum(eo, axis=1, keepdims=True)
        inv = 1.0 / total
        p = (e * inv).astype(jnp.bfloat16)
        po = (eo * inv).astype(jnp.bfloat16)
        o = jnp.dot(p, v_all[:, cols], preferred_element_type=jnp.float32) + jnp.dot(
            po, vo_all[:, cols], preferred_element_type=jnp.float32
        )
        outs.append(o)
        lse_ref[j] = jnp.broadcast_to(top + jnp.log(total), (rows, LANES))
    o = jnp.concatenate(outs, axis=1)
    o_ref[...] = o.astype(o_ref.dtype)
    of_ref[...] = o


def attn_bwd_kernel(
    meta_ref, q_ref, k_ref, v_ref, do_ref, lse_ref, dl_ref, ko_ref, vo_ref, qr_ref, dor_ref, lser_ref, dlr_ref,
    dq_ref, dk_ref, dv_ref,
):
    f32 = jnp.float32
    bf16 = jnp.bfloat16
    half = meta_ref[0]
    prefix_len = meta_ref[1]
    rows = q_ref.shape[0]
    reps = rows // LANES
    scale = HEAD ** (-0.5)
    second = half == 1
    q_all = q_ref[...]
    k_all = k_ref[...]
    v_all = v_ref[...]
    do_all = do_ref[...]
    xq_all = jnp.where(second, q_all, qr_ref[...])
    xdo_all = jnp.where(second, do_all, dor_ref[...])
    xk_all = jnp.where(second, ko_ref[...], k_all)
    xv_all = jnp.where(second, vo_ref[...], v_all)
    dqs, dks, dvs = [], [], []
    for j in range(q_all.shape[1] // HEAD):
        cols = slice(j * HEAD, (j + 1) * HEAD)
        q = q_all[:, cols]
        k = k_all[:, cols]
        v = v_all[:, cols]
        do = do_all[:, cols]
        lse = lse_ref[j]
        dl = dl_ref[j]
        s = lax.dot_general(q, k, NT, preferred_element_type=f32) * scale
        row = lax.broadcasted_iota(jnp.int32, s.shape, 0)
        col = lax.broadcasted_iota(jnp.int32, s.shape, 1)
        visible = (col <= row) | (half * rows + col < prefix_len)
        s = jnp.where(visible, s, masked_score)
        p = jnp.exp(s - jnp.tile(lse, (1, reps)))
        dp = lax.dot_general(do, v, NT, preferred_element_type=f32)
        ds = (p * (dp - jnp.tile(dl, (1, reps)))).astype(bf16)
        dq = jnp.dot(ds, k, preferred_element_type=f32)
        dk = jnp.dot(ds.T, q, preferred_element_type=f32)
        dv = jnp.dot(p.astype(bf16).T, do, preferred_element_type=f32)
        xq = xq_all[:, cols]
        xdo = xdo_all[:, cols]
        xk = xk_all[:, cols]
        xv = xv_all[:, cols]
        xlse = jnp.tile(jnp.where(second, lse, lser_ref[j]), (1, reps))
        xdl = jnp.tile(jnp.where(second, dl, dlr_ref[j]), (1, reps))
        s2 = lax.dot_general(xq, xk, NT, preferred_element_type=f32) * scale
        p2 = jnp.exp(s2 - xlse)
        dp2 = lax.dot_general(xdo, xv, NT, preferred_element_type=f32)
        ds2 = (p2 * (dp2 - xdl)).astype(bf16)
        dq_x = jnp.dot(ds2, xk, preferred_element_type=f32)
        dk_x = jnp.dot(ds2.T, xq, preferred_element_type=f32)
        dv_x = jnp.dot(p2.astype(bf16).T, xdo, preferred_element_type=f32)
        dqs.append((dq + jnp.where(second, dq_x, 0.0)) * scale)
        dks.append((dk + jnp.where(second, 0.0, dk_x)) * scale)
        dvs.append(dv + jnp.where(second, 0.0, dv_x))
    dq_ref[...] = jnp.concatenate(dqs, axis=1).astype(dq_ref.dtype)
    dk_ref[...] = jnp.concatenate(dks, axis=1).astype(dk_ref.dtype)
    dv_ref[...] = jnp.concatenate(dvs, axis=1).astype(dv_ref.dtype)


PAIR = 2 * HEAD


def row_spec(rows):
    return pl.BlockSpec((rows, PAIR), lambda g, meta: (0, g))


def wide_spec(rows):
    return pl.BlockSpec((2, rows, LANES), lambda g, meta: (g, 0, 0))


def attention_forward(meta, q, k, v, ko, vo):
    rows, width = q.shape
    heads = width // HEAD
    spec = row_spec(rows)
    return pl.pallas_call(
        attn_fwd_kernel,
        out_shape=(
            jax.ShapeDtypeStruct(q.shape, jnp.bfloat16),
            jax.ShapeDtypeStruct(q.shape, jnp.float32),
            jax.ShapeDtypeStruct((heads, rows, LANES), jnp.float32),
        ),
        grid_spec=pltpu.PrefetchScalarGridSpec(
            num_scalar_prefetch=1,
            grid=(width // PAIR,),
            in_specs=[spec] * 5,
            out_specs=(spec, spec, wide_spec(rows)),
        ),
        cost_estimate=pl.CostEstimate(
            flops=8 * heads * rows * rows * HEAD,
            transcendentals=2 * heads * rows * rows,
            bytes_accessed=5 * q.size * 2 + q.size * 6 + heads * rows * LANES * 4,
        ),
    )(meta, q, k, v, ko, vo)


def attention_backward(meta, q, k, v, do, lse, dl, ko, vo, qr, dor, lser, dlr):
    rows, width = q.shape
    heads = width // HEAD
    spec = row_spec(rows)
    wspec = wide_spec(rows)
    return pl.pallas_call(
        attn_bwd_kernel,
        out_shape=tuple(jax.ShapeDtypeStruct(q.shape, jnp.bfloat16) for _ in range(3)),
        grid_spec=pltpu.PrefetchScalarGridSpec(
            num_scalar_prefetch=1,
            grid=(width // PAIR,),
            in_specs=[spec, spec, spec, spec, wspec, wspec, spec, spec, spec, spec, wspec, wspec],
            out_specs=(spec, spec, spec),
        ),
        cost_estimate=pl.CostEstimate(
            flops=20 * heads * rows * rows * HEAD,
            transcendentals=2 * heads * rows * rows,
            bytes_accessed=11 * q.size * 2 + 4 * lse.size * 4,
        ),
    )(meta, q, k, v, do, lse, dl, ko, vo, qr, dor, lser, dlr)


def layer(
    inputs,
    prefix,
    cotangent,
    w_query,
    w_key,
    w_value,
    w_out,
    w_up,
    w_down,
    b_query,
    b_value,
    b_out,
    b_up,
    b_down,
    gain_one,
    shift_one,
    gain_two,
    shift_two,
):
    f32 = jnp.float32
    bf16 = jnp.bfloat16
    tp = lax.axis_size("tensor")
    t_index = lax.axis_index("tensor")
    rows = inputs.shape[0]
    pieces = SEQ_LEN // rows
    assert pieces == 2
    half = t_index % pieces
    seq_here = (t_index * rows) // SEQ_LEN
    prefix_len = lax.dynamic_index_in_dim(prefix, seq_here, keepdims=False)
    to_first = [(t + 1, t) for t in range(0, tp, 2)]

    full_query, full_key, full_value, out_t = gather_joined([w_query, w_key, w_value, w_out.T], tp)
    full_up, down_t = gather_joined([w_up, w_down.T], tp)
    width = full_query.shape[1]
    heads = width // HEAD

    gain_first = gain_one.astype(f32)
    shift_first = shift_one.astype(f32)
    gain_second = gain_two.astype(f32)
    shift_second = shift_two.astype(f32)

    in_rows = inputs.astype(f32)
    normed_one = layer_norm(in_rows, gain_first, shift_first).astype(bf16)
    swap = [(t, t ^ 1) for t in range(tp)]
    normed_oth = lax.ppermute(normed_one, "tensor", swap)
    key_rows = dot_right(normed_one, full_key).astype(bf16)
    value_rows = (dot_right(normed_one, full_value) + b_value.astype(f32)).astype(bf16)
    queries = (dot_right(normed_one, full_query) + b_query.astype(f32)).astype(bf16)
    meta = jnp.stack([half, prefix_len]).astype(jnp.int32)
    k_oth = dot_right(normed_oth, full_key).astype(bf16)
    v_oth = (dot_right(normed_oth, full_value) + b_value.astype(f32)).astype(bf16)
    q_rcv = (dot_right(normed_oth, full_query) + b_query.astype(f32)).astype(bf16)
    attended, o_full, lse_wide = attention_forward(meta, queries, key_rows, value_rows, k_oth, v_oth)
    lse_rcv = lax.ppermute(lse_wide[:, :, 0], "tensor", to_first)

    middle = in_rows + dot_back(attended, out_t) + b_out.astype(f32)
    normed_two = layer_norm(middle, gain_second, shift_second).astype(bf16)
    pre_act = dot_right(normed_two, full_up) + b_up.astype(f32)
    activated = gelu_exact(pre_act).astype(bf16)
    result = (middle + dot_back(activated, down_t) + b_down.astype(f32)).astype(bf16)

    grad_result = cotangent.astype(f32)
    grad_act = dot_right(cotangent, down_t)
    grad_pre = jax.vjp(gelu_exact, pre_act)[1](grad_act)[0].astype(bf16)
    ffn_grad = lax.dot_general(
        jnp.stack([normed_two, cotangent]),
        jnp.stack([grad_pre, activated]),
        (((1,), (1,)), ((0,), (0,))),
        preferred_element_type=f32,
    )
    grad_norm_two = dot_back(grad_pre, full_up)
    ffn_rows = scatter_rows(ffn_grad, axis=1)
    up_rows = ffn_rows[0]
    down_rows = ffn_rows[1]
    norm_two_back = jax.vjp(layer_norm, middle, gain_second, shift_second)[1](grad_norm_two)
    grad_middle = grad_result + norm_two_back[0]
    grad_attn_rows = grad_middle.astype(bf16)
    grad_attended = dot_right(grad_attn_rows, out_t).astype(bf16)

    delta = jnp.sum((grad_attended.astype(f32) * o_full).reshape(rows, heads, HEAD), axis=-1).T
    do_rcv, delta_rcv = lax.ppermute((grad_attended, delta), "tensor", to_first)

    def wide(x):
        return jnp.broadcast_to(x[:, :, None], x.shape + (LANES,))

    grad_q, grad_k, grad_v = attention_backward(
        meta, queries, key_rows, value_rows, grad_attended, lse_wide, wide(delta), k_oth, v_oth,
        q_rcv, do_rcv, wide(lse_rcv), wide(delta_rcv),
    )
    grad_qkv = jnp.concatenate([grad_q, grad_k, grad_v], axis=1)
    attn_grad = jnp.concatenate(
        [dot_over_rows(normed_one, grad_qkv), dot_over_rows(grad_attn_rows, attended)], axis=1
    )
    attn_rows = scatter_rows(attn_grad)
    qkv_rows = attn_rows[:, : 3 * width]
    out_rows = attn_rows[:, 3 * width :]
    grad_norm_one = dot_back(grad_q, full_query) + dot_back(grad_k, full_key) + dot_back(grad_v, full_value)
    norm_one_back = jax.vjp(layer_norm, in_rows, gain_first, shift_first)[1](grad_norm_one)
    grad_input = grad_middle + norm_one_back[0]

    shard_up, shard_down_t = sum_over_tensor([up_rows, down_rows], tp)
    shard_query, shard_key, shard_value, shard_out_t = sum_over_tensor(
        [qkv_rows[:, :width], qkv_rows[:, width : 2 * width], qkv_rows[:, 2 * width :], out_rows], tp
    )
    shard_out = shard_out_t.T
    shard_down = shard_down_t.T
    vectors = [
        jnp.sum(grad_q, axis=0, dtype=f32),
        jnp.sum(grad_v, axis=0, dtype=f32),
        jnp.sum(grad_middle, axis=0),
        jnp.sum(grad_pre, axis=0, dtype=f32),
        jnp.sum(grad_result, axis=0),
        norm_one_back[1],
        norm_one_back[2],
        norm_two_back[1],
        norm_two_back[2],
    ]
    joined = lax.psum(jnp.concatenate(vectors), "dp")
    total = joined
    for step in range(1, tp):
        total = total + lax.ppermute(joined, "tensor", [(i, (i + step) % tp) for i in range(tp)])
    vector_sums = []
    start = 0
    for v in vectors:
        vector_sums.append(total[start : start + v.shape[0]])
        start += v.shape[0]
    return (
        result,
        grad_input,
        shard_query,
        shard_key,
        shard_value,
        shard_out,
        shard_up,
        shard_down,
    ) + tuple(vector_sums)


def solution(mesh):
    rows_spec = P(("dp", "tensor"), None)
    placed = (
        rows_spec,
        P("dp"),
        rows_spec,
        P("dp", "tensor"),
        P("dp", "tensor"),
        P("dp", "tensor"),
        P("tensor", "dp"),
        P("dp", "tensor"),
        P("tensor", "dp"),
    ) + (P(),) * 9
    return jax.shard_map(
        layer,
        mesh=mesh,
        in_specs=placed,
        out_specs=(
            rows_spec,
            rows_spec,
            P("dp", "tensor"),
            P("dp", "tensor"),
            P("dp", "tensor"),
            P("tensor", "dp"),
            P("dp", "tensor"),
            P("tensor", "dp"),
        )
        + (P(),) * 9,
        check_vma=False,
    )
```

```python
import jax
import jax.numpy as jnp
from jax import lax
from jax.sharding import PartitionSpec as P

from jax.experimental import pallas as pl
from jax.experimental.pallas import tpu as pltpu


HEAD = 64
SEQ_LEN = 1024

norm_eps = 1e-12
masked_score = -1e30


def layer_norm(values, norm_gain, norm_shift):
    center = values - jnp.mean(values, axis=-1, keepdims=True)
    spread = jnp.mean(center * center, axis=-1, keepdims=True)
    return center * lax.rsqrt(spread + norm_eps) * norm_gain + norm_shift


def gelu_exact(values):
    return jax.nn.gelu(values, approximate=False)


def dot_right(first_op, second_op):
    return jnp.dot(first_op, second_op, preferred_element_type=jnp.float32)


def dot_back(first_op, second_op):
    return lax.dot_general(
        first_op, second_op, (((1,), (1,)), ((), ())), preferred_element_type=jnp.float32
    )


def dot_over_rows(first_op, second_op):
    return lax.dot_general(
        first_op, second_op, (((0,), (0,)), ((), ())), preferred_element_type=jnp.float32
    )


def gather_joined(shards, tp):
    r = shards[0].shape[0]
    joined = jnp.concatenate(shards, axis=1)
    pieces = [joined] + [
        lax.ppermute(joined, "tensor", [(i, (i + step) % tp) for i in range(tp)]) for step in range(1, tp)
    ]
    t_index = lax.axis_index("tensor")
    order = (t_index - jnp.arange(tp, dtype=jnp.int32)) % tp
    by_tensor = jnp.take(jnp.stack(pieces), order, axis=0)
    strips = []
    start = 0
    for piece in shards:
        c = piece.shape[1]
        strips.append(by_tensor[:, :, start : start + c].transpose(1, 0, 2).reshape(r, tp * c))
        start += c
    full = lax.all_gather(jnp.concatenate(strips, axis=1), "dp", axis=0, tiled=True)
    out = []
    start = 0
    for piece in shards:
        c = tp * piece.shape[1]
        out.append(full[:, start : start + c])
        start += c
    return out


LINK = jnp.bfloat16


def scatter_rows(grad, axis=0):
    return lax.psum_scatter(grad.astype(LINK), "dp", scatter_dimension=axis, tiled=True)


def sum_over_tensor(pieces, tp):
    parts = []
    for piece in pieces:
        r, c = piece.shape
        parts.append(piece.reshape(r, tp, c // tp).transpose(1, 0, 2))
    joined = jnp.concatenate(parts, axis=2)
    t_index = lax.axis_index("tensor")
    mine = lax.dynamic_index_in_dim(joined, t_index, keepdims=False).astype(jnp.float32)
    for step in range(1, tp):
        sent = lax.dynamic_index_in_dim(joined, (t_index + step) % tp, keepdims=False)
        mine = mine + lax.ppermute(sent, "tensor", [(i, (i + step) % tp) for i in range(tp)]).astype(jnp.float32)
    out = []
    start = 0
    for piece in pieces:
        c = piece.shape[1] // tp
        out.append(mine[:, start : start + c])
        start += c
    return out


NT = (((1,), (1,)), ((), ()))
LANES = 128


def attn_fwd_kernel(meta_ref, q_ref, k_ref, v_ref, ko_ref, vo_ref, o_ref, of_ref, lse_ref):
    half = meta_ref[0]
    prefix_len = meta_ref[1]
    rows = q_ref.shape[0]
    scale = HEAD ** (-0.5)
    q_all = q_ref[...]
    k_all = k_ref[...]
    v_all = v_ref[...]
    ko_all = ko_ref[...]
    vo_all = vo_ref[...]
    outs = []
    for j in range(q_all.shape[1] // HEAD):
        cols = slice(j * HEAD, (j + 1) * HEAD)
        q = q_all[:, cols]
        s = lax.dot_general(q, k_all[:, cols], NT, preferred_element_type=jnp.float32) * scale
        row = lax.broadcasted_iota(jnp.int32, s.shape, 0)
        col = lax.broadcasted_iota(jnp.int32, s.shape, 1)
        visible = (col <= row) | (half * rows + col < prefix_len)
        s = jnp.where(visible, s, masked_score)
        so = lax.dot_general(q, ko_all[:, cols], NT, preferred_element_type=jnp.float32) * scale
        so = jnp.where(half == 1, so, masked_score)
        top = jnp.maximum(jnp.max(s, axis=1, keepdims=True), jnp.max(so, axis=1, keepdims=True))
        e = jnp.exp(s - top)
        eo = jnp.exp(so - top)
        total = jnp.sum(e, axis=1, keepdims=True) + jnp.sum(eo, axis=1, keepdims=True)
        inv = 1.0 / total
        p = (e * inv).astype(jnp.bfloat16)
        po = (eo * inv).astype(jnp.bfloat16)
        o = jnp.dot(p, v_all[:, cols], preferred_element_type=jnp.float32) + jnp.dot(
            po, vo_all[:, cols], preferred_element_type=jnp.float32
        )
        outs.append(o)
        lse_ref[j] = jnp.broadcast_to(top + jnp.log(total), (rows, LANES))
    o = jnp.concatenate(outs, axis=1)
    o_ref[...] = o.astype(o_ref.dtype)
    of_ref[...] = o


def attn_bwd_kernel(
    meta_ref, q_ref, k_ref, v_ref, do_ref, lse_ref, dl_ref, ko_ref, vo_ref, qr_ref, dor_ref, lser_ref, dlr_ref,
    dq_ref, dk_ref, dv_ref,
):
    f32 = jnp.float32
    bf16 = jnp.bfloat16
    half = meta_ref[0]
    prefix_len = meta_ref[1]
    rows = q_ref.shape[0]
    reps = rows // LANES
    scale = HEAD ** (-0.5)
    second = half == 1
    q_all = q_ref[...]
    k_all = k_ref[...]
    v_all = v_ref[...]
    do_all = do_ref[...]
    xq_all = jnp.where(second, q_all, qr_ref[...])
    xdo_all = jnp.where(second, do_all, dor_ref[...])
    xk_all = jnp.where(second, ko_ref[...], k_all)
    xv_all = jnp.where(second, vo_ref[...], v_all)
    dqs, dks, dvs = [], [], []
    for j in range(q_all.shape[1] // HEAD):
        cols = slice(j * HEAD, (j + 1) * HEAD)
        q = q_all[:, cols]
        k = k_all[:, cols]
        v = v_all[:, cols]
        do = do_all[:, cols]
        lse = lse_ref[j]
        dl = dl_ref[j]
        s = lax.dot_general(q, k, NT, preferred_element_type=f32) * scale
        row = lax.broadcasted_iota(jnp.int32, s.shape, 0)
        col = lax.broadcasted_iota(jnp.int32, s.shape, 1)
        visible = (col <= row) | (half * rows + col < prefix_len)
        s = jnp.where(visible, s, masked_score)
        p = jnp.exp(s - jnp.tile(lse, (1, reps)))
        dp = lax.dot_general(do, v, NT, preferred_element_type=f32)
        ds = (p * (dp - jnp.tile(dl, (1, reps)))).astype(bf16)
        dq = jnp.dot(ds, k, preferred_element_type=f32)
        dk = jnp.dot(ds.T, q, preferred_element_type=f32)
        dv = jnp.dot(p.astype(bf16).T, do, preferred_element_type=f32)
        xq = xq_all[:, cols]
        xdo = xdo_all[:, cols]
        xk = xk_all[:, cols]
        xv = xv_all[:, cols]
        xlse = jnp.tile(jnp.where(second, lse, lser_ref[j]), (1, reps))
        xdl = jnp.tile(jnp.where(second, dl, dlr_ref[j]), (1, reps))
        s2 = lax.dot_general(xq, xk, NT, preferred_element_type=f32) * scale
        p2 = jnp.exp(s2 - xlse)
        dp2 = lax.dot_general(xdo, xv, NT, preferred_element_type=f32)
        ds2 = (p2 * (dp2 - xdl)).astype(bf16)
        dq_x = jnp.dot(ds2, xk, preferred_element_type=f32)
        dk_x = jnp.dot(ds2.T, xq, preferred_element_type=f32)
        dv_x = jnp.dot(p2.astype(bf16).T, xdo, preferred_element_type=f32)
        dqs.append((dq + jnp.where(second, dq_x, 0.0)) * scale)
        dks.append((dk + jnp.where(second, 0.0, dk_x)) * scale)
        dvs.append(dv + jnp.where(second, 0.0, dv_x))
    dq_ref[...] = jnp.concatenate(dqs, axis=1).astype(dq_ref.dtype)
    dk_ref[...] = jnp.concatenate(dks, axis=1).astype(dk_ref.dtype)
    dv_ref[...] = jnp.concatenate(dvs, axis=1).astype(dv_ref.dtype)


PAIR = 2 * HEAD


def row_spec(rows):
    return pl.BlockSpec((rows, PAIR), lambda g, meta: (0, g))


def wide_spec(rows):
    return pl.BlockSpec((2, rows, LANES), lambda g, meta: (g, 0, 0))


def attention_forward(meta, q, k, v, ko, vo):
    rows, width = q.shape
    heads = width // HEAD
    spec = row_spec(rows)
    return pl.pallas_call(
        attn_fwd_kernel,
        out_shape=(
            jax.ShapeDtypeStruct(q.shape, jnp.bfloat16),
            jax.ShapeDtypeStruct(q.shape, jnp.float32),
            jax.ShapeDtypeStruct((heads, rows, LANES), jnp.float32),
        ),
        grid_spec=pltpu.PrefetchScalarGridSpec(
            num_scalar_prefetch=1,
            grid=(width // PAIR,),
            in_specs=[spec] * 5,
            out_specs=(spec, spec, wide_spec(rows)),
        ),
        cost_estimate=pl.CostEstimate(
            flops=8 * heads * rows * rows * HEAD,
            transcendentals=2 * heads * rows * rows,
            bytes_accessed=5 * q.size * 2 + q.size * 6 + heads * rows * LANES * 4,
        ),
    )(meta, q, k, v, ko, vo)


def attention_backward(meta, q, k, v, do, lse, dl, ko, vo, qr, dor, lser, dlr):
    rows, width = q.shape
    heads = width // HEAD
    spec = row_spec(rows)
    wspec = wide_spec(rows)
    return pl.pallas_call(
        attn_bwd_kernel,
        out_shape=tuple(jax.ShapeDtypeStruct(q.shape, jnp.bfloat16) for _ in range(3)),
        grid_spec=pltpu.PrefetchScalarGridSpec(
            num_scalar_prefetch=1,
            grid=(width // PAIR,),
            in_specs=[spec, spec, spec, spec, wspec, wspec, spec, spec, spec, spec, wspec, wspec],
            out_specs=(spec, spec, spec),
        ),
        cost_estimate=pl.CostEstimate(
            flops=20 * heads * rows * rows * HEAD,
            transcendentals=2 * heads * rows * rows,
            bytes_accessed=11 * q.size * 2 + 4 * lse.size * 4,
        ),
    )(meta, q, k, v, do, lse, dl, ko, vo, qr, dor, lser, dlr)


def layer(
    inputs,
    prefix,
    cotangent,
    w_query,
    w_key,
    w_value,
    w_out,
    w_up,
    w_down,
    b_query,
    b_value,
    b_out,
    b_up,
    b_down,
    gain_one,
    shift_one,
    gain_two,
    shift_two,
):
    f32 = jnp.float32
    bf16 = jnp.bfloat16
    tp = lax.axis_size("tensor")
    t_index = lax.axis_index("tensor")
    rows = inputs.shape[0]
    pieces = SEQ_LEN // rows
    assert pieces == 2
    half = t_index % pieces
    seq_here = (t_index * rows) // SEQ_LEN
    prefix_len = lax.dynamic_index_in_dim(prefix, seq_here, keepdims=False)
    to_first = [(t + 1, t) for t in range(0, tp, 2)]

    full_query, full_key, full_value, out_t = gather_joined([w_query, w_key, w_value, w_out.T], tp)
    full_up, down_t = gather_joined([w_up, w_down.T], tp)
    width = full_query.shape[1]
    heads = width // HEAD

    gain_first = gain_one.astype(f32)
    shift_first = shift_one.astype(f32)
    gain_second = gain_two.astype(f32)
    shift_second = shift_two.astype(f32)

    in_rows = inputs.astype(f32)
    normed_one = layer_norm(in_rows, gain_first, shift_first).astype(bf16)
    swap = [(t, t ^ 1) for t in range(tp)]
    normed_oth = lax.ppermute(normed_one, "tensor", swap)
    key_rows = dot_right(normed_one, full_key).astype(bf16)
    value_rows = (dot_right(normed_one, full_value) + b_value.astype(f32)).astype(bf16)
    queries = (dot_right(normed_one, full_query) + b_query.astype(f32)).astype(bf16)
    meta = jnp.stack([half, prefix_len]).astype(jnp.int32)
    k_oth = dot_right(normed_oth, full_key).astype(bf16)
    v_oth = (dot_right(normed_oth, full_value) + b_value.astype(f32)).astype(bf16)
    q_rcv = (dot_right(normed_oth, full_query) + b_query.astype(f32)).astype(bf16)
    attended, o_full, lse_wide = attention_forward(meta, queries, key_rows, value_rows, k_oth, v_oth)
    q_rcv, attended = lax.optimization_barrier((q_rcv, attended))
    lse_rcv = lax.ppermute(lse_wide[:, :, 0], "tensor", to_first)

    middle = in_rows + dot_back(attended, out_t) + b_out.astype(f32)
    normed_two = layer_norm(middle, gain_second, shift_second).astype(bf16)
    pre_act = dot_right(normed_two, full_up) + b_up.astype(f32)
    activated = gelu_exact(pre_act).astype(bf16)
    result = (middle + dot_back(activated, down_t) + b_down.astype(f32)).astype(bf16)

    grad_result = cotangent.astype(f32)
    grad_act = dot_right(cotangent, down_t)
    grad_pre = jax.vjp(gelu_exact, pre_act)[1](grad_act)[0].astype(bf16)
    ffn_grad = lax.dot_general(
        jnp.stack([normed_two, cotangent]),
        jnp.stack([grad_pre, activated]),
        (((1,), (1,)), ((0,), (0,))),
        preferred_element_type=f32,
    )
    grad_norm_two = dot_back(grad_pre, full_up)
    ffn_rows = scatter_rows(ffn_grad, axis=1)
    up_rows = ffn_rows[0]
    down_rows = ffn_rows[1]
    norm_two_back = jax.vjp(layer_norm, middle, gain_second, shift_second)[1](grad_norm_two)
    grad_middle = grad_result + norm_two_back[0]
    grad_attn_rows = grad_middle.astype(bf16)
    grad_attended = dot_right(grad_attn_rows, out_t).astype(bf16)

    delta = jnp.sum((grad_attended.astype(f32) * o_full).reshape(rows, heads, HEAD), axis=-1).T
    do_rcv, delta_rcv = lax.ppermute((grad_attended, delta), "tensor", to_first)

    def wide(x):
        return jnp.broadcast_to(x[:, :, None], x.shape + (LANES,))

    grad_q, grad_k, grad_v = attention_backward(
        meta, queries, key_rows, value_rows, grad_attended, lse_wide, wide(delta), k_oth, v_oth,
        q_rcv, do_rcv, wide(lse_rcv), wide(delta_rcv),
    )
    grad_qkv = jnp.concatenate([grad_q, grad_k, grad_v], axis=1)
    attn_grad = jnp.concatenate(
        [dot_over_rows(normed_one, grad_qkv), dot_over_rows(grad_attn_rows, attended)], axis=1
    )
    attn_rows = scatter_rows(attn_grad)
    qkv_rows = attn_rows[:, : 3 * width]
    out_rows = attn_rows[:, 3 * width :]
    grad_norm_one = dot_back(grad_q, full_query) + dot_back(grad_k, full_key) + dot_back(grad_v, full_value)
    norm_one_back = jax.vjp(layer_norm, in_rows, gain_first, shift_first)[1](grad_norm_one)
    grad_input = grad_middle + norm_one_back[0]

    shard_up, shard_down_t = sum_over_tensor([up_rows, down_rows], tp)
    shard_query, shard_key, shard_value, shard_out_t = sum_over_tensor(
        [qkv_rows[:, :width], qkv_rows[:, width : 2 * width], qkv_rows[:, 2 * width :], out_rows], tp
    )
    shard_out = shard_out_t.T
    shard_down = shard_down_t.T
    vectors = [
        jnp.sum(grad_q, axis=0, dtype=f32),
        jnp.sum(grad_v, axis=0, dtype=f32),
        jnp.sum(grad_middle, axis=0),
        jnp.sum(grad_pre, axis=0, dtype=f32),
        jnp.sum(grad_result, axis=0),
        norm_one_back[1],
        norm_one_back[2],
        norm_two_back[1],
        norm_two_back[2],
    ]
    joined = lax.psum(jnp.concatenate(vectors), "dp")
    pieces = [joined] + [
        lax.ppermute(joined, "tensor", [(i, (i + step) % tp) for i in range(tp)]) for step in range(1, tp)
    ]
    t_index = lax.axis_index("tensor")
    by_source = jnp.take(jnp.stack(pieces), (t_index - jnp.arange(tp, dtype=jnp.int32)) % tp, axis=0)
    total = by_source[0]
    for source in range(1, tp):
        total = total + by_source[source]
    vector_sums = []
    start = 0
    for v in vectors:
        vector_sums.append(total[start : start + v.shape[0]])
        start += v.shape[0]
    return (
        result,
        grad_input,
        shard_query,
        shard_key,
        shard_value,
        shard_out,
        shard_up,
        shard_down,
    ) + tuple(vector_sums)


def solution(mesh):
    rows_spec = P(("dp", "tensor"), None)
    placed = (
        rows_spec,
        P("dp"),
        rows_spec,
        P("dp", "tensor"),
        P("dp", "tensor"),
        P("dp", "tensor"),
        P("tensor", "dp"),
        P("dp", "tensor"),
        P("tensor", "dp"),
    ) + (P(),) * 9
    return jax.shard_map(
        layer,
        mesh=mesh,
        in_specs=placed,
        out_specs=(
            rows_spec,
            rows_spec,
            P("dp", "tensor"),
            P("dp", "tensor"),
            P("dp", "tensor"),
            P("tensor", "dp"),
            P("dp", "tensor"),
            P("tensor", "dp"),
        )
        + (P(),) * 9,
        check_vma=False,
    )
```
